32 devices in a mesh: dp: 2 (over y), row: 4 (over x, core), col: 4 (over z).
Axes of the slice: x: 2, y: 2, z: 4, core: 2. Of those that a mesh axis runs over, the one named last changes fastest.
Arguments:
- patches: bfloat16 [2, 512, 1456], P('dp', 'col', 'row'), may hold values from -6 to 6
- queries: bfloat16 [2, 512, 6144], P('dp', 'col', 'row'), may hold values from -6 to 6
- attn_keys: bfloat16 [2, 512, 6144], P('dp', 'col', 'row'), may hold values from -6 to 6
- attn_values: bfloat16 [2, 512, 6144], P('dp', 'col', 'row'), may hold values from -6 to 6
- out_weight: bfloat16 [6144, 12288], P('row', 'col'), may hold values from -0.15625 to 0.15625
- output_grad: bfloat16 [2, 512, 12288], P('dp', 'row', 'col'), may hold values from -4 to 4
Outputs:
- query_grad: float32 [2, 512, 6144], P('dp', 'col', 'row')
- key_grad: float32 [2, 512, 6144], P('dp', 'col', 'row')
- value_grad: float32 [2, 512, 6144], P('dp', 'col', 'row')
- out_weight_grad: float32 [6144, 12288], P('row', 'col')
- embed_weight_grad: float32 [1456, 12288], P('row', 'col')
The draws below stay inside these ranges and needn't reach their ends.
All inputs are finite; a program needn't handle non-finite values.
Results may differ from the reference program's by a relative error of at most 0.025.
Values may be sent and summed in bfloat16 or wider, within the bound.
No kernel may reach another device: no remote copies, remote signals or barrier semaphores. Data moves between devices by JAX's collectives and lax.ppermute only.
A program may use at most 128 MiB of HBM per device.

```python
import jax
import jax.numpy as jnp
from jax import lax

D = 12288
H = 48
DH = 128
SEQ = 512
BATCH = 2
HD = 6144
P_SIZE = 1456
DBLK = 3072


def draw_queries(key, part):
    shape = (BATCH, SEQ, HD)
    return jnp.clip(0.5 * jax.random.normal(jax.random.fold_in(key, 1), shape, jnp.float32), -6.0, 6.0).astype(jnp.bfloat16)


def draw_attn_keys(key, part):
    shape = (BATCH, SEQ, HD)
    return jnp.clip(0.5 * jax.random.normal(jax.random.fold_in(key, 11), shape, jnp.float32), -6.0, 6.0).astype(jnp.bfloat16)


def raised(values, key, source, target, shards_of, factor):
    owner, partner = [(jnp.arange(values.shape[dim]) // (values.shape[dim] // shards_of)).reshape([-1 if axis == dim else 1 for axis in range(values.ndim)]) for dim in (source, target)]
    chosen = jax.random.permutation(key, shards_of)[partner]
    strong = (owner == chosen) | (owner == (partner + shards_of // 2) % shards_of)
    return jnp.where(strong, factor * values, values)


def steps_of(own_key, shape, shards, smallest, largest):
    loudness, own = 1.0, jax.random.fold_in(own_key, 6)
    for axis_at, parts in shards:
        heights = jnp.exp(jax.random.uniform(jax.random.fold_in(own, axis_at), (parts,), jnp.float32, smallest / len(shards), largest / len(shards)))
        loudness = loudness * jnp.repeat(heights, shape[axis_at] // parts).reshape([-1 if axis == axis_at else 1 for axis in range(len(shape))])
    return loudness


def normal_values(key, dims, width, reach, split=(), kind=jnp.bfloat16):
    array = jax.random.normal(key, dims, jnp.float32) * width
    if len(split) > 0:
        array = steps_of(key, dims, split, -0.22, 0.18) * array
    return jnp.clip(array, min=-reach, max=reach).astype(kind)


def bell_draw_with(stream_key, shape, scale, bound, cuts, heavy, kind=jnp.bfloat16):
    array = scale * jax.random.normal(stream_key, shape, jnp.float32)
    if cuts:
        array = array * steps_of(stream_key, shape, cuts, -0.22, 0.18)
    return jnp.clip(raised(array, jax.random.fold_in(stream_key, 3), *heavy), -bound, bound).astype(kind)


def setup_inputs(seed: int = 0) -> dict:
    splits = jax.random.split(jax.random.key(seed), 7)
    return {
        "patches": normal_values(splits[0], (BATCH, SEQ, P_SIZE), 1.0, 6.0, ((0, 2), (1, 4), (2, 4))),
        "queries": draw_queries(jax.random.fold_in(splits[6], 71), 0),
        "attn_keys": draw_attn_keys(jax.random.fold_in(splits[6], 71), 0),
        "attn_values": normal_values(splits[3], (BATCH, SEQ, HD), 1.0, 6.0, ((0, 2), (1, 4), (2, 4))),
        "out_weight": normal_values(splits[4], (HD, D), (HD // 4) ** -0.5, 0.15625, ((0, 4), (1, 4))),
        "output_grad": bell_draw_with(splits[5], (BATCH, SEQ, D), 0.5, 4.0, ((0, 2), (1, 4), (2, 4)), (2, 1, 4, 2.0)),
    }


def split_heads(tensor):
    shaped = tensor.reshape(BATCH, SEQ, H, DH)
    return jnp.transpose(shaped, (0, 2, 1, 3)).reshape(BATCH * H, SEQ, DH)

def join_heads(tensor):
    shaped = tensor.reshape(BATCH, H, SEQ, DH)
    return jnp.transpose(shaped, (0, 2, 1, 3)).reshape(BATCH, SEQ, H * DH)

def head_probs(query_head, key_head):
    scores = jnp.dot(query_head, key_head.T, preferred_element_type=jnp.float32) * DH ** (-0.5)
    row_max = lax.optimization_barrier(jnp.max(scores, axis=1, keepdims=True))
    log_total = row_max + jnp.log(lax.optimization_barrier(jnp.sum(jnp.exp(scores - row_max), axis=1, keepdims=True)))
    return jnp.exp(scores - log_total).astype(jnp.bfloat16)

def forward_head(operands):
    query_head, key_head, value_head = operands
    attn_probs = head_probs(query_head, key_head)
    return jnp.dot(attn_probs, value_head, preferred_element_type=jnp.float32).astype(jnp.bfloat16)

def backward_head(operands):
    query_head, key_head, value_head, out_head, grad_head = operands
    attn_probs = head_probs(query_head, key_head)
    factor = DH ** (-0.5)
    prob_grad = jnp.dot(grad_head, value_head.T, preferred_element_type=jnp.float32)
    row_dot = lax.optimization_barrier(jnp.sum(grad_head.astype(jnp.float32) * out_head.astype(jnp.float32), axis=1, keepdims=True))
    score_grad = (attn_probs.astype(jnp.float32) * (prob_grad - row_dot)).astype(jnp.bfloat16)
    query_grad = jnp.dot(score_grad, key_head, preferred_element_type=jnp.float32) * factor
    key_grad = jnp.dot(score_grad.T, query_head, preferred_element_type=jnp.float32) * factor
    value_grad = jnp.dot(attn_probs.T, grad_head, preferred_element_type=jnp.float32)
    return (query_grad, key_grad, value_grad)

def attention_grad(flat_grad, out_weight):

    def add_block(running_total, block_index):
        first_col = (block_index * DBLK).astype(jnp.int32)
        grad_cols = lax.dynamic_slice_in_dim(flat_grad, first_col, DBLK, 1)
        weight_cols = lax.dynamic_slice_in_dim(out_weight, first_col, DBLK, 1)
        block_term = jnp.dot(grad_cols, weight_cols.T, preferred_element_type=jnp.float32)
        return (running_total + block_term, None)
    start_total = jnp.zeros((BATCH * SEQ, HD), jnp.float32)
    summed, _ = lax.scan(add_block, start_total, jnp.arange(D // DBLK, dtype=jnp.int32))
    return summed.astype(jnp.bfloat16)

def reference(patches, queries, attn_keys, attn_values, out_weight, output_grad):
    query_heads = split_heads(queries)
    key_heads = split_heads(attn_keys)
    value_heads = split_heads(attn_values)
    out_heads = lax.map(forward_head, (query_heads, key_heads, value_heads))
    attn_out = join_heads(out_heads)
    flat_out = attn_out.reshape(BATCH * SEQ, HD)
    flat_grad = output_grad.reshape(BATCH * SEQ, D)
    flat_patches = patches.reshape(BATCH * SEQ, P_SIZE)
    out_weight_grad = jnp.dot(flat_out.T, flat_grad, preferred_element_type=jnp.float32)
    embed_weight_grad = jnp.dot(flat_patches.T, flat_grad, preferred_element_type=jnp.float32)
    attn_grad = attention_grad(flat_grad, out_weight).reshape(BATCH, SEQ, HD)
    head_grads = lax.map(backward_head, (query_heads, key_heads, value_heads, out_heads, split_heads(attn_grad)))
    return (join_heads(head_grads[0]), join_heads(head_grads[1]), join_heads(head_grads[2]), out_weight_grad, embed_weight_grad)
```

```python
import jax
import jax.numpy as jnp
from jax import lax
from jax.sharding import PartitionSpec as P

DH = 128


def contract_rows(left, right):
    return lax.dot_general(
        left, right, (((0,), (0,)), ((), ())), preferred_element_type=jnp.float32
    )


def swap_dp(x):
    return lax.ppermute(x, "dp", [(0, 1), (1, 0)])


def body(patches, queries, attn_keys, attn_values, out_weight, output_grad):
    factor = DH ** (-0.5)
    local_rows = queries.shape[1]
    feature_width = queries.shape[2]
    head_count = feature_width // DH
    grad_other = swap_dp(output_grad)
    patch_other = swap_dp(lax.all_gather(patches, "col", axis=1, tiled=True))
    every_key, every_value, every_patch = (
        lax.all_gather(attn_keys, "col", axis=1, tiled=True),
        lax.all_gather(attn_values, "col", axis=1, tiled=True),
        lax.all_gather(patches, "col", axis=1, tiled=True),
    )
    local_query = queries[0].reshape(local_rows, head_count, DH)
    all_keys = every_key[0].reshape(-1, head_count, DH)
    all_values = every_value[0].reshape(-1, head_count, DH)
    scores = (
        jnp.einsum("qhd,khd->hqk", local_query, all_keys, preferred_element_type=jnp.float32)
        * factor
    )
    row_max = jnp.max(scores, axis=2, keepdims=True)
    log_total = row_max + jnp.log(jnp.sum(jnp.exp(scores - row_max), axis=2, keepdims=True))
    attn_probs = jnp.exp(scores - log_total).astype(jnp.bfloat16)
    attn_out = jnp.einsum(
        "hqk,khd->qhd", attn_probs, all_values, preferred_element_type=jnp.float32
    ).astype(jnp.bfloat16)
    out_local = attn_out.reshape(1, local_rows, feature_width)
    dense_grad = lax.all_gather(output_grad, "row", axis=1, tiled=True)[0]
    attn_grad = lax.psum_scatter(
        lax.dot_general(
            dense_grad, out_weight, (((1,), (1,)), ((), ())), preferred_element_type=jnp.float32
        ),
        "col",
        scatter_dimension=0,
        tiled=True,
    ).astype(jnp.bfloat16)
    grad_heads = attn_grad.reshape(local_rows, head_count, DH)
    prob_grad = jnp.einsum(
        "qhd,khd->hqk", grad_heads, all_values, preferred_element_type=jnp.float32
    )
    row_dot = jnp.transpose(
        jnp.sum(grad_heads.astype(jnp.float32) * attn_out.astype(jnp.float32), axis=2)
    )[:, :, None]
    score_grad = (attn_probs.astype(jnp.float32) * (prob_grad - row_dot)).astype(jnp.bfloat16)
    query_grad = (
        jnp.einsum("hqk,khd->qhd", score_grad, all_keys, preferred_element_type=jnp.float32)
        * factor
    )
    every_out = lax.all_gather(out_local, "col", axis=1, tiled=True)
    key_term = (
        jnp.einsum("hqk,qhd->khd", score_grad, local_query, preferred_element_type=jnp.float32)
        * factor
    )
    value_term = jnp.einsum(
        "hqk,qhd->khd", attn_probs, grad_heads, preferred_element_type=jnp.float32
    )
    key_sum, value_sum = (
        lax.psum_scatter(
            key_term.reshape(-1, feature_width).astype(jnp.bfloat16),
            "col",
            scatter_dimension=0,
            tiled=True,
        ).astype(jnp.float32),
        lax.psum_scatter(
            value_term.reshape(-1, feature_width).astype(jnp.bfloat16),
            "col",
            scatter_dimension=0,
            tiled=True,
        ).astype(jnp.float32),
    )
    out_pair = jnp.concatenate([every_out, swap_dp(every_out)], axis=0)
    grad_pair = lax.all_gather(
        jnp.concatenate([output_grad, grad_other], axis=0), "row", axis=1, tiled=True
    )
    patch_pair = jnp.concatenate([every_patch, patch_other], axis=0)
    out_weight_grad = lax.dot_general(
        out_pair, grad_pair, (((0, 1), (0, 1)), ((), ())), preferred_element_type=jnp.float32
    )
    embed_weight_grad = lax.dot_general(
        patch_pair, grad_pair, (((0, 1), (0, 1)), ((), ())), preferred_element_type=jnp.float32
    )
    return (
        query_grad.reshape(1, local_rows, feature_width),
        key_sum.reshape(1, local_rows, feature_width),
        value_sum.reshape(1, local_rows, feature_width),
        out_weight_grad,
        embed_weight_grad,
    )


def solution(mesh):
    placed = (
        P("dp", "col", "row"),
        P("dp", "col", "row"),
        P("dp", "col", "row"),
        P("dp", "col", "row"),
        P("row", "col"),
        P("dp", "row", "col"),
    )
    return jax.shard_map(
        body,
        mesh=mesh,
        in_specs=placed,
        out_specs=(
            P("dp", "col", "row"),
            P("dp", "col", "row"),
            P("dp", "col", "row"),
            P("row", "col"),
            P("row", "col"),
        ),
        check_vma=False,
    )
```

```python
import jax
import jax.numpy as jnp
from jax import lax
from jax.sharding import PartitionSpec as P

DH = 128


def contract_rows(left, right):
    return lax.dot_general(
        left, right, (((0,), (0,)), ((), ())), preferred_element_type=jnp.float32
    )


def swap_dp(x):
    return lax.ppermute(x, "dp", [(0, 1), (1, 0)])


def body_tokens(patches, queries, attn_keys, attn_values, out_weight, output_grad):
    factor = DH ** (-0.5)
    local_rows = queries.shape[1]
    feature_width = queries.shape[2]
    head_count = feature_width // DH
    grad_other = swap_dp(output_grad)
    patch_other = swap_dp(lax.all_gather(patches, "col", axis=1, tiled=True))
    every_key, every_value, every_patch = (
        lax.all_gather(attn_keys, "col", axis=1, tiled=True),
        lax.all_gather(attn_values, "col", axis=1, tiled=True),
        lax.all_gather(patches, "col", axis=1, tiled=True),
    )
    local_query = queries[0].reshape(local_rows, head_count, DH)
    all_keys = every_key[0].reshape(-1, head_count, DH)
    all_values = every_value[0].reshape(-1, head_count, DH)
    scores = (
        jnp.einsum("qhd,khd->hqk", local_query, all_keys, preferred_element_type=jnp.float32)
        * factor
    )
    row_max = jnp.max(scores, axis=2, keepdims=True)
    log_total = row_max + jnp.log(jnp.sum(jnp.exp(scores - row_max), axis=2, keepdims=True))
    attn_probs = jnp.exp(scores - log_total).astype(jnp.bfloat16)
    attn_out = jnp.einsum(
        "hqk,khd->qhd", attn_probs, all_values, preferred_element_type=jnp.float32
    ).astype(jnp.bfloat16)
    out_local = attn_out.reshape(1, local_rows, feature_width)
    dense_grad = lax.all_gather(output_grad, "row", axis=1, tiled=True)[0]
    attn_grad = lax.psum_scatter(
        lax.dot_general(
            dense_grad, out_weight, (((1,), (1,)), ((), ())), preferred_element_type=jnp.float32
        ),
        "col",
        scatter_dimension=0,
        tiled=True,
    ).astype(jnp.bfloat16)
    grad_heads = attn_grad.reshape(local_rows, head_count, DH)
    prob_grad = jnp.einsum(
        "qhd,khd->hqk", grad_heads, all_values, preferred_element_type=jnp.float32
    )
    row_dot = jnp.transpose(
        jnp.sum(grad_heads.astype(jnp.float32) * attn_out.astype(jnp.float32), axis=2)
    )[:, :, None]
    score_grad = (attn_probs.astype(jnp.float32) * (prob_grad - row_dot)).astype(jnp.bfloat16)
    query_grad = (
        jnp.einsum("hqk,khd->qhd", score_grad, all_keys, preferred_element_type=jnp.float32)
        * factor
    )
    every_out = lax.all_gather(out_local, "col", axis=1, tiled=True)
    key_term = (
        jnp.einsum("hqk,qhd->khd", score_grad, local_query, preferred_element_type=jnp.float32)
        * factor
    )
    value_term = jnp.einsum(
        "hqk,qhd->khd", attn_probs, grad_heads, preferred_element_type=jnp.float32
    )
    key_sum, value_sum = (
        lax.psum_scatter(
            key_term.reshape(-1, feature_width).astype(jnp.bfloat16),
            "col",
            scatter_dimension=0,
            tiled=True,
        ).astype(jnp.float32),
        lax.psum_scatter(
            value_term.reshape(-1, feature_width).astype(jnp.bfloat16),
            "col",
            scatter_dimension=0,
            tiled=True,
        ).astype(jnp.float32),
    )
    out_pair = jnp.concatenate([every_out, swap_dp(every_out)], axis=0)
    grad_pair = lax.all_gather(
        jnp.concatenate([output_grad, grad_other], axis=0), "row", axis=1, tiled=True
    )
    patch_pair = jnp.concatenate([every_patch, patch_other], axis=0)
    out_weight_grad = lax.dot_general(
        out_pair, grad_pair, (((0, 1), (0, 1)), ((), ())), preferred_element_type=jnp.float32
    )
    embed_weight_grad = lax.dot_general(
        patch_pair, grad_pair, (((0, 1), (0, 1)), ((), ())), preferred_element_type=jnp.float32
    )
    return (
        query_grad.reshape(1, local_rows, feature_width),
        key_sum.reshape(1, local_rows, feature_width),
        value_sum.reshape(1, local_rows, feature_width),
        out_weight_grad,
        embed_weight_grad,
    )


def axis_size(axis):
    return lax.psum(1, axis)


def shifted(x, axis, step):
    n = axis_size(axis)
    return lax.ppermute(x, axis, [(j, (j + step) % n) for j in range(n)])


def natural(pieces, axis):
    n = len(pieces)
    order = (lax.axis_index(axis) - jnp.arange(n)) % n
    return jnp.take(jnp.stack(pieces, 0), order, axis=0)


def gather_rows(x, axis):
    n = axis_size(axis)
    pieces = [x] + [shifted(x, axis, s) for s in range(1, n)]
    stacked = natural(pieces, axis)
    return stacked.reshape((n * x.shape[0],) + x.shape[1:])


def group_cols(x, axis, group):
    width = x.shape[1] // axis_size(axis)
    return lax.dynamic_slice_in_dim(x, group * width, width, 1)


def to_heads(x, axis):
    n, me = axis_size(axis), lax.axis_index(axis)
    pieces = [group_cols(x, axis, me)] + [
        shifted(group_cols(x, axis, (me + s) % n), axis, s) for s in range(1, n)
    ]
    stacked = natural(pieces, axis)
    return stacked.reshape((n * x.shape[0],) + stacked.shape[2:])


def from_heads(x, axis):
    n, me = axis_size(axis), lax.axis_index(axis)
    rows = x.shape[0] // n
    block = lambda k: lax.dynamic_slice_in_dim(x, k * rows, rows, 0)
    pieces = [block(me)] + [
        shifted(block((me + s) % n).astype(jnp.bfloat16), axis, s).astype(jnp.float32)
        for s in range(1, n)
    ]
    stacked = natural(pieces, axis)
    return jnp.transpose(stacked, (1, 0, 2)).reshape(rows, n * x.shape[1])


def sum_to_heads(partial, axis):
    n, me = axis_size(axis), lax.axis_index(axis)
    total = group_cols(partial, axis, me)
    for s in range(1, n):
        sent = group_cols(partial, axis, (me - s) % n).astype(jnp.bfloat16)
        total = total + shifted(sent, axis, -s % n).astype(jnp.float32)
    return total


def body_heads(patches, queries, attn_keys, attn_values, out_weight, output_grad):
    factor = DH ** (-0.5)
    ncol = axis_size("col")
    grad_other = swap_dp(output_grad)
    dense_grad = gather_rows(output_grad[0], "row")
    other_grad = gather_rows(grad_other[0], "row")
    query_h, key_h, value_h = (to_heads(a[0], "col") for a in (queries, attn_keys, attn_values))
    rows, width = query_h.shape
    heads = width // DH
    local_query = query_h.reshape(rows, heads, DH)
    all_keys = key_h.reshape(rows, heads, DH)
    all_values = value_h.reshape(rows, heads, DH)
    scores = (
        jnp.einsum("qhd,khd->hqk", local_query, all_keys, preferred_element_type=jnp.float32)
        * factor
    )
    row_max = jnp.max(scores, axis=2, keepdims=True)
    log_total = row_max + jnp.log(jnp.sum(jnp.exp(scores - row_max), axis=2, keepdims=True))
    attn_probs = jnp.exp(scores - log_total).astype(jnp.bfloat16)
    attn_out = jnp.einsum(
        "hqk,khd->qhd", attn_probs, all_values, preferred_element_type=jnp.float32
    ).astype(jnp.bfloat16)
    grad_partial = lax.dot_general(
        dense_grad, out_weight, (((1,), (1,)), ((), ())), preferred_element_type=jnp.float32
    )
    attn_grad = sum_to_heads(grad_partial, "col").astype(jnp.bfloat16)
    grad_heads = attn_grad.reshape(rows, heads, DH)
    prob_grad = jnp.einsum(
        "qhd,khd->hqk", grad_heads, all_values, preferred_element_type=jnp.float32
    )
    row_dot = jnp.transpose(
        jnp.sum(grad_heads.astype(jnp.float32) * attn_out.astype(jnp.float32), axis=2)
    )[:, :, None]
    score_grad = (attn_probs.astype(jnp.float32) * (prob_grad - row_dot)).astype(jnp.bfloat16)
    query_grad = (
        jnp.einsum("hqk,khd->qhd", score_grad, all_keys, preferred_element_type=jnp.float32)
        * factor
    )
    key_grad = (
        jnp.einsum("hqk,qhd->khd", score_grad, local_query, preferred_element_type=jnp.float32)
        * factor
    )
    value_grad = jnp.einsum(
        "hqk,qhd->khd", attn_probs, grad_heads, preferred_element_type=jnp.float32
    )
    outs = [from_heads(g.reshape(rows, width), "col")[None] for g in (query_grad, key_grad, value_grad)]
    out_groups = natural(
        [attn_out.reshape(rows, width)]
        + [shifted(attn_out.reshape(rows, width), "col", s) for s in range(1, ncol)],
        "col",
    )
    every_out = jnp.transpose(out_groups, (1, 0, 2)).reshape(rows, ncol * width)
    other_out = swap_dp(every_out)
    every_patch = gather_rows(patches[0], "col")
    other_patch = swap_dp(every_patch)
    out_weight_grad = contract_rows(every_out, dense_grad) + contract_rows(other_out, other_grad)
    embed_weight_grad = contract_rows(every_patch, dense_grad) + contract_rows(
        other_patch, other_grad
    )
    return (*outs, out_weight_grad, embed_weight_grad)


def body(patches, queries, attn_keys, attn_values, out_weight, output_grad):
    heads_here = queries.shape[2] // DH
    if heads_here % axis_size("col") == 0 and queries.shape[1] == output_grad.shape[1]:
        return body_heads(patches, queries, attn_keys, attn_values, out_weight, output_grad)
    return body_tokens(patches, queries, attn_keys, attn_values, out_weight, output_grad)


def solution(mesh):
    placed = (
        P("dp", "col", "row"),
        P("dp", "col", "row"),
        P("dp", "col", "row"),
        P("dp", "col", "row"),
        P("row", "col"),
        P("dp", "row", "col"),
    )
    return jax.shard_map(
        body,
        mesh=mesh,
        in_specs=placed,
        out_specs=(
            P("dp", "col", "row"),
            P("dp", "col", "row"),
            P("dp", "col", "row"),
            P("row", "col"),
            P("row", "col"),
        ),
        check_vma=False,
    )
```

```python
import jax
import numpy as np
import jax.numpy as jnp
from jax import lax
from jax.sharding import PartitionSpec as P

DH = 128


def contract_rows(left, right):
    return lax.dot_general(
        left, right, (((0,), (0,)), ((), ())), preferred_element_type=jnp.float32
    )


def swap_dp(x):
    return lax.ppermute(x, "dp", [(0, 1), (1, 0)])


def body_tokens(patches, queries, attn_keys, attn_values, out_weight, output_grad):
    factor = DH ** (-0.5)
    local_rows = queries.shape[1]
    feature_width = queries.shape[2]
    head_count = feature_width // DH
    grad_other = swap_dp(output_grad)
    patch_other = swap_dp(lax.all_gather(patches, "col", axis=1, tiled=True))
    every_key, every_value, every_patch = (
        lax.all_gather(attn_keys, "col", axis=1, tiled=True),
        lax.all_gather(attn_values, "col", axis=1, tiled=True),
        lax.all_gather(patches, "col", axis=1, tiled=True),
    )
    local_query = queries[0].reshape(local_rows, head_count, DH)
    all_keys = every_key[0].reshape(-1, head_count, DH)
    all_values = every_value[0].reshape(-1, head_count, DH)
    scores = (
        jnp.einsum("qhd,khd->hqk", local_query, all_keys, preferred_element_type=jnp.float32)
        * factor
    )
    row_max = jnp.max(scores, axis=2, keepdims=True)
    log_total = row_max + jnp.log(jnp.sum(jnp.exp(scores - row_max), axis=2, keepdims=True))
    attn_probs = jnp.exp(scores - log_total).astype(jnp.bfloat16)
    attn_out = jnp.einsum(
        "hqk,khd->qhd", attn_probs, all_values, preferred_element_type=jnp.float32
    ).astype(jnp.bfloat16)
    out_local = attn_out.reshape(1, local_rows, feature_width)
    dense_grad = lax.all_gather(output_grad, "row", axis=1, tiled=True)[0]
    attn_grad = lax.psum_scatter(
        lax.dot_general(
            dense_grad, out_weight, (((1,), (1,)), ((), ())), preferred_element_type=jnp.float32
        ),
        "col",
        scatter_dimension=0,
        tiled=True,
    ).astype(jnp.bfloat16)
    grad_heads = attn_grad.reshape(local_rows, head_count, DH)
    prob_grad = jnp.einsum(
        "qhd,khd->hqk", grad_heads, all_values, preferred_element_type=jnp.float32
    )
    row_dot = jnp.transpose(
        jnp.sum(grad_heads.astype(jnp.float32) * attn_out.astype(jnp.float32), axis=2)
    )[:, :, None]
    score_grad = (attn_probs.astype(jnp.float32) * (prob_grad - row_dot)).astype(jnp.bfloat16)
    query_grad = (
        jnp.einsum("hqk,khd->qhd", score_grad, all_keys, preferred_element_type=jnp.float32)
        * factor
    )
    every_out = lax.all_gather(out_local, "col", axis=1, tiled=True)
    key_term = (
        jnp.einsum("hqk,qhd->khd", score_grad, local_query, preferred_element_type=jnp.float32)
        * factor
    )
    value_term = jnp.einsum(
        "hqk,qhd->khd", attn_probs, grad_heads, preferred_element_type=jnp.float32
    )
    key_sum, value_sum = (
        lax.psum_scatter(
            key_term.reshape(-1, feature_width).astype(jnp.bfloat16),
            "col",
            scatter_dimension=0,
            tiled=True,
        ).astype(jnp.float32),
        lax.psum_scatter(
            value_term.reshape(-1, feature_width).astype(jnp.bfloat16),
            "col",
            scatter_dimension=0,
            tiled=True,
        ).astype(jnp.float32),
    )
    out_pair = jnp.concatenate([every_out, swap_dp(every_out)], axis=0)
    grad_pair = lax.all_gather(
        jnp.concatenate([output_grad, grad_other], axis=0), "row", axis=1, tiled=True
    )
    patch_pair = jnp.concatenate([every_patch, patch_other], axis=0)
    out_weight_grad = lax.dot_general(
        out_pair, grad_pair, (((0, 1), (0, 1)), ((), ())), preferred_element_type=jnp.float32
    )
    embed_weight_grad = lax.dot_general(
        patch_pair, grad_pair, (((0, 1), (0, 1)), ((), ())), preferred_element_type=jnp.float32
    )
    return (
        query_grad.reshape(1, local_rows, feature_width),
        key_sum.reshape(1, local_rows, feature_width),
        value_sum.reshape(1, local_rows, feature_width),
        out_weight_grad,
        embed_weight_grad,
    )


def axis_size(axis):
    return lax.psum(1, axis)


def shifted(x, axis, step):
    n = axis_size(axis)
    return lax.ppermute(x, axis, [(j, (j + step) % n) for j in range(n)])


def natural(pieces, axis):
    n = len(pieces)
    order = (lax.axis_index(axis) - jnp.arange(n)) % n
    return jnp.take(jnp.stack(pieces, 0), order, axis=0)


def gather_rows(x, axis):
    n = axis_size(axis)
    pieces = [x] + [shifted(x, axis, s) for s in range(1, n)]
    stacked = natural(pieces, axis)
    return stacked.reshape((n * x.shape[0],) + x.shape[1:])


def group_cols(x, axis, group):
    width = x.shape[1] // axis_size(axis)
    return lax.dynamic_slice_in_dim(x, group * width, width, 1)


def to_heads(x, axis):
    n, me = axis_size(axis), lax.axis_index(axis)
    pieces = [group_cols(x, axis, me)] + [
        shifted(group_cols(x, axis, (me + s) % n), axis, s) for s in range(1, n)
    ]
    stacked = natural(pieces, axis)
    return stacked.reshape((n * x.shape[0],) + stacked.shape[2:])


def from_heads(x, axis):
    n, me = axis_size(axis), lax.axis_index(axis)
    rows = x.shape[0] // n
    block = lambda k: lax.dynamic_slice_in_dim(x, k * rows, rows, 0)
    pieces = [block(me)] + [
        shifted(block((me + s) % n).astype(jnp.bfloat16), axis, s).astype(jnp.float32)
        for s in range(1, n)
    ]
    stacked = natural(pieces, axis)
    return jnp.transpose(stacked, (1, 0, 2)).reshape(rows, n * x.shape[1])


def sum_to_heads(partial, axis):
    n, me = axis_size(axis), lax.axis_index(axis)
    total = group_cols(partial, axis, me)
    for s in range(1, n):
        sent = group_cols(partial, axis, (me - s) % n).astype(jnp.bfloat16)
        total = total + shifted(sent, axis, -s % n).astype(jnp.float32)
    return total


def flat(*arrays):
    return jnp.concatenate([a.reshape(-1) for a in arrays])


def unflat(vector, shapes):
    out, at = [], 0
    for shape in shapes:
        size = int(np.prod(shape))
        out.append(vector[..., at:at + size].reshape(vector.shape[:-1] + shape))
        at += size
    return out


def gather_rows_relayed(x, axis):
    n, me = axis_size(axis), lax.axis_index(axis)
    chips = n // 2
    cross = [x] + [
        lax.ppermute(x, axis, [(j, (j + 2 * s) % n) for j in range(n)]) for s in range(1, chips)
    ]
    partner_own = lax.ppermute(x, axis, [(j, j ^ 1) for j in range(n)])
    if chips > 1:
        relayed = lax.ppermute(jnp.stack(cross[1:], 0), axis, [(j, j ^ 1) for j in range(n)])
        partner = [partner_own] + [relayed[k] for k in range(chips - 1)]
    else:
        partner = [partner_own]
    pieces = jnp.stack(cross + partner, 0)
    j = jnp.arange(n)
    mine = (j % 2) == (me % 2)
    order = jnp.where(mine, ((me - j) % n) // 2, chips + (((me ^ 1) - j) % n) // 2)
    stacked = jnp.take(pieces, order, axis=0)
    return stacked.reshape((n * x.shape[0],) + x.shape[1:])


def body_heads(patches, queries, attn_keys, attn_values, out_weight, output_grad):
    factor = DH ** (-0.5)
    n, me = axis_size("col"), lax.axis_index("col")
    tokens, width_all = queries.shape[1], queries.shape[2]
    width = width_all // n
    heads = width // DH
    patch_here = patches[0]
    dense_grad = gather_rows_relayed(output_grad[0], "row")
    grad_other = swap_dp(output_grad)
    other_grad = gather_rows_relayed(grad_other[0], "row")
    qkv = jnp.stack([queries[0], attn_keys[0], attn_values[0]], 0)
    part = lambda g: lax.dynamic_slice_in_dim(qkv, g * width, width, 2)
    shapes = [(3, tokens, width), patch_here.shape]
    pieces = [(part(me), patch_here)]
    for s in range(1, n):
        got = shifted(flat(part((me + s) % n), patch_here), "col", s)
        pieces.append(tuple(unflat(got, shapes)))
    qkv_h = natural([p[0] for p in pieces], "col")
    every_patch = natural([p[1] for p in pieces], "col").reshape(n * tokens, -1)
    rows = n * tokens
    qkv_h = jnp.transpose(qkv_h, (1, 0, 2, 3)).reshape(3, rows, heads, DH)
    local_query, all_keys, all_values = qkv_h[0], qkv_h[1], qkv_h[2]
    scores = (
        jnp.einsum("qhd,khd->hqk", local_query, all_keys, preferred_element_type=jnp.float32)
        * factor
    )
    row_max = jnp.max(scores, axis=2, keepdims=True)
    log_total = row_max + jnp.log(jnp.sum(jnp.exp(scores - row_max), axis=2, keepdims=True))
    attn_probs = jnp.exp(scores - log_total).astype(jnp.bfloat16)
    attn_out = jnp.einsum(
        "hqk,khd->qhd", attn_probs, all_values, preferred_element_type=jnp.float32
    ).astype(jnp.bfloat16)
    grad_partial = lax.dot_general(
        dense_grad, out_weight, (((1,), (1,)), ((), ())), preferred_element_type=jnp.float32
    )
    attn_grad = sum_to_heads(grad_partial, "col").astype(jnp.bfloat16)
    grad_heads = attn_grad.reshape(rows, heads, DH)
    prob_grad = jnp.einsum(
        "qhd,khd->hqk", grad_heads, all_values, preferred_element_type=jnp.float32
    )
    row_dot = jnp.transpose(
        jnp.sum(grad_heads.astype(jnp.float32) * attn_out.astype(jnp.float32), axis=2)
    )[:, :, None]
    score_grad = (attn_probs.astype(jnp.float32) * (prob_grad - row_dot)).astype(jnp.bfloat16)
    query_grad = (
        jnp.einsum("hqk,khd->qhd", score_grad, all_keys, preferred_element_type=jnp.float32)
        * factor
    )
    key_grad = (
        jnp.einsum("hqk,qhd->khd", score_grad, local_query, preferred_element_type=jnp.float32)
        * factor
    )
    value_grad = jnp.einsum(
        "hqk,qhd->khd", attn_probs, grad_heads, preferred_element_type=jnp.float32
    )
    grads = jnp.stack([g.reshape(n, tokens, width) for g in (query_grad, key_grad, value_grad)], 1)
    back = [grads[me]] + [
        shifted(grads[(me + s) % n].astype(jnp.bfloat16), "col", s).astype(jnp.float32)
        for s in range(1, n)
    ]
    back = jnp.transpose(natural(back, "col"), (1, 2, 0, 3)).reshape(3, 1, tokens, width_all)
    out_flat = attn_out.reshape(rows, width)
    out_groups = natural([out_flat] + [shifted(out_flat, "col", s) for s in range(1, n)], "col")
    every_out = jnp.transpose(out_groups, (1, 0, 2)).reshape(rows, width_all)
    other_out, other_patch = unflat(
        swap_dp(flat(every_out, every_patch)), [every_out.shape, every_patch.shape]
    )
    out_weight_grad = contract_rows(every_out, dense_grad) + contract_rows(other_out, other_grad)
    embed_weight_grad = contract_rows(every_patch, dense_grad) + contract_rows(
        other_patch, other_grad
    )
    return (back[0], back[1], back[2], out_weight_grad, embed_weight_grad)


def body(patches, queries, attn_keys, attn_values, out_weight, output_grad):
    heads_here = queries.shape[2] // DH
    if heads_here % axis_size("col") == 0 and queries.shape[1] == output_grad.shape[1]:
        return body_heads(patches, queries, attn_keys, attn_values, out_weight, output_grad)
    return body_tokens(patches, queries, attn_keys, attn_values, out_weight, output_grad)


def solution(mesh):
    placed = (
        P("dp", "col", "row"),
        P("dp", "col", "row"),
        P("dp", "col", "row"),
        P("dp", "col", "row"),
        P("row", "col"),
        P("dp", "row", "col"),
    )
    return jax.shard_map(
        body,
        mesh=mesh,
        in_specs=placed,
        out_specs=(
            P("dp", "col", "row"),
            P("dp", "col", "row"),
            P("dp", "col", "row"),
            P("row", "col"),
            P("row", "col"),
        ),
        check_vma=False,
    )
```

```python
import jax
import numpy as np
import jax.numpy as jnp
from jax import lax
from jax.sharding import PartitionSpec as P

DH = 128


def contract_rows(left, right):
    return lax.dot_general(
        left, right, (((0,), (0,)), ((), ())), preferred_element_type=jnp.float32
    )


def swap_dp(x):
    return lax.ppermute(x, "dp", [(0, 1), (1, 0)])


def body_tokens(patches, queries, attn_keys, attn_values, out_weight, output_grad):
    factor = DH ** (-0.5)
    local_rows = queries.shape[1]
    feature_width = queries.shape[2]
    head_count = feature_width // DH
    grad_other = swap_dp(output_grad)
    patch_other = swap_dp(lax.all_gather(patches, "col", axis=1, tiled=True))
    every_key, every_value, every_patch = (
        lax.all_gather(attn_keys, "col", axis=1, tiled=True),
        lax.all_gather(attn_values, "col", axis=1, tiled=True),
        lax.all_gather(patches, "col", axis=1, tiled=True),
    )
    local_query = queries[0].reshape(local_rows, head_count, DH)
    all_keys = every_key[0].reshape(-1, head_count, DH)
    all_values = every_value[0].reshape(-1, head_count, DH)
    scores = (
        jnp.einsum("qhd,khd->hqk", local_query, all_keys, preferred_element_type=jnp.float32)
        * factor
    )
    row_max = jnp.max(scores, axis=2, keepdims=True)
    log_total = row_max + jnp.log(jnp.sum(jnp.exp(scores - row_max), axis=2, keepdims=True))
    attn_probs = jnp.exp(scores - log_total).astype(jnp.bfloat16)
    attn_out = jnp.einsum(
        "hqk,khd->qhd", attn_probs, all_values, preferred_element_type=jnp.float32
    ).astype(jnp.bfloat16)
    out_local = attn_out.reshape(1, local_rows, feature_width)
    dense_grad = lax.all_gather(output_grad, "row", axis=1, tiled=True)[0]
    attn_grad = lax.psum_scatter(
        lax.dot_general(
            dense_grad, out_weight, (((1,), (1,)), ((), ())), preferred_element_type=jnp.float32
        ),
        "col",
        scatter_dimension=0,
        tiled=True,
    ).astype(jnp.bfloat16)
    grad_heads = attn_grad.reshape(local_rows, head_count, DH)
    prob_grad = jnp.einsum(
        "qhd,khd->hqk", grad_heads, all_values, preferred_element_type=jnp.float32
    )
    row_dot = jnp.transpose(
        jnp.sum(grad_heads.astype(jnp.float32) * attn_out.astype(jnp.float32), axis=2)
    )[:, :, None]
    score_grad = (attn_probs.astype(jnp.float32) * (prob_grad - row_dot)).astype(jnp.bfloat16)
    query_grad = (
        jnp.einsum("hqk,khd->qhd", score_grad, all_keys, preferred_element_type=jnp.float32)
        * factor
    )
    every_out = lax.all_gather(out_local, "col", axis=1, tiled=True)
    key_term = (
        jnp.einsum("hqk,qhd->khd", score_grad, local_query, preferred_element_type=jnp.float32)
        * factor
    )
    value_term = jnp.einsum(
        "hqk,qhd->khd", attn_probs, grad_heads, preferred_element_type=jnp.float32
    )
    key_sum, value_sum = (
        lax.psum_scatter(
            key_term.reshape(-1, feature_width).astype(jnp.bfloat16),
            "col",
            scatter_dimension=0,
            tiled=True,
        ).astype(jnp.float32),
        lax.psum_scatter(
            value_term.reshape(-1, feature_width).astype(jnp.bfloat16),
            "col",
            scatter_dimension=0,
            tiled=True,
        ).astype(jnp.float32),
    )
    out_pair = jnp.concatenate([every_out, swap_dp(every_out)], axis=0)
    grad_pair = lax.all_gather(
        jnp.concatenate([output_grad, grad_other], axis=0), "row", axis=1, tiled=True
    )
    patch_pair = jnp.concatenate([every_patch, patch_other], axis=0)
    out_weight_grad = lax.dot_general(
        out_pair, grad_pair, (((0, 1), (0, 1)), ((), ())), preferred_element_type=jnp.float32
    )
    embed_weight_grad = lax.dot_general(
        patch_pair, grad_pair, (((0, 1), (0, 1)), ((), ())), preferred_element_type=jnp.float32
    )
    return (
        query_grad.reshape(1, local_rows, feature_width),
        key_sum.reshape(1, local_rows, feature_width),
        value_sum.reshape(1, local_rows, feature_width),
        out_weight_grad,
        embed_weight_grad,
    )


def axis_size(axis):
    return lax.psum(1, axis)


def shifted(x, axis, step):
    n = axis_size(axis)
    return lax.ppermute(x, axis, [(j, (j + step) % n) for j in range(n)])


def natural(pieces, axis):
    n = len(pieces)
    order = (lax.axis_index(axis) - jnp.arange(n)) % n
    return jnp.take(jnp.stack(pieces, 0), order, axis=0)


def gather_rows(x, axis):
    n = axis_size(axis)
    pieces = [x] + [shifted(x, axis, s) for s in range(1, n)]
    stacked = natural(pieces, axis)
    return stacked.reshape((n * x.shape[0],) + x.shape[1:])


def group_cols(x, axis, group):
    width = x.shape[1] // axis_size(axis)
    return lax.dynamic_slice_in_dim(x, group * width, width, 1)


def to_heads(x, axis):
    n, me = axis_size(axis), lax.axis_index(axis)
    pieces = [group_cols(x, axis, me)] + [
        shifted(group_cols(x, axis, (me + s) % n), axis, s) for s in range(1, n)
    ]
    stacked = natural(pieces, axis)
    return stacked.reshape((n * x.shape[0],) + stacked.shape[2:])


def from_heads(x, axis):
    n, me = axis_size(axis), lax.axis_index(axis)
    rows = x.shape[0] // n
    block = lambda k: lax.dynamic_slice_in_dim(x, k * rows, rows, 0)
    pieces = [block(me)] + [
        shifted(block((me + s) % n).astype(jnp.bfloat16), axis, s).astype(jnp.float32)
        for s in range(1, n)
    ]
    stacked = natural(pieces, axis)
    return jnp.transpose(stacked, (1, 0, 2)).reshape(rows, n * x.shape[1])


def sum_to_heads(partial, axis):
    n, me = axis_size(axis), lax.axis_index(axis)
    total = group_cols(partial, axis, me)
    for s in range(1, n):
        sent = group_cols(partial, axis, (me - s) % n).astype(jnp.bfloat16)
        total = total + shifted(sent, axis, -s % n).astype(jnp.float32)
    return total


def flat(*arrays):
    return jnp.concatenate([a.reshape(-1) for a in arrays])


def unflat(vector, shapes):
    out, at = [], 0
    for shape in shapes:
        size = int(np.prod(shape))
        out.append(vector[..., at:at + size].reshape(vector.shape[:-1] + shape))
        at += size
    return out


def gather_rows_relayed(x, axis):
    n, me = axis_size(axis), lax.axis_index(axis)
    chips = n // 2
    cross = [x] + [
        lax.ppermute(x, axis, [(j, (j + 2 * s) % n) for j in range(n)]) for s in range(1, chips)
    ]
    partner_own = lax.ppermute(x, axis, [(j, j ^ 1) for j in range(n)])
    if chips > 1:
        relayed = lax.ppermute(jnp.stack(cross[1:], 0), axis, [(j, j ^ 1) for j in range(n)])
        partner = [partner_own] + [relayed[k] for k in range(chips - 1)]
    else:
        partner = [partner_own]
    pieces = jnp.stack(cross + partner, 0)
    j = jnp.arange(n)
    mine = (j % 2) == (me % 2)
    order = jnp.where(mine, ((me - j) % n) // 2, chips + (((me ^ 1) - j) % n) // 2)
    stacked = jnp.take(pieces, order, axis=0)
    return stacked.reshape((n * x.shape[0],) + x.shape[1:])


def body_heads(patches, queries, attn_keys, attn_values, out_weight, output_grad):
    factor = DH ** (-0.5)
    n, me = axis_size("col"), lax.axis_index("col")
    tokens, width_all = queries.shape[1], queries.shape[2]
    width = width_all // n
    heads = width // DH
    patch_here = patches[0]
    dense_grad = gather_rows_relayed(output_grad[0], "row")
    grad_other = swap_dp(output_grad)
    other_grad = gather_rows_relayed(grad_other[0], "row")
    qkv = jnp.stack([queries[0], attn_keys[0], attn_values[0]], 0)
    part = lambda g: lax.dynamic_slice_in_dim(qkv, g * width, width, 2)
    shapes = [(3, tokens, width), patch_here.shape]
    pieces = [(part(me), patch_here)]
    for s in range(1, n):
        got = shifted(flat(part((me + s) % n), patch_here), "col", s)
        pieces.append(tuple(unflat(got, shapes)))
    qkv_h = natural([p[0] for p in pieces], "col")
    every_patch = natural([p[1] for p in pieces], "col").reshape(n * tokens, -1)
    rows = n * tokens
    qkv_h = jnp.transpose(qkv_h, (1, 0, 2, 3)).reshape(3, rows, heads, DH)
    local_query, all_keys, all_values = qkv_h[0], qkv_h[1], qkv_h[2]
    scores = (
        jnp.einsum("qhd,khd->hqk", local_query, all_keys, preferred_element_type=jnp.float32)
        * factor
    )
    row_max = jnp.max(scores, axis=2, keepdims=True)
    log_total = row_max + jnp.log(jnp.sum(jnp.exp(scores - row_max), axis=2, keepdims=True))
    attn_probs = jnp.exp(scores - log_total).astype(jnp.bfloat16)
    attn_out = jnp.einsum(
        "hqk,khd->qhd", attn_probs, all_values, preferred_element_type=jnp.float32
    ).astype(jnp.bfloat16)
    grad_partial = lax.dot_general(
        dense_grad, out_weight, (((1,), (1,)), ((), ())), preferred_element_type=jnp.float32
    )
    attn_grad = sum_to_heads(grad_partial, "col").astype(jnp.bfloat16)
    grad_heads = attn_grad.reshape(rows, heads, DH)
    prob_grad = jnp.einsum(
        "qhd,khd->hqk", grad_heads, all_values, preferred_element_type=jnp.float32
    )
    row_dot = jnp.transpose(
        jnp.sum(grad_heads.astype(jnp.float32) * attn_out.astype(jnp.float32), axis=2)
    )[:, :, None]
    score_grad = (attn_probs.astype(jnp.float32) * (prob_grad - row_dot)).astype(jnp.bfloat16)
    query_grad = (
        jnp.einsum("hqk,khd->qhd", score_grad, all_keys, preferred_element_type=jnp.float32)
        * factor
    )
    key_grad = (
        jnp.einsum("hqk,qhd->khd", score_grad, local_query, preferred_element_type=jnp.float32)
        * factor
    )
    value_grad = jnp.einsum(
        "hqk,qhd->khd", attn_probs, grad_heads, preferred_element_type=jnp.float32
    )
    other_patch = swap_dp(every_patch)
    embed_weight_grad = contract_rows(every_patch, dense_grad) + contract_rows(
        other_patch, other_grad
    )
    out_flat = attn_out.reshape(rows, width)
    own_pair = (out_flat, swap_dp(out_flat))
    attn_grad, sent_out = lax.optimization_barrier((attn_grad, out_flat))
    out_pieces = [own_pair] + [
        (got, swap_dp(got)) for got in (shifted(sent_out, "col", s) for s in range(1, n))
    ]
    out_own = natural([p[0] for p in out_pieces], "col")
    out_other = natural([p[1] for p in out_pieces], "col")
    out_weight_grad = (
        lax.dot_general(out_own, dense_grad, (((1,), (0,)), ((), ())), preferred_element_type=jnp.float32)
        + lax.dot_general(out_other, other_grad, (((1,), (0,)), ((), ())), preferred_element_type=jnp.float32)
    ).reshape(width_all, -1)
    grads = jnp.stack([g.reshape(n, tokens, width) for g in (query_grad, key_grad, value_grad)], 1)
    grads, out_own = lax.optimization_barrier((grads, out_own))
    back = [grads[me]] + [
        shifted(grads[(me + s) % n].astype(jnp.bfloat16), "col", s).astype(jnp.float32)
        for s in range(1, n)
    ]
    back = jnp.transpose(natural(back, "col"), (1, 2, 0, 3)).reshape(3, 1, tokens, width_all)
    return (back[0], back[1], back[2], out_weight_grad, embed_weight_grad)


def body(patches, queries, attn_keys, attn_values, out_weight, output_grad):
    heads_here = queries.shape[2] // DH
    if heads_here % axis_size("col") == 0 and queries.shape[1] == output_grad.shape[1]:
        return body_heads(patches, queries, attn_keys, attn_values, out_weight, output_grad)
    return body_tokens(patches, queries, attn_keys, attn_values, out_weight, output_grad)


def solution(mesh):
    placed = (
        P("dp", "col", "row"),
        P("dp", "col", "row"),
        P("dp", "col", "row"),
        P("dp", "col", "row"),
        P("row", "col"),
        P("dp", "row", "col"),
    )
    return jax.shard_map(
        body,
        mesh=mesh,
        in_specs=placed,
        out_specs=(
            P("dp", "col", "row"),
            P("dp", "col", "row"),
            P("dp", "col", "row"),
            P("row", "col"),
            P("row", "col"),
        ),
        check_vma=False,
    )
```

```python
import jax
import numpy as np
import jax.numpy as jnp
from jax import lax
from jax.sharding import PartitionSpec as P

DH = 128


def contract_rows(left, right):
    return lax.dot_general(
        left, right, (((0,), (0,)), ((), ())), preferred_element_type=jnp.float32
    )


def swap_dp(x):
    return lax.ppermute(x, "dp", [(0, 1), (1, 0)])


def body_tokens(patches, queries, attn_keys, attn_values, out_weight, output_grad):
    factor = DH ** (-0.5)
    local_rows = queries.shape[1]
    feature_width = queries.shape[2]
    head_count = feature_width // DH
    grad_other = swap_dp(output_grad)
    patch_other = swap_dp(lax.all_gather(patches, "col", axis=1, tiled=True))
    every_key, every_value, every_patch = (
        lax.all_gather(attn_keys, "col", axis=1, tiled=True),
        lax.all_gather(attn_values, "col", axis=1, tiled=True),
        lax.all_gather(patches, "col", axis=1, tiled=True),
    )
    local_query = queries[0].reshape(local_rows, head_count, DH)
    all_keys = every_key[0].reshape(-1, head_count, DH)
    all_values = every_value[0].reshape(-1, head_count, DH)
    scores = (
        jnp.einsum("qhd,khd->hqk", local_query, all_keys, preferred_element_type=jnp.float32)
        * factor
    )
    row_max = jnp.max(scores, axis=2, keepdims=True)
    log_total = row_max + jnp.log(jnp.sum(jnp.exp(scores - row_max), axis=2, keepdims=True))
    attn_probs = jnp.exp(scores - log_total).astype(jnp.bfloat16)
    attn_out = jnp.einsum(
        "hqk,khd->qhd", attn_probs, all_values, preferred_element_type=jnp.float32
    ).astype(jnp.bfloat16)
    out_local = attn_out.reshape(1, local_rows, feature_width)
    dense_grad = lax.all_gather(output_grad, "row", axis=1, tiled=True)[0]
    attn_grad = lax.psum_scatter(
        lax.dot_general(
            dense_grad, out_weight, (((1,), (1,)), ((), ())), preferred_element_type=jnp.float32
        ),
        "col",
        scatter_dimension=0,
        tiled=True,
    ).astype(jnp.bfloat16)
    grad_heads = attn_grad.reshape(local_rows, head_count, DH)
    prob_grad = jnp.einsum(
        "qhd,khd->hqk", grad_heads, all_values, preferred_element_type=jnp.float32
    )
    row_dot = jnp.transpose(
        jnp.sum(grad_heads.astype(jnp.float32) * attn_out.astype(jnp.float32), axis=2)
    )[:, :, None]
    score_grad = (attn_probs.astype(jnp.float32) * (prob_grad - row_dot)).astype(jnp.bfloat16)
    query_grad = (
        jnp.einsum("hqk,khd->qhd", score_grad, all_keys, preferred_element_type=jnp.float32)
        * factor
    )
    every_out = lax.all_gather(out_local, "col", axis=1, tiled=True)
    key_term = (
        jnp.einsum("hqk,qhd->khd", score_grad, local_query, preferred_element_type=jnp.float32)
        * factor
    )
    value_term = jnp.einsum(
        "hqk,qhd->khd", attn_probs, grad_heads, preferred_element_type=jnp.float32
    )
    key_sum, value_sum = (
        lax.psum_scatter(
            key_term.reshape(-1, feature_width).astype(jnp.bfloat16),
            "col",
            scatter_dimension=0,
            tiled=True,
        ).astype(jnp.float32),
        lax.psum_scatter(
            value_term.reshape(-1, feature_width).astype(jnp.bfloat16),
            "col",
            scatter_dimension=0,
            tiled=True,
        ).astype(jnp.float32),
    )
    out_pair = jnp.concatenate([every_out, swap_dp(every_out)], axis=0)
    grad_pair = lax.all_gather(
        jnp.concatenate([output_grad, grad_other], axis=0), "row", axis=1, tiled=True
    )
    patch_pair = jnp.concatenate([every_patch, patch_other], axis=0)
    out_weight_grad = lax.dot_general(
        out_pair, grad_pair, (((0, 1), (0, 1)), ((), ())), preferred_element_type=jnp.float32
    )
    embed_weight_grad = lax.dot_general(
        patch_pair, grad_pair, (((0, 1), (0, 1)), ((), ())), preferred_element_type=jnp.float32
    )
    return (
        query_grad.reshape(1, local_rows, feature_width),
        key_sum.reshape(1, local_rows, feature_width),
        value_sum.reshape(1, local_rows, feature_width),
        out_weight_grad,
        embed_weight_grad,
    )


def axis_size(axis):
    return lax.psum(1, axis)


def shifted(x, axis, step):
    n = axis_size(axis)
    return lax.ppermute(x, axis, [(j, (j + step) % n) for j in range(n)])


def natural(pieces, axis):
    n = len(pieces)
    order = (lax.axis_index(axis) - jnp.arange(n)) % n
    return jnp.take(jnp.stack(pieces, 0), order, axis=0)


def gather_rows(x, axis):
    n = axis_size(axis)
    pieces = [x] + [shifted(x, axis, s) for s in range(1, n)]
    stacked = natural(pieces, axis)
    return stacked.reshape((n * x.shape[0],) + x.shape[1:])


def group_cols(x, axis, group):
    width = x.shape[1] // axis_size(axis)
    return lax.dynamic_slice_in_dim(x, group * width, width, 1)


def to_heads(x, axis):
    n, me = axis_size(axis), lax.axis_index(axis)
    pieces = [group_cols(x, axis, me)] + [
        shifted(group_cols(x, axis, (me + s) % n), axis, s) for s in range(1, n)
    ]
    stacked = natural(pieces, axis)
    return stacked.reshape((n * x.shape[0],) + stacked.shape[2:])


def from_heads(x, axis):
    n, me = axis_size(axis), lax.axis_index(axis)
    rows = x.shape[0] // n
    block = lambda k: lax.dynamic_slice_in_dim(x, k * rows, rows, 0)
    pieces = [block(me)] + [
        shifted(block((me + s) % n).astype(jnp.bfloat16), axis, s).astype(jnp.float32)
        for s in range(1, n)
    ]
    stacked = natural(pieces, axis)
    return jnp.transpose(stacked, (1, 0, 2)).reshape(rows, n * x.shape[1])


def sum_to_heads(partial, axis):
    n, me = axis_size(axis), lax.axis_index(axis)
    total = group_cols(partial, axis, me)
    for s in range(1, n):
        sent = group_cols(partial, axis, (me - s) % n).astype(jnp.bfloat16)
        total = total + shifted(sent, axis, -s % n).astype(jnp.float32)
    return total


def flat(*arrays):
    return jnp.concatenate([a.reshape(-1) for a in arrays])


def unflat(vector, shapes):
    out, at = [], 0
    for shape in shapes:
        size = int(np.prod(shape))
        out.append(vector[..., at:at + size].reshape(vector.shape[:-1] + shape))
        at += size
    return out


def gather_rows_relayed(x, axis):
    n, me = axis_size(axis), lax.axis_index(axis)
    chips = n // 2
    cross = [x] + [
        lax.ppermute(x, axis, [(j, (j + 2 * s) % n) for j in range(n)]) for s in range(1, chips)
    ]
    partner_own = lax.ppermute(x, axis, [(j, j ^ 1) for j in range(n)])
    if chips > 1:
        relayed = lax.ppermute(jnp.stack(cross[1:], 0), axis, [(j, j ^ 1) for j in range(n)])
        partner = [partner_own] + [relayed[k] for k in range(chips - 1)]
    else:
        partner = [partner_own]
    pieces = jnp.stack(cross + partner, 0)
    j = jnp.arange(n)
    mine = (j % 2) == (me % 2)
    order = jnp.where(mine, ((me - j) % n) // 2, chips + (((me ^ 1) - j) % n) // 2)
    stacked = jnp.take(pieces, order, axis=0)
    return stacked.reshape((n * x.shape[0],) + x.shape[1:])


def body_heads(patches, queries, attn_keys, attn_values, out_weight, output_grad):
    factor = DH ** (-0.5)
    n, me = axis_size("col"), lax.axis_index("col")
    tokens, width_all = queries.shape[1], queries.shape[2]
    width = width_all // n
    heads = width // DH
    patch_here = patches[0]
    dense_grad = gather_rows(output_grad[0], "row")
    grad_other = swap_dp(output_grad)
    other_grad = gather_rows(grad_other[0], "row")
    qkv = jnp.stack([queries[0], attn_keys[0], attn_values[0]], 0)
    part = lambda g: lax.dynamic_slice_in_dim(qkv, g * width, width, 2)
    shapes = [(3, tokens, width), patch_here.shape]
    pieces = [(part(me), patch_here)]
    for s in range(1, n):
        got = shifted(flat(part((me + s) % n), patch_here), "col", s)
        pieces.append(tuple(unflat(got, shapes)))
    qkv_h = natural([p[0] for p in pieces], "col")
    every_patch = natural([p[1] for p in pieces], "col").reshape(n * tokens, -1)
    rows = n * tokens
    qkv_h = jnp.transpose(qkv_h, (1, 0, 2, 3)).reshape(3, rows, heads, DH)
    local_query, all_keys, all_values = qkv_h[0], qkv_h[1], qkv_h[2]
    scores = (
        jnp.einsum("qhd,khd->hqk", local_query, all_keys, preferred_element_type=jnp.float32)
        * factor
    )
    row_max = jnp.max(scores, axis=2, keepdims=True)
    log_total = row_max + jnp.log(jnp.sum(jnp.exp(scores - row_max), axis=2, keepdims=True))
    attn_probs = jnp.exp(scores - log_total).astype(jnp.bfloat16)
    attn_out = jnp.einsum(
        "hqk,khd->qhd", attn_probs, all_values, preferred_element_type=jnp.float32
    ).astype(jnp.bfloat16)
    grad_partial = lax.dot_general(
        dense_grad, out_weight, (((1,), (1,)), ((), ())), preferred_element_type=jnp.float32
    )
    attn_grad = sum_to_heads(grad_partial, "col").astype(jnp.bfloat16)
    grad_heads = attn_grad.reshape(rows, heads, DH)
    prob_grad = jnp.einsum(
        "qhd,khd->hqk", grad_heads, all_values, preferred_element_type=jnp.float32
    )
    row_dot = jnp.transpose(
        jnp.sum(grad_heads.astype(jnp.float32) * attn_out.astype(jnp.float32), axis=2)
    )[:, :, None]
    score_grad = (attn_probs.astype(jnp.float32) * (prob_grad - row_dot)).astype(jnp.bfloat16)
    query_grad = (
        jnp.einsum("hqk,khd->qhd", score_grad, all_keys, preferred_element_type=jnp.float32)
        * factor
    )
    key_grad = (
        jnp.einsum("hqk,qhd->khd", score_grad, local_query, preferred_element_type=jnp.float32)
        * factor
    )
    value_grad = jnp.einsum(
        "hqk,qhd->khd", attn_probs, grad_heads, preferred_element_type=jnp.float32
    )
    other_patch = swap_dp(every_patch)
    embed_weight_grad = contract_rows(every_patch, dense_grad) + contract_rows(
        other_patch, other_grad
    )
    out_flat = attn_out.reshape(rows, width)
    cols = dense_grad.shape[1]

    def weight_rows(own, other):
        return lax.dot_general(
            own, dense_grad, (((0,), (0,)), ((), ())), preferred_element_type=jnp.float32
        ) + lax.dot_general(
            other, other_grad, (((0,), (0,)), ((), ())), preferred_element_type=jnp.float32
        )

    out_weight_grad = jnp.zeros((width_all, cols), jnp.float32)
    out_weight_grad = lax.dynamic_update_slice_in_dim(
        out_weight_grad, weight_rows(out_flat, swap_dp(out_flat)), me * width, 0
    )
    attn_grad, sent_out = lax.optimization_barrier((attn_grad, out_flat))
    arrived = []
    for s in range(1, n):
        got = shifted(sent_out, "col", s)
        arrived.append(got)
        out_weight_grad = lax.dynamic_update_slice_in_dim(
            out_weight_grad, weight_rows(got, swap_dp(got)), ((me - s) % n) * width, 0
        )
    grads = jnp.stack([g.reshape(n, tokens, width) for g in (query_grad, key_grad, value_grad)], 1)
    grads, arrived = lax.optimization_barrier((grads, arrived))
    pick = lambda k: lax.dynamic_index_in_dim(grads, k, 0, keepdims=False)
    back = jnp.zeros((3, tokens, width_all), jnp.float32)
    back = lax.dynamic_update_slice_in_dim(back, pick(me), me * width, 2)
    for s in range(1, n):
        got = shifted(pick((me + s) % n).astype(jnp.bfloat16), "col", s).astype(jnp.float32)
        back = lax.dynamic_update_slice_in_dim(back, got, ((me - s) % n) * width, 2)
    back = back.reshape(3, 1, tokens, width_all)
    return (back[0], back[1], back[2], out_weight_grad, embed_weight_grad)


def body(patches, queries, attn_keys, attn_values, out_weight, output_grad):
    heads_here = queries.shape[2] // DH
    if heads_here % axis_size("col") == 0 and queries.shape[1] == output_grad.shape[1]:
        return body_heads(patches, queries, attn_keys, attn_values, out_weight, output_grad)
    return body_tokens(patches, queries, attn_keys, attn_values, out_weight, output_grad)


def solution(mesh):
    placed = (
        P("dp", "col", "row"),
        P("dp", "col", "row"),
        P("dp", "col", "row"),
        P("dp", "col", "row"),
        P("row", "col"),
        P("dp", "row", "col"),
    )
    return jax.shard_map(
        body,
        mesh=mesh,
        in_specs=placed,
        out_specs=(
            P("dp", "col", "row"),
            P("dp", "col", "row"),
            P("dp", "col", "row"),
            P("row", "col"),
            P("row", "col"),
        ),
        check_vma=False,
    )
```

```python
import jax
import numpy as np
import jax.numpy as jnp
from jax import lax
from jax.sharding import PartitionSpec as P

DH = 128


def contract_rows(left, right):
    return lax.dot_general(
        left, right, (((0,), (0,)), ((), ())), preferred_element_type=jnp.float32
    )


def swap_dp(x):
    return lax.ppermute(x, "dp", [(0, 1), (1, 0)])


def body_tokens(patches, queries, attn_keys, attn_values, out_weight, output_grad):
    factor = DH ** (-0.5)
    local_rows = queries.shape[1]
    feature_width = queries.shape[2]
    head_count = feature_width // DH
    grad_other = swap_dp(output_grad)
    patch_other = swap_dp(lax.all_gather(patches, "col", axis=1, tiled=True))
    every_key, every_value, every_patch = (
        lax.all_gather(attn_keys, "col", axis=1, tiled=True),
        lax.all_gather(attn_values, "col", axis=1, tiled=True),
        lax.all_gather(patches, "col", axis=1, tiled=True),
    )
    local_query = queries[0].reshape(local_rows, head_count, DH)
    all_keys = every_key[0].reshape(-1, head_count, DH)
    all_values = every_value[0].reshape(-1, head_count, DH)
    scores = (
        jnp.einsum("qhd,khd->hqk", local_query, all_keys, preferred_element_type=jnp.float32)
        * factor
    )
    row_max = jnp.max(scores, axis=2, keepdims=True)
    log_total = row_max + jnp.log(jnp.sum(jnp.exp(scores - row_max), axis=2, keepdims=True))
    attn_probs = jnp.exp(scores - log_total).astype(jnp.bfloat16)
    attn_out = jnp.einsum(
        "hqk,khd->qhd", attn_probs, all_values, preferred_element_type=jnp.float32
    ).astype(jnp.bfloat16)
    out_local = attn_out.reshape(1, local_rows, feature_width)
    dense_grad = lax.all_gather(output_grad, "row", axis=1, tiled=True)[0]
    attn_grad = lax.psum_scatter(
        lax.dot_general(
            dense_grad, out_weight, (((1,), (1,)), ((), ())), preferred_element_type=jnp.float32
        ),
        "col",
        scatter_dimension=0,
        tiled=True,
    ).astype(jnp.bfloat16)
    grad_heads = attn_grad.reshape(local_rows, head_count, DH)
    prob_grad = jnp.einsum(
        "qhd,khd->hqk", grad_heads, all_values, preferred_element_type=jnp.float32
    )
    row_dot = jnp.transpose(
        jnp.sum(grad_heads.astype(jnp.float32) * attn_out.astype(jnp.float32), axis=2)
    )[:, :, None]
    score_grad = (attn_probs.astype(jnp.float32) * (prob_grad - row_dot)).astype(jnp.bfloat16)
    query_grad = (
        jnp.einsum("hqk,khd->qhd", score_grad, all_keys, preferred_element_type=jnp.float32)
        * factor
    )
    every_out = lax.all_gather(out_local, "col", axis=1, tiled=True)
    key_term = (
        jnp.einsum("hqk,qhd->khd", score_grad, local_query, preferred_element_type=jnp.float32)
        * factor
    )
    value_term = jnp.einsum(
        "hqk,qhd->khd", attn_probs, grad_heads, preferred_element_type=jnp.float32
    )
    key_sum, value_sum = (
        lax.psum_scatter(
            key_term.reshape(-1, feature_width).astype(jnp.bfloat16),
            "col",
            scatter_dimension=0,
            tiled=True,
        ).astype(jnp.float32),
        lax.psum_scatter(
            value_term.reshape(-1, feature_width).astype(jnp.bfloat16),
            "col",
            scatter_dimension=0,
            tiled=True,
        ).astype(jnp.float32),
    )
    out_pair = jnp.concatenate([every_out, swap_dp(every_out)], axis=0)
    grad_pair = lax.all_gather(
        jnp.concatenate([output_grad, grad_other], axis=0), "row", axis=1, tiled=True
    )
    patch_pair = jnp.concatenate([every_patch, patch_other], axis=0)
    out_weight_grad = lax.dot_general(
        out_pair, grad_pair, (((0, 1), (0, 1)), ((), ())), preferred_element_type=jnp.float32
    )
    embed_weight_grad = lax.dot_general(
        patch_pair, grad_pair, (((0, 1), (0, 1)), ((), ())), preferred_element_type=jnp.float32
    )
    return (
        query_grad.reshape(1, local_rows, feature_width),
        key_sum.reshape(1, local_rows, feature_width),
        value_sum.reshape(1, local_rows, feature_width),
        out_weight_grad,
        embed_weight_grad,
    )


def axis_size(axis):
    return lax.psum(1, axis)


def shifted(x, axis, step):
    n = axis_size(axis)
    return lax.ppermute(x, axis, [(j, (j + step) % n) for j in range(n)])


def natural(pieces, axis):
    n = len(pieces)
    order = (lax.axis_index(axis) - jnp.arange(n)) % n
    return jnp.take(jnp.stack(pieces, 0), order, axis=0)


def gather_rows(x, axis):
    n = axis_size(axis)
    pieces = [x] + [shifted(x, axis, s) for s in range(1, n)]
    stacked = natural(pieces, axis)
    return stacked.reshape((n * x.shape[0],) + x.shape[1:])


def group_cols(x, axis, group):
    width = x.shape[1] // axis_size(axis)
    return lax.dynamic_slice_in_dim(x, group * width, width, 1)


def to_heads(x, axis):
    n, me = axis_size(axis), lax.axis_index(axis)
    pieces = [group_cols(x, axis, me)] + [
        shifted(group_cols(x, axis, (me + s) % n), axis, s) for s in range(1, n)
    ]
    stacked = natural(pieces, axis)
    return stacked.reshape((n * x.shape[0],) + stacked.shape[2:])


def from_heads(x, axis):
    n, me = axis_size(axis), lax.axis_index(axis)
    rows = x.shape[0] // n
    block = lambda k: lax.dynamic_slice_in_dim(x, k * rows, rows, 0)
    pieces = [block(me)] + [
        shifted(block((me + s) % n).astype(jnp.bfloat16), axis, s).astype(jnp.float32)
        for s in range(1, n)
    ]
    stacked = natural(pieces, axis)
    return jnp.transpose(stacked, (1, 0, 2)).reshape(rows, n * x.shape[1])


def sum_to_heads(partial, axis):
    n, me = axis_size(axis), lax.axis_index(axis)
    total = group_cols(partial, axis, me)
    for s in range(1, n):
        sent = group_cols(partial, axis, (me - s) % n).astype(jnp.bfloat16)
        total = total + shifted(sent, axis, -s % n).astype(jnp.float32)
    return total


def flat(*arrays):
    return jnp.concatenate([a.reshape(-1) for a in arrays])


def unflat(vector, shapes):
    out, at = [], 0
    for shape in shapes:
        size = int(np.prod(shape))
        out.append(vector[..., at:at + size].reshape(vector.shape[:-1] + shape))
        at += size
    return out


def gather_rows_relayed(x, axis):
    n, me = axis_size(axis), lax.axis_index(axis)
    chips = n // 2
    cross = [x] + [
        lax.ppermute(x, axis, [(j, (j + 2 * s) % n) for j in range(n)]) for s in range(1, chips)
    ]
    partner_own = lax.ppermute(x, axis, [(j, j ^ 1) for j in range(n)])
    if chips > 1:
        relayed = lax.ppermute(jnp.stack(cross[1:], 0), axis, [(j, j ^ 1) for j in range(n)])
        partner = [partner_own] + [relayed[k] for k in range(chips - 1)]
    else:
        partner = [partner_own]
    pieces = jnp.stack(cross + partner, 0)
    j = jnp.arange(n)
    mine = (j % 2) == (me % 2)
    order = jnp.where(mine, ((me - j) % n) // 2, chips + (((me ^ 1) - j) % n) // 2)
    stacked = jnp.take(pieces, order, axis=0)
    return stacked.reshape((n * x.shape[0],) + x.shape[1:])


def body_heads(patches, queries, attn_keys, attn_values, out_weight, output_grad):
    factor = DH ** (-0.5)
    n, me = axis_size("col"), lax.axis_index("col")
    tokens, width_all = queries.shape[1], queries.shape[2]
    width = width_all // n
    heads = width // DH
    patch_here = patches[0]
    dense_grad = gather_rows(output_grad[0], "row")
    grad_other = swap_dp(output_grad)
    qkv = jnp.stack([queries[0], attn_keys[0], attn_values[0]], 0)
    part = lambda g: lax.dynamic_slice_in_dim(qkv, g * width, width, 2)
    shapes = [(3, tokens, width), patch_here.shape]
    pieces = [(part(me), patch_here)]
    for s in range(1, n):
        got = shifted(flat(part((me + s) % n), patch_here), "col", s)
        pieces.append(tuple(unflat(got, shapes)))
    qkv_h = natural([p[0] for p in pieces], "col")
    every_patch = natural([p[1] for p in pieces], "col").reshape(n * tokens, -1)
    rows = n * tokens
    qkv_h = jnp.transpose(qkv_h, (1, 0, 2, 3)).reshape(3, rows, heads, DH)
    local_query, all_keys, all_values = qkv_h[0], qkv_h[1], qkv_h[2]
    scores = (
        jnp.einsum("qhd,khd->hqk", local_query, all_keys, preferred_element_type=jnp.float32)
        * factor
    )
    row_max = jnp.max(scores, axis=2, keepdims=True)
    log_total = row_max + jnp.log(jnp.sum(jnp.exp(scores - row_max), axis=2, keepdims=True))
    attn_probs = jnp.exp(scores - log_total).astype(jnp.bfloat16)
    attn_out = jnp.einsum(
        "hqk,khd->qhd", attn_probs, all_values, preferred_element_type=jnp.float32
    ).astype(jnp.bfloat16)
    grad_partial = lax.dot_general(
        dense_grad, out_weight, (((1,), (1,)), ((), ())), preferred_element_type=jnp.float32
    )
    grad_partial, grad_other = lax.optimization_barrier((grad_partial, grad_other))
    other_grad = gather_rows(grad_other[0], "row")
    attn_grad = sum_to_heads(grad_partial, "col").astype(jnp.bfloat16)
    grad_heads = attn_grad.reshape(rows, heads, DH)
    prob_grad = jnp.einsum(
        "qhd,khd->hqk", grad_heads, all_values, preferred_element_type=jnp.float32
    )
    row_dot = jnp.transpose(
        jnp.sum(grad_heads.astype(jnp.float32) * attn_out.astype(jnp.float32), axis=2)
    )[:, :, None]
    score_grad = (attn_probs.astype(jnp.float32) * (prob_grad - row_dot)).astype(jnp.bfloat16)
    query_grad = (
        jnp.einsum("hqk,khd->qhd", score_grad, all_keys, preferred_element_type=jnp.float32)
        * factor
    )
    key_grad = (
        jnp.einsum("hqk,qhd->khd", score_grad, local_query, preferred_element_type=jnp.float32)
        * factor
    )
    value_grad = jnp.einsum(
        "hqk,qhd->khd", attn_probs, grad_heads, preferred_element_type=jnp.float32
    )
    other_patch = swap_dp(every_patch)
    embed_weight_grad = contract_rows(every_patch, dense_grad) + contract_rows(
        other_patch, other_grad
    )
    out_flat = attn_out.reshape(rows, width)
    own_pair = (out_flat, swap_dp(out_flat))
    attn_grad, sent_out = lax.optimization_barrier((attn_grad, out_flat))
    out_pieces = [own_pair] + [
        (got, swap_dp(got)) for got in (shifted(sent_out, "col", s) for s in range(1, n))
    ]
    out_own = natural([p[0] for p in out_pieces], "col")
    out_other = natural([p[1] for p in out_pieces], "col")
    out_weight_grad = (
        lax.dot_general(out_own, dense_grad, (((1,), (0,)), ((), ())), preferred_element_type=jnp.float32)
        + lax.dot_general(out_other, other_grad, (((1,), (0,)), ((), ())), preferred_element_type=jnp.float32)
    ).reshape(width_all, -1)
    grad_list = [g.reshape(n, tokens, width) for g in (query_grad, key_grad, value_grad)]
    sendable = jnp.stack([g.astype(jnp.bfloat16) for g in grad_list], 1)
    sendable, out_own = lax.optimization_barrier((sendable, out_own))
    back = jnp.zeros((3, tokens, width_all), jnp.float32)
    mine = jnp.stack([lax.dynamic_index_in_dim(g, me, 0, keepdims=False) for g in grad_list], 0)
    back = lax.dynamic_update_slice_in_dim(back, mine, me * width, 2)
    for s in range(1, n):
        piece = lax.dynamic_index_in_dim(sendable, (me + s) % n, 0, keepdims=False)
        got = shifted(piece, "col", s).astype(jnp.float32)
        back = lax.dynamic_update_slice_in_dim(back, got, ((me - s) % n) * width, 2)
    back = back.reshape(3, 1, tokens, width_all)
    return (back[0], back[1], back[2], out_weight_grad, embed_weight_grad)


def body(patches, queries, attn_keys, attn_values, out_weight, output_grad):
    heads_here = queries.shape[2] // DH
    if heads_here % axis_size("col") == 0 and queries.shape[1] == output_grad.shape[1]:
        return body_heads(patches, queries, attn_keys, attn_values, out_weight, output_grad)
    return body_tokens(patches, queries, attn_keys, attn_values, out_weight, output_grad)


def solution(mesh):
    placed = (
        P("dp", "col", "row"),
        P("dp", "col", "row"),
        P("dp", "col", "row"),
        P("dp", "col", "row"),
        P("row", "col"),
        P("dp", "row", "col"),
    )
    return jax.shard_map(
        body,
        mesh=mesh,
        in_specs=placed,
        out_specs=(
            P("dp", "col", "row"),
            P("dp", "col", "row"),
            P("dp", "col", "row"),
            P("row", "col"),
            P("row", "col"),
        ),
        check_vma=False,
    )
```

```python
import jax
import numpy as np
import jax.numpy as jnp
from jax import lax
from jax.sharding import PartitionSpec as P

DH = 128


def contract_rows(left, right):
    return lax.dot_general(
        left, right, (((0,), (0,)), ((), ())), preferred_element_type=jnp.float32
    )


def swap_dp(x):
    return lax.ppermute(x, "dp", [(0, 1), (1, 0)])


def body_tokens(patches, queries, attn_keys, attn_values, out_weight, output_grad):
    factor = DH ** (-0.5)
    local_rows = queries.shape[1]
    feature_width = queries.shape[2]
    head_count = feature_width // DH
    grad_other = swap_dp(output_grad)
    patch_other = swap_dp(lax.all_gather(patches, "col", axis=1, tiled=True))
    every_key, every_value, every_patch = (
        lax.all_gather(attn_keys, "col", axis=1, tiled=True),
        lax.all_gather(attn_values, "col", axis=1, tiled=True),
        lax.all_gather(patches, "col", axis=1, tiled=True),
    )
    local_query = queries[0].reshape(local_rows, head_count, DH)
    all_keys = every_key[0].reshape(-1, head_count, DH)
    all_values = every_value[0].reshape(-1, head_count, DH)
    scores = (
        jnp.einsum("qhd,khd->hqk", local_query, all_keys, preferred_element_type=jnp.float32)
        * factor
    )
    row_max = jnp.max(scores, axis=2, keepdims=True)
    log_total = row_max + jnp.log(jnp.sum(jnp.exp(scores - row_max), axis=2, keepdims=True))
    attn_probs = jnp.exp(scores - log_total).astype(jnp.bfloat16)
    attn_out = jnp.einsum(
        "hqk,khd->qhd", attn_probs, all_values, preferred_element_type=jnp.float32
    ).astype(jnp.bfloat16)
    out_local = attn_out.reshape(1, local_rows, feature_width)
    dense_grad = lax.all_gather(output_grad, "row", axis=1, tiled=True)[0]
    attn_grad = lax.psum_scatter(
        lax.dot_general(
            dense_grad, out_weight, (((1,), (1,)), ((), ())), preferred_element_type=jnp.float32
        ),
        "col",
        scatter_dimension=0,
        tiled=True,
    ).astype(jnp.bfloat16)
    grad_heads = attn_grad.reshape(local_rows, head_count, DH)
    prob_grad = jnp.einsum(
        "qhd,khd->hqk", grad_heads, all_values, preferred_element_type=jnp.float32
    )
    row_dot = jnp.transpose(
        jnp.sum(grad_heads.astype(jnp.float32) * attn_out.astype(jnp.float32), axis=2)
    )[:, :, None]
    score_grad = (attn_probs.astype(jnp.float32) * (prob_grad - row_dot)).astype(jnp.bfloat16)
    query_grad = (
        jnp.einsum("hqk,khd->qhd", score_grad, all_keys, preferred_element_type=jnp.float32)
        * factor
    )
    every_out = lax.all_gather(out_local, "col", axis=1, tiled=True)
    key_term = (
        jnp.einsum("hqk,qhd->khd", score_grad, local_query, preferred_element_type=jnp.float32)
        * factor
    )
    value_term = jnp.einsum(
        "hqk,qhd->khd", attn_probs, grad_heads, preferred_element_type=jnp.float32
    )
    key_sum, value_sum = (
        lax.psum_scatter(
            key_term.reshape(-1, feature_width).astype(jnp.bfloat16),
            "col",
            scatter_dimension=0,
            tiled=True,
        ).astype(jnp.float32),
        lax.psum_scatter(
            value_term.reshape(-1, feature_width).astype(jnp.bfloat16),
            "col",
            scatter_dimension=0,
            tiled=True,
        ).astype(jnp.float32),
    )
    out_pair = jnp.concatenate([every_out, swap_dp(every_out)], axis=0)
    grad_pair = lax.all_gather(
        jnp.concatenate([output_grad, grad_other], axis=0), "row", axis=1, tiled=True
    )
    patch_pair = jnp.concatenate([every_patch, patch_other], axis=0)
    out_weight_grad = lax.dot_general(
        out_pair, grad_pair, (((0, 1), (0, 1)), ((), ())), preferred_element_type=jnp.float32
    )
    embed_weight_grad = lax.dot_general(
        patch_pair, grad_pair, (((0, 1), (0, 1)), ((), ())), preferred_element_type=jnp.float32
    )
    return (
        query_grad.reshape(1, local_rows, feature_width),
        key_sum.reshape(1, local_rows, feature_width),
        value_sum.reshape(1, local_rows, feature_width),
        out_weight_grad,
        embed_weight_grad,
    )


def axis_size(axis):
    return lax.psum(1, axis)


def shifted(x, axis, step):
    n = axis_size(axis)
    return lax.ppermute(x, axis, [(j, (j + step) % n) for j in range(n)])


def natural(pieces, axis):
    n = len(pieces)
    order = (lax.axis_index(axis) - jnp.arange(n)) % n
    return jnp.take(jnp.stack(pieces, 0), order, axis=0)


def gather_rows(x, axis):
    n = axis_size(axis)
    pieces = [x] + [shifted(x, axis, s) for s in range(1, n)]
    stacked = natural(pieces, axis)
    return stacked.reshape((n * x.shape[0],) + x.shape[1:])


def group_cols(x, axis, group):
    width = x.shape[1] // axis_size(axis)
    return lax.dynamic_slice_in_dim(x, group * width, width, 1)


def to_heads(x, axis):
    n, me = axis_size(axis), lax.axis_index(axis)
    pieces = [group_cols(x, axis, me)] + [
        shifted(group_cols(x, axis, (me + s) % n), axis, s) for s in range(1, n)
    ]
    stacked = natural(pieces, axis)
    return stacked.reshape((n * x.shape[0],) + stacked.shape[2:])


def from_heads(x, axis):
    n, me = axis_size(axis), lax.axis_index(axis)
    rows = x.shape[0] // n
    block = lambda k: lax.dynamic_slice_in_dim(x, k * rows, rows, 0)
    pieces = [block(me)] + [
        shifted(block((me + s) % n).astype(jnp.bfloat16), axis, s).astype(jnp.float32)
        for s in range(1, n)
    ]
    stacked = natural(pieces, axis)
    return jnp.transpose(stacked, (1, 0, 2)).reshape(rows, n * x.shape[1])


def sum_to_heads(partial, axis):
    n, me = axis_size(axis), lax.axis_index(axis)
    total = group_cols(partial, axis, me)
    for s in range(1, n):
        sent = group_cols(partial, axis, (me - s) % n).astype(jnp.bfloat16)
        total = total + shifted(sent, axis, -s % n).astype(jnp.float32)
    return total


def flat(*arrays):
    return jnp.concatenate([a.reshape(-1) for a in arrays])


def unflat(vector, shapes):
    out, at = [], 0
    for shape in shapes:
        size = int(np.prod(shape))
        out.append(vector[..., at:at + size].reshape(vector.shape[:-1] + shape))
        at += size
    return out


def gather_rows_relayed(x, axis):
    n, me = axis_size(axis), lax.axis_index(axis)
    chips = n // 2
    cross = [x] + [
        lax.ppermute(x, axis, [(j, (j + 2 * s) % n) for j in range(n)]) for s in range(1, chips)
    ]
    partner_own = lax.ppermute(x, axis, [(j, j ^ 1) for j in range(n)])
    if chips > 1:
        relayed = lax.ppermute(jnp.stack(cross[1:], 0), axis, [(j, j ^ 1) for j in range(n)])
        partner = [partner_own] + [relayed[k] for k in range(chips - 1)]
    else:
        partner = [partner_own]
    pieces = jnp.stack(cross + partner, 0)
    j = jnp.arange(n)
    mine = (j % 2) == (me % 2)
    order = jnp.where(mine, ((me - j) % n) // 2, chips + (((me ^ 1) - j) % n) // 2)
    stacked = jnp.take(pieces, order, axis=0)
    return stacked.reshape((n * x.shape[0],) + x.shape[1:])


def roll_blocks(x, shift):
    n = x.shape[0]
    return lax.dynamic_slice_in_dim(jnp.concatenate([x, x], 0), shift % n, n, 0)


def body_heads(patches, queries, attn_keys, attn_values, out_weight, output_grad):
    factor = DH ** (-0.5)
    n, me = axis_size("col"), lax.axis_index("col")
    rank = lax.axis_index("row")
    tokens, width_all = queries.shape[1], queries.shape[2]
    width = width_all // n
    heads = width // DH
    patch_here = patches[0]
    grad_blocks = [output_grad[0]] + [shifted(output_grad[0], "row", s) for s in range(1, n)]
    dense_grad = jnp.concatenate(grad_blocks, 0)
    grad_other = swap_dp(output_grad)
    qkv = jnp.stack([queries[0], attn_keys[0], attn_values[0]], 0)
    part = lambda g: lax.dynamic_slice_in_dim(qkv, g * width, width, 2)
    shapes = [(3, tokens, width), patch_here.shape]
    pieces = [(part(me), patch_here)]
    for s in range(1, n):
        got = shifted(flat(part((me + s) % n), patch_here), "col", s)
        pieces.append(tuple(unflat(got, shapes)))
    order = me - rank
    qkv_h = roll_blocks(jnp.stack([p[0] for p in pieces], 0), order)
    every_patch = roll_blocks(jnp.stack([p[1] for p in pieces], 0), order).reshape(n * tokens, -1)
    rows = n * tokens
    qkv_h = jnp.transpose(qkv_h, (1, 0, 2, 3)).reshape(3, rows, heads, DH)
    local_query, all_keys, all_values = qkv_h[0], qkv_h[1], qkv_h[2]
    grad_partial = lax.dot_general(
        dense_grad, out_weight, (((1,), (1,)), ((), ())), preferred_element_type=jnp.float32
    )
    grad_partial, grad_other = lax.optimization_barrier((grad_partial, grad_other))
    other_blocks = [grad_other[0]] + [shifted(grad_other[0], "row", s) for s in range(1, n)]
    scores = (
        jnp.einsum("qhd,khd->hqk", local_query, all_keys, preferred_element_type=jnp.float32)
        * factor
    )
    row_max = jnp.max(scores, axis=2, keepdims=True)
    log_total = row_max + jnp.log(jnp.sum(jnp.exp(scores - row_max), axis=2, keepdims=True))
    attn_probs = jnp.exp(scores - log_total).astype(jnp.bfloat16)
    attn_out = jnp.einsum(
        "hqk,khd->qhd", attn_probs, all_values, preferred_element_type=jnp.float32
    ).astype(jnp.bfloat16)
    attn_grad = sum_to_heads(grad_partial, "col").astype(jnp.bfloat16)
    grad_heads = attn_grad.reshape(rows, heads, DH)
    prob_grad = jnp.einsum(
        "qhd,khd->hqk", grad_heads, all_values, preferred_element_type=jnp.float32
    )
    row_dot = jnp.transpose(
        jnp.sum(grad_heads.astype(jnp.float32) * attn_out.astype(jnp.float32), axis=2)
    )[:, :, None]
    score_grad = (attn_probs.astype(jnp.float32) * (prob_grad - row_dot)).astype(jnp.bfloat16)
    query_grad = (
        jnp.einsum("hqk,khd->qhd", score_grad, all_keys, preferred_element_type=jnp.float32)
        * factor
    )
    key_grad = (
        jnp.einsum("hqk,qhd->khd", score_grad, local_query, preferred_element_type=jnp.float32)
        * factor
    )
    value_grad = jnp.einsum(
        "hqk,qhd->khd", attn_probs, grad_heads, preferred_element_type=jnp.float32
    )
    other_patch = swap_dp(every_patch)
    out_flat = attn_out.reshape(rows, width)
    own_pair = (out_flat, swap_dp(out_flat))
    attn_grad, sent_out = lax.optimization_barrier((attn_grad, out_flat))
    out_pieces = [own_pair] + [
        (got, swap_dp(got)) for got in (shifted(sent_out, "col", -s % n) for s in range(1, n))
    ]
    out_both = roll_blocks(
        jnp.stack([jnp.concatenate(p, 0) for p in out_pieces], 0), -me
    )
    grad_both = jnp.concatenate([dense_grad] + other_blocks, 0)
    out_weight_grad = lax.dot_general(
        out_both, grad_both, (((1,), (0,)), ((), ())), preferred_element_type=jnp.float32
    ).reshape(width_all, -1)
    embed_weight_grad = contract_rows(jnp.concatenate([every_patch, other_patch], 0), grad_both)
    grad_list = [g.reshape(n, tokens, width) for g in (query_grad, key_grad, value_grad)]
    sendable = roll_blocks(
        jnp.stack([g.astype(jnp.bfloat16) for g in grad_list], 1), rank - me
    )
    sendable, out_both = lax.optimization_barrier((sendable, out_both))
    mine = jnp.stack(
        [lax.dynamic_index_in_dim(g, (rank - me) % n, 0, keepdims=False) for g in grad_list], 0
    )
    back = jnp.zeros((3, tokens, width_all), jnp.float32)
    back = lax.dynamic_update_slice_in_dim(back, mine, me * width, 2)
    for s in range(1, n):
        got = shifted(sendable[s], "col", -s % n).astype(jnp.float32)
        back = lax.dynamic_update_slice_in_dim(back, got, ((me + s) % n) * width, 2)
    back = back.reshape(3, 1, tokens, width_all)
    return (back[0], back[1], back[2], out_weight_grad, embed_weight_grad)


def body(patches, queries, attn_keys, attn_values, out_weight, output_grad):
    heads_here = queries.shape[2] // DH
    if (
        heads_here % axis_size("col") == 0
        and queries.shape[1] == output_grad.shape[1]
        and axis_size("row") == axis_size("col")
    ):
        return body_heads(patches, queries, attn_keys, attn_values, out_weight, output_grad)
    return body_tokens(patches, queries, attn_keys, attn_values, out_weight, output_grad)


def solution(mesh):
    placed = (
        P("dp", "col", "row"),
        P("dp", "col", "row"),
        P("dp", "col", "row"),
        P("dp", "col", "row"),
        P("row", "col"),
        P("dp", "row", "col"),
    )
    return jax.shard_map(
        body,
        mesh=mesh,
        in_specs=placed,
        out_specs=(
            P("dp", "col", "row"),
            P("dp", "col", "row"),
            P("dp", "col", "row"),
            P("row", "col"),
            P("row", "col"),
        ),
        check_vma=False,
    )
```

```python
import functools

import jax
import numpy as np
import jax.numpy as jnp
from jax import lax
from jax.experimental import pallas as pl
from jax.experimental.pallas import tpu as pltpu
from jax.sharding import PartitionSpec as P

DH = 128


def contract_rows(left, right):
    return lax.dot_general(
        left, right, (((0,), (0,)), ((), ())), preferred_element_type=jnp.float32
    )


def swap_dp(x):
    return lax.ppermute(x, "dp", [(0, 1), (1, 0)])


def body_tokens(patches, queries, attn_keys, attn_values, out_weight, output_grad):
    factor = DH ** (-0.5)
    local_rows = queries.shape[1]
    feature_width = queries.shape[2]
    head_count = feature_width // DH
    grad_other = swap_dp(output_grad)
    patch_other = swap_dp(lax.all_gather(patches, "col", axis=1, tiled=True))
    every_key, every_value, every_patch = (
        lax.all_gather(attn_keys, "col", axis=1, tiled=True),
        lax.all_gather(attn_values, "col", axis=1, tiled=True),
        lax.all_gather(patches, "col", axis=1, tiled=True),
    )
    local_query = queries[0].reshape(local_rows, head_count, DH)
    all_keys = every_key[0].reshape(-1, head_count, DH)
    all_values = every_value[0].reshape(-1, head_count, DH)
    scores = (
        jnp.einsum("qhd,khd->hqk", local_query, all_keys, preferred_element_type=jnp.float32)
        * factor
    )
    row_max = jnp.max(scores, axis=2, keepdims=True)
    log_total = row_max + jnp.log(jnp.sum(jnp.exp(scores - row_max), axis=2, keepdims=True))
    attn_probs = jnp.exp(scores - log_total).astype(jnp.bfloat16)
    attn_out = jnp.einsum(
        "hqk,khd->qhd", attn_probs, all_values, preferred_element_type=jnp.float32
    ).astype(jnp.bfloat16)
    out_local = attn_out.reshape(1, local_rows, feature_width)
    dense_grad = lax.all_gather(output_grad, "row", axis=1, tiled=True)[0]
    attn_grad = lax.psum_scatter(
        lax.dot_general(
            dense_grad, out_weight, (((1,), (1,)), ((), ())), preferred_element_type=jnp.float32
        ),
        "col",
        scatter_dimension=0,
        tiled=True,
    ).astype(jnp.bfloat16)
    grad_heads = attn_grad.reshape(local_rows, head_count, DH)
    prob_grad = jnp.einsum(
        "qhd,khd->hqk", grad_heads, all_values, preferred_element_type=jnp.float32
    )
    row_dot = jnp.transpose(
        jnp.sum(grad_heads.astype(jnp.float32) * attn_out.astype(jnp.float32), axis=2)
    )[:, :, None]
    score_grad = (attn_probs.astype(jnp.float32) * (prob_grad - row_dot)).astype(jnp.bfloat16)
    query_grad = (
        jnp.einsum("hqk,khd->qhd", score_grad, all_keys, preferred_element_type=jnp.float32)
        * factor
    )
    every_out = lax.all_gather(out_local, "col", axis=1, tiled=True)
    key_term = (
        jnp.einsum("hqk,qhd->khd", score_grad, local_query, preferred_element_type=jnp.float32)
        * factor
    )
    value_term = jnp.einsum(
        "hqk,qhd->khd", attn_probs, grad_heads, preferred_element_type=jnp.float32
    )
    key_sum, value_sum = (
        lax.psum_scatter(
            key_term.reshape(-1, feature_width).astype(jnp.bfloat16),
            "col",
            scatter_dimension=0,
            tiled=True,
        ).astype(jnp.float32),
        lax.psum_scatter(
            value_term.reshape(-1, feature_width).astype(jnp.bfloat16),
            "col",
            scatter_dimension=0,
            tiled=True,
        ).astype(jnp.float32),
    )
    out_pair = jnp.concatenate([every_out, swap_dp(every_out)], axis=0)
    grad_pair = lax.all_gather(
        jnp.concatenate([output_grad, grad_other], axis=0), "row", axis=1, tiled=True
    )
    patch_pair = jnp.concatenate([every_patch, patch_other], axis=0)
    out_weight_grad = lax.dot_general(
        out_pair, grad_pair, (((0, 1), (0, 1)), ((), ())), preferred_element_type=jnp.float32
    )
    embed_weight_grad = lax.dot_general(
        patch_pair, grad_pair, (((0, 1), (0, 1)), ((), ())), preferred_element_type=jnp.float32
    )
    return (
        query_grad.reshape(1, local_rows, feature_width),
        key_sum.reshape(1, local_rows, feature_width),
        value_sum.reshape(1, local_rows, feature_width),
        out_weight_grad,
        embed_weight_grad,
    )


def axis_size(axis):
    return lax.psum(1, axis)


def shifted(x, axis, step):
    n = axis_size(axis)
    return lax.ppermute(x, axis, [(j, (j + step) % n) for j in range(n)])


def natural(pieces, axis):
    n = len(pieces)
    order = (lax.axis_index(axis) - jnp.arange(n)) % n
    return jnp.take(jnp.stack(pieces, 0), order, axis=0)


def gather_rows(x, axis):
    n = axis_size(axis)
    pieces = [x] + [shifted(x, axis, s) for s in range(1, n)]
    stacked = natural(pieces, axis)
    return stacked.reshape((n * x.shape[0],) + x.shape[1:])


def group_cols(x, axis, group):
    width = x.shape[1] // axis_size(axis)
    return lax.dynamic_slice_in_dim(x, group * width, width, 1)


def to_heads(x, axis):
    n, me = axis_size(axis), lax.axis_index(axis)
    pieces = [group_cols(x, axis, me)] + [
        shifted(group_cols(x, axis, (me + s) % n), axis, s) for s in range(1, n)
    ]
    stacked = natural(pieces, axis)
    return stacked.reshape((n * x.shape[0],) + stacked.shape[2:])


def from_heads(x, axis):
    n, me = axis_size(axis), lax.axis_index(axis)
    rows = x.shape[0] // n
    block = lambda k: lax.dynamic_slice_in_dim(x, k * rows, rows, 0)
    pieces = [block(me)] + [
        shifted(block((me + s) % n).astype(jnp.bfloat16), axis, s).astype(jnp.float32)
        for s in range(1, n)
    ]
    stacked = natural(pieces, axis)
    return jnp.transpose(stacked, (1, 0, 2)).reshape(rows, n * x.shape[1])


def sum_to_heads(partial, axis):
    n, me = axis_size(axis), lax.axis_index(axis)
    total = group_cols(partial, axis, me)
    for s in range(1, n):
        sent = group_cols(partial, axis, (me - s) % n).astype(jnp.bfloat16)
        total = total + shifted(sent, axis, -s % n).astype(jnp.float32)
    return total


def flat(*arrays):
    return jnp.concatenate([a.reshape(-1) for a in arrays])


def unflat(vector, shapes):
    out, at = [], 0
    for shape in shapes:
        size = int(np.prod(shape))
        out.append(vector[..., at:at + size].reshape(vector.shape[:-1] + shape))
        at += size
    return out


def gather_rows_relayed(x, axis):
    n, me = axis_size(axis), lax.axis_index(axis)
    chips = n // 2
    cross = [x] + [
        lax.ppermute(x, axis, [(j, (j + 2 * s) % n) for j in range(n)]) for s in range(1, chips)
    ]
    partner_own = lax.ppermute(x, axis, [(j, j ^ 1) for j in range(n)])
    if chips > 1:
        relayed = lax.ppermute(jnp.stack(cross[1:], 0), axis, [(j, j ^ 1) for j in range(n)])
        partner = [partner_own] + [relayed[k] for k in range(chips - 1)]
    else:
        partner = [partner_own]
    pieces = jnp.stack(cross + partner, 0)
    j = jnp.arange(n)
    mine = (j % 2) == (me % 2)
    order = jnp.where(mine, ((me - j) % n) // 2, chips + (((me ^ 1) - j) % n) // 2)
    stacked = jnp.take(pieces, order, axis=0)
    return stacked.reshape((n * x.shape[0],) + x.shape[1:])


def _wg_kernel(nblk, blk, shift_ref, lhs_ref, *refs):
    grads, out_ref = refs[:nblk], refs[nblk]
    acc = None
    for k in range(nblk):
        part = lax.dot_general(
            lhs_ref[0, k * blk:(k + 1) * blk, :], grads[k][...],
            (((0,), (0,)), ((), ())), preferred_element_type=jnp.float32,
        )
        acc = part if acc is None else acc + part
    out_ref[...] = acc


def weight_grad(lhs, grads, shift, tile=768):
    slots, toks, m = lhs.shape
    nblk = len(grads)
    blk, cols = grads[0].shape
    tile = tile if cols % tile == 0 else cols
    grid = (slots, cols // tile)
    in_specs = [pl.BlockSpec((1, toks, m), lambda s, j, sh: (s, 0, 0))] + [
        pl.BlockSpec((blk, tile), lambda s, j, sh: (0, j)) for _ in range(nblk)
    ]
    out_spec = pl.BlockSpec((m, tile), lambda s, j, sh: ((s + sh[0]) % slots, j))
    return pl.pallas_call(
        functools.partial(_wg_kernel, nblk, blk),
        out_shape=jax.ShapeDtypeStruct((slots * m, cols), jnp.float32),
        grid_spec=pltpu.PrefetchScalarGridSpec(
            num_scalar_prefetch=1, grid=grid, in_specs=in_specs, out_specs=out_spec
        ),
        cost_estimate=pl.CostEstimate(
            flops=2 * slots * toks * m * cols, transcendentals=0,
            bytes_accessed=2 * slots * toks * m + 2 * toks * cols + 4 * slots * m * cols,
        ),
    )(jnp.reshape(shift, (1,)).astype(jnp.int32), lhs, *grads)


def roll_blocks(x, shift):
    n = x.shape[0]
    return lax.dynamic_slice_in_dim(jnp.concatenate([x, x], 0), shift % n, n, 0)


def body_heads(patches, queries, attn_keys, attn_values, out_weight, output_grad):
    factor = DH ** (-0.5)
    n, me = axis_size("col"), lax.axis_index("col")
    rank = lax.axis_index("row")
    tokens, width_all = queries.shape[1], queries.shape[2]
    width = width_all // n
    heads = width // DH
    patch_here = patches[0]
    grad_blocks = [output_grad[0]] + [shifted(output_grad[0], "row", s) for s in range(1, n)]
    grad_other = swap_dp(output_grad)
    qkv = jnp.stack([queries[0], attn_keys[0], attn_values[0]], 0)
    part = lambda g: lax.dynamic_slice_in_dim(qkv, g * width, width, 2)
    shapes = [(3, tokens, width), patch_here.shape]
    pieces = [(part(me), patch_here)]
    for s in range(1, n):
        got = shifted(flat(part((me + s) % n), patch_here), "col", s)
        pieces.append(tuple(unflat(got, shapes)))
    order = me - rank
    qkv_h = roll_blocks(jnp.stack([p[0] for p in pieces], 0), order)
    every_patch = roll_blocks(jnp.stack([p[1] for p in pieces], 0), order).reshape(n * tokens, -1)
    rows = n * tokens
    qkv_h = jnp.transpose(qkv_h, (1, 0, 2, 3)).reshape(3, rows, heads, DH)
    local_query, all_keys, all_values = qkv_h[0], qkv_h[1], qkv_h[2]
    grad_partial = [
        lax.dot_general(g, out_weight, (((1,), (1,)), ((), ())), preferred_element_type=jnp.float32)
        for g in grad_blocks
    ]
    grad_partial, grad_other = lax.optimization_barrier((grad_partial, grad_other))
    other_blocks = [grad_other[0]] + [shifted(grad_other[0], "row", s) for s in range(1, n)]
    scores = (
        jnp.einsum("qhd,khd->hqk", local_query, all_keys, preferred_element_type=jnp.float32)
        * factor
    )
    row_max = jnp.max(scores, axis=2, keepdims=True)
    log_total = row_max + jnp.log(jnp.sum(jnp.exp(scores - row_max), axis=2, keepdims=True))
    attn_probs = jnp.exp(scores - log_total).astype(jnp.bfloat16)
    attn_out = jnp.einsum(
        "hqk,khd->qhd", attn_probs, all_values, preferred_element_type=jnp.float32
    ).astype(jnp.bfloat16)
    group_rows = lambda g: jnp.concatenate([group_cols(p, "col", g) for p in grad_partial], 0)
    attn_grad = group_rows(me)
    for s in range(1, n):
        sent = group_rows((me - s) % n).astype(jnp.bfloat16)
        attn_grad = attn_grad + shifted(sent, "col", -s % n).astype(jnp.float32)
    attn_grad = attn_grad.astype(jnp.bfloat16)
    grad_heads = attn_grad.reshape(rows, heads, DH)
    prob_grad = jnp.einsum(
        "qhd,khd->hqk", grad_heads, all_values, preferred_element_type=jnp.float32
    )
    row_dot = jnp.transpose(
        jnp.sum(grad_heads.astype(jnp.float32) * attn_out.astype(jnp.float32), axis=2)
    )[:, :, None]
    score_grad = (attn_probs.astype(jnp.float32) * (prob_grad - row_dot)).astype(jnp.bfloat16)
    query_grad = (
        jnp.einsum("hqk,khd->qhd", score_grad, all_keys, preferred_element_type=jnp.float32)
        * factor
    )
    key_grad = (
        jnp.einsum("hqk,qhd->khd", score_grad, local_query, preferred_element_type=jnp.float32)
        * factor
    )
    value_grad = jnp.einsum(
        "hqk,qhd->khd", attn_probs, grad_heads, preferred_element_type=jnp.float32
    )
    other_patch = swap_dp(every_patch)
    out_flat = attn_out.reshape(rows, width)
    own_pair = (out_flat, swap_dp(out_flat))
    attn_grad, sent_out = lax.optimization_barrier((attn_grad, out_flat))
    out_pieces = [own_pair] + [
        (got, swap_dp(got)) for got in (shifted(sent_out, "col", -s % n) for s in range(1, n))
    ]
    out_both = jnp.stack([jnp.concatenate(p, 0) for p in out_pieces], 0)
    grad_both = grad_blocks + other_blocks
    out_weight_grad = weight_grad(out_both, grad_both, me)
    embed_weight_grad = weight_grad(
        jnp.concatenate([every_patch, other_patch], 0)[None], grad_both, jnp.int32(0)
    )
    grad_list = [g.reshape(n, tokens, width) for g in (query_grad, key_grad, value_grad)]
    sendable = roll_blocks(
        jnp.stack([g.astype(jnp.bfloat16) for g in grad_list], 1), rank - me
    )
    sendable, out_both = lax.optimization_barrier((sendable, out_both))
    mine = jnp.stack(
        [lax.dynamic_index_in_dim(g, (rank - me) % n, 0, keepdims=False) for g in grad_list], 0
    )
    back = jnp.zeros((3, tokens, width_all), jnp.float32)
    back = lax.dynamic_update_slice_in_dim(back, mine, me * width, 2)
    for s in range(1, n):
        got = shifted(sendable[s], "col", -s % n).astype(jnp.float32)
        back = lax.dynamic_update_slice_in_dim(back, got, ((me + s) % n) * width, 2)
    back = back.reshape(3, 1, tokens, width_all)
    return (back[0], back[1], back[2], out_weight_grad, embed_weight_grad)


def body(patches, queries, attn_keys, attn_values, out_weight, output_grad):
    heads_here = queries.shape[2] // DH
    if (
        heads_here % axis_size("col") == 0
        and queries.shape[1] == output_grad.shape[1]
        and axis_size("row") == axis_size("col")
    ):
        return body_heads(patches, queries, attn_keys, attn_values, out_weight, output_grad)
    return body_tokens(patches, queries, attn_keys, attn_values, out_weight, output_grad)


def solution(mesh):
    placed = (
        P("dp", "col", "row"),
        P("dp", "col", "row"),
        P("dp", "col", "row"),
        P("dp", "col", "row"),
        P("row", "col"),
        P("dp", "row", "col"),
    )
    return jax.shard_map(
        body,
        mesh=mesh,
        in_specs=placed,
        out_specs=(
            P("dp", "col", "row"),
            P("dp", "col", "row"),
            P("dp", "col", "row"),
            P("row", "col"),
            P("row", "col"),
        ),
        check_vma=False,
    )
```

```python
import jax
import numpy as np
import jax.numpy as jnp
from jax import lax
from jax.sharding import PartitionSpec as P

DH = 128


def contract_rows(left, right):
    return lax.dot_general(
        left, right, (((0,), (0,)), ((), ())), preferred_element_type=jnp.float32
    )


def swap_dp(x):
    return lax.ppermute(x, "dp", [(0, 1), (1, 0)])


def body_tokens(patches, queries, attn_keys, attn_values, out_weight, output_grad):
    factor = DH ** (-0.5)
    local_rows = queries.shape[1]
    feature_width = queries.shape[2]
    head_count = feature_width // DH
    grad_other = swap_dp(output_grad)
    patch_other = swap_dp(lax.all_gather(patches, "col", axis=1, tiled=True))
    every_key, every_value, every_patch = (
        lax.all_gather(attn_keys, "col", axis=1, tiled=True),
        lax.all_gather(attn_values, "col", axis=1, tiled=True),
        lax.all_gather(patches, "col", axis=1, tiled=True),
    )
    local_query = queries[0].reshape(local_rows, head_count, DH)
    all_keys = every_key[0].reshape(-1, head_count, DH)
    all_values = every_value[0].reshape(-1, head_count, DH)
    scores = (
        jnp.einsum("qhd,khd->hqk", local_query, all_keys, preferred_element_type=jnp.float32)
        * factor
    )
    row_max = jnp.max(scores, axis=2, keepdims=True)
    log_total = row_max + jnp.log(jnp.sum(jnp.exp(scores - row_max), axis=2, keepdims=True))
    attn_probs = jnp.exp(scores - log_total).astype(jnp.bfloat16)
    attn_out = jnp.einsum(
        "hqk,khd->qhd", attn_probs, all_values, preferred_element_type=jnp.float32
    ).astype(jnp.bfloat16)
    out_local = attn_out.reshape(1, local_rows, feature_width)
    dense_grad = lax.all_gather(output_grad, "row", axis=1, tiled=True)[0]
    attn_grad = lax.psum_scatter(
        lax.dot_general(
            dense_grad, out_weight, (((1,), (1,)), ((), ())), preferred_element_type=jnp.float32
        ),
        "col",
        scatter_dimension=0,
        tiled=True,
    ).astype(jnp.bfloat16)
    grad_heads = attn_grad.reshape(local_rows, head_count, DH)
    prob_grad = jnp.einsum(
        "qhd,khd->hqk", grad_heads, all_values, preferred_element_type=jnp.float32
    )
    row_dot = jnp.transpose(
        jnp.sum(grad_heads.astype(jnp.float32) * attn_out.astype(jnp.float32), axis=2)
    )[:, :, None]
    score_grad = (attn_probs.astype(jnp.float32) * (prob_grad - row_dot)).astype(jnp.bfloat16)
    query_grad = (
        jnp.einsum("hqk,khd->qhd", score_grad, all_keys, preferred_element_type=jnp.float32)
        * factor
    )
    every_out = lax.all_gather(out_local, "col", axis=1, tiled=True)
    key_term = (
        jnp.einsum("hqk,qhd->khd", score_grad, local_query, preferred_element_type=jnp.float32)
        * factor
    )
    value_term = jnp.einsum(
        "hqk,qhd->khd", attn_probs, grad_heads, preferred_element_type=jnp.float32
    )
    key_sum, value_sum = (
        lax.psum_scatter(
            key_term.reshape(-1, feature_width).astype(jnp.bfloat16),
            "col",
            scatter_dimension=0,
            tiled=True,
        ).astype(jnp.float32),
        lax.psum_scatter(
            value_term.reshape(-1, feature_width).astype(jnp.bfloat16),
            "col",
            scatter_dimension=0,
            tiled=True,
        ).astype(jnp.float32),
    )
    out_pair = jnp.concatenate([every_out, swap_dp(every_out)], axis=0)
    grad_pair = lax.all_gather(
        jnp.concatenate([output_grad, grad_other], axis=0), "row", axis=1, tiled=True
    )
    patch_pair = jnp.concatenate([every_patch, patch_other], axis=0)
    out_weight_grad = lax.dot_general(
        out_pair, grad_pair, (((0, 1), (0, 1)), ((), ())), preferred_element_type=jnp.float32
    )
    embed_weight_grad = lax.dot_general(
        patch_pair, grad_pair, (((0, 1), (0, 1)), ((), ())), preferred_element_type=jnp.float32
    )
    return (
        query_grad.reshape(1, local_rows, feature_width),
        key_sum.reshape(1, local_rows, feature_width),
        value_sum.reshape(1, local_rows, feature_width),
        out_weight_grad,
        embed_weight_grad,
    )


def axis_size(axis):
    return lax.psum(1, axis)


def shifted(x, axis, step):
    n = axis_size(axis)
    return lax.ppermute(x, axis, [(j, (j + step) % n) for j in range(n)])


def natural(pieces, axis):
    n = len(pieces)
    order = (lax.axis_index(axis) - jnp.arange(n)) % n
    return jnp.take(jnp.stack(pieces, 0), order, axis=0)


def gather_rows(x, axis):
    n = axis_size(axis)
    pieces = [x] + [shifted(x, axis, s) for s in range(1, n)]
    stacked = natural(pieces, axis)
    return stacked.reshape((n * x.shape[0],) + x.shape[1:])


def group_cols(x, axis, group):
    width = x.shape[1] // axis_size(axis)
    return lax.dynamic_slice_in_dim(x, group * width, width, 1)


def to_heads(x, axis):
    n, me = axis_size(axis), lax.axis_index(axis)
    pieces = [group_cols(x, axis, me)] + [
        shifted(group_cols(x, axis, (me + s) % n), axis, s) for s in range(1, n)
    ]
    stacked = natural(pieces, axis)
    return stacked.reshape((n * x.shape[0],) + stacked.shape[2:])


def from_heads(x, axis):
    n, me = axis_size(axis), lax.axis_index(axis)
    rows = x.shape[0] // n
    block = lambda k: lax.dynamic_slice_in_dim(x, k * rows, rows, 0)
    pieces = [block(me)] + [
        shifted(block((me + s) % n).astype(jnp.bfloat16), axis, s).astype(jnp.float32)
        for s in range(1, n)
    ]
    stacked = natural(pieces, axis)
    return jnp.transpose(stacked, (1, 0, 2)).reshape(rows, n * x.shape[1])


def sum_to_heads(partial, axis):
    n, me = axis_size(axis), lax.axis_index(axis)
    total = group_cols(partial, axis, me)
    for s in range(1, n):
        sent = group_cols(partial, axis, (me - s) % n).astype(jnp.bfloat16)
        total = total + shifted(sent, axis, -s % n).astype(jnp.float32)
    return total


def flat(*arrays):
    return jnp.concatenate([a.reshape(-1) for a in arrays])


def unflat(vector, shapes):
    out, at = [], 0
    for shape in shapes:
        size = int(np.prod(shape))
        out.append(vector[..., at:at + size].reshape(vector.shape[:-1] + shape))
        at += size
    return out


def gather_rows_relayed(x, axis):
    n, me = axis_size(axis), lax.axis_index(axis)
    chips = n // 2
    cross = [x] + [
        lax.ppermute(x, axis, [(j, (j + 2 * s) % n) for j in range(n)]) for s in range(1, chips)
    ]
    partner_own = lax.ppermute(x, axis, [(j, j ^ 1) for j in range(n)])
    if chips > 1:
        relayed = lax.ppermute(jnp.stack(cross[1:], 0), axis, [(j, j ^ 1) for j in range(n)])
        partner = [partner_own] + [relayed[k] for k in range(chips - 1)]
    else:
        partner = [partner_own]
    pieces = jnp.stack(cross + partner, 0)
    j = jnp.arange(n)
    mine = (j % 2) == (me % 2)
    order = jnp.where(mine, ((me - j) % n) // 2, chips + (((me ^ 1) - j) % n) // 2)
    stacked = jnp.take(pieces, order, axis=0)
    return stacked.reshape((n * x.shape[0],) + x.shape[1:])


def roll_blocks(x, shift):
    n = x.shape[0]
    return lax.dynamic_slice_in_dim(jnp.concatenate([x, x], 0), shift % n, n, 0)


def body_heads(patches, queries, attn_keys, attn_values, out_weight, output_grad):
    factor = DH ** (-0.5)
    n, me = axis_size("col"), lax.axis_index("col")
    rank = lax.axis_index("row")
    tokens, width_all = queries.shape[1], queries.shape[2]
    width = width_all // n
    heads = width // DH
    patch_here = patches[0]
    grad_blocks = [output_grad[0]] + [shifted(output_grad[0], "row", s) for s in range(1, n)]
    dense_grad = jnp.concatenate(grad_blocks, 0)
    grad_other = swap_dp(output_grad)
    qkv = jnp.stack([queries[0], attn_keys[0], attn_values[0]], 0)
    part = lambda g: lax.dynamic_slice_in_dim(qkv, g * width, width, 2)
    shapes = [(3, tokens, width), patch_here.shape]
    pieces = [(part(me), patch_here)]
    for s in range(1, n):
        got = shifted(flat(part((me + s) % n), patch_here), "col", s)
        pieces.append(tuple(unflat(got, shapes)))
    grad_partial = lax.dot_general(
        dense_grad, out_weight, (((1,), (1,)), ((), ())), preferred_element_type=jnp.float32
    )
    pieces, grad_partial = lax.optimization_barrier((pieces, grad_partial))
    order = me - rank
    qkv_h = roll_blocks(jnp.stack([p[0] for p in pieces], 0), order)
    every_patch = roll_blocks(jnp.stack([p[1] for p in pieces], 0), order).reshape(n * tokens, -1)
    rows = n * tokens
    qkv_h = jnp.transpose(qkv_h, (1, 0, 2, 3)).reshape(3, rows, heads, DH)
    local_query, all_keys, all_values = qkv_h[0], qkv_h[1], qkv_h[2]
    grad_partial, grad_other = lax.optimization_barrier((grad_partial, grad_other))
    other_blocks = [grad_other[0]] + [shifted(grad_other[0], "row", s) for s in range(1, n)]
    scores = (
        jnp.einsum("qhd,khd->hqk", local_query, all_keys, preferred_element_type=jnp.float32)
        * factor
    )
    row_max = jnp.max(scores, axis=2, keepdims=True)
    log_total = row_max + jnp.log(jnp.sum(jnp.exp(scores - row_max), axis=2, keepdims=True))
    attn_probs = jnp.exp(scores - log_total).astype(jnp.bfloat16)
    attn_out = jnp.einsum(
        "hqk,khd->qhd", attn_probs, all_values, preferred_element_type=jnp.float32
    ).astype(jnp.bfloat16)
    attn_grad = sum_to_heads(grad_partial, "col").astype(jnp.bfloat16)
    grad_heads = attn_grad.reshape(rows, heads, DH)
    prob_grad = jnp.einsum(
        "qhd,khd->hqk", grad_heads, all_values, preferred_element_type=jnp.float32
    )
    row_dot = jnp.transpose(
        jnp.sum(grad_heads.astype(jnp.float32) * attn_out.astype(jnp.float32), axis=2)
    )[:, :, None]
    score_grad = (attn_probs.astype(jnp.float32) * (prob_grad - row_dot)).astype(jnp.bfloat16)
    query_grad = (
        jnp.einsum("hqk,khd->qhd", score_grad, all_keys, preferred_element_type=jnp.float32)
        * factor
    )
    key_grad = (
        jnp.einsum("hqk,qhd->khd", score_grad, local_query, preferred_element_type=jnp.float32)
        * factor
    )
    value_grad = jnp.einsum(
        "hqk,qhd->khd", attn_probs, grad_heads, preferred_element_type=jnp.float32
    )
    other_patch = swap_dp(every_patch)
    out_flat = attn_out.reshape(rows, width)
    own_pair = (out_flat, swap_dp(out_flat))
    attn_grad, sent_out = lax.optimization_barrier((attn_grad, out_flat))
    out_pieces = [own_pair] + [
        (got, swap_dp(got)) for got in (shifted(sent_out, "col", -s % n) for s in range(1, n))
    ]
    out_both = roll_blocks(
        jnp.stack([jnp.concatenate(p, 0) for p in out_pieces], 0), -me
    )
    grad_both = jnp.concatenate([dense_grad] + other_blocks, 0)
    out_weight_grad = lax.dot_general(
        out_both, grad_both, (((1,), (0,)), ((), ())), preferred_element_type=jnp.float32
    ).reshape(width_all, -1)
    embed_weight_grad = contract_rows(jnp.concatenate([every_patch, other_patch], 0), grad_both)
    grad_list = [g.reshape(n, tokens, width) for g in (query_grad, key_grad, value_grad)]
    sendable = roll_blocks(
        jnp.stack([g.astype(jnp.bfloat16) for g in grad_list], 1), rank - me
    )
    sendable, out_both = lax.optimization_barrier((sendable, out_both))
    mine = jnp.stack(
        [lax.dynamic_index_in_dim(g, (rank - me) % n, 0, keepdims=False) for g in grad_list], 0
    )
    back = jnp.zeros((3, tokens, width_all), jnp.float32)
    back = lax.dynamic_update_slice_in_dim(back, mine, me * width, 2)
    for s in range(1, n):
        got = shifted(sendable[s], "col", -s % n).astype(jnp.float32)
        back = lax.dynamic_update_slice_in_dim(back, got, ((me + s) % n) * width, 2)
    back = back.reshape(3, 1, tokens, width_all)
    return (back[0], back[1], back[2], out_weight_grad, embed_weight_grad)


def body(patches, queries, attn_keys, attn_values, out_weight, output_grad):
    heads_here = queries.shape[2] // DH
    if (
        heads_here % axis_size("col") == 0
        and queries.shape[1] == output_grad.shape[1]
        and axis_size("row") == axis_size("col")
    ):
        return body_heads(patches, queries, attn_keys, attn_values, out_weight, output_grad)
    return body_tokens(patches, queries, attn_keys, attn_values, out_weight, output_grad)


def solution(mesh):
    placed = (
        P("dp", "col", "row"),
        P("dp", "col", "row"),
        P("dp", "col", "row"),
        P("dp", "col", "row"),
        P("row", "col"),
        P("dp", "row", "col"),
    )
    return jax.shard_map(
        body,
        mesh=mesh,
        in_specs=placed,
        out_specs=(
            P("dp", "col", "row"),
            P("dp", "col", "row"),
            P("dp", "col", "row"),
            P("row", "col"),
            P("row", "col"),
        ),
        check_vma=False,
    )
```

```python
import jax
import numpy as np
import jax.numpy as jnp
from jax import lax
from jax.sharding import PartitionSpec as P

DH = 128


def contract_rows(left, right):
    return lax.dot_general(
        left, right, (((0,), (0,)), ((), ())), preferred_element_type=jnp.float32
    )


def swap_dp(x):
    return lax.ppermute(x, "dp", [(0, 1), (1, 0)])


def body_tokens(patches, queries, attn_keys, attn_values, out_weight, output_grad):
    factor = DH ** (-0.5)
    local_rows = queries.shape[1]
    feature_width = queries.shape[2]
    head_count = feature_width // DH
    grad_other = swap_dp(output_grad)
    patch_other = swap_dp(lax.all_gather(patches, "col", axis=1, tiled=True))
    every_key, every_value, every_patch = (
        lax.all_gather(attn_keys, "col", axis=1, tiled=True),
        lax.all_gather(attn_values, "col", axis=1, tiled=True),
        lax.all_gather(patches, "col", axis=1, tiled=True),
    )
    local_query = queries[0].reshape(local_rows, head_count, DH)
    all_keys = every_key[0].reshape(-1, head_count, DH)
    all_values = every_value[0].reshape(-1, head_count, DH)
    scores = (
        jnp.einsum("qhd,khd->hqk", local_query, all_keys, preferred_element_type=jnp.float32)
        * factor
    )
    row_max = jnp.max(scores, axis=2, keepdims=True)
    log_total = row_max + jnp.log(jnp.sum(jnp.exp(scores - row_max), axis=2, keepdims=True))
    attn_probs = jnp.exp(scores - log_total).astype(jnp.bfloat16)
    attn_out = jnp.einsum(
        "hqk,khd->qhd", attn_probs, all_values, preferred_element_type=jnp.float32
    ).astype(jnp.bfloat16)
    out_local = attn_out.reshape(1, local_rows, feature_width)
    dense_grad = lax.all_gather(output_grad, "row", axis=1, tiled=True)[0]
    attn_grad = lax.psum_scatter(
        lax.dot_general(
            dense_grad, out_weight, (((1,), (1,)), ((), ())), preferred_element_type=jnp.float32
        ),
        "col",
        scatter_dimension=0,
        tiled=True,
    ).astype(jnp.bfloat16)
    grad_heads = attn_grad.reshape(local_rows, head_count, DH)
    prob_grad = jnp.einsum(
        "qhd,khd->hqk", grad_heads, all_values, preferred_element_type=jnp.float32
    )
    row_dot = jnp.transpose(
        jnp.sum(grad_heads.astype(jnp.float32) * attn_out.astype(jnp.float32), axis=2)
    )[:, :, None]
    score_grad = (attn_probs.astype(jnp.float32) * (prob_grad - row_dot)).astype(jnp.bfloat16)
    query_grad = (
        jnp.einsum("hqk,khd->qhd", score_grad, all_keys, preferred_element_type=jnp.float32)
        * factor
    )
    every_out = lax.all_gather(out_local, "col", axis=1, tiled=True)
    key_term = (
        jnp.einsum("hqk,qhd->khd", score_grad, local_query, preferred_element_type=jnp.float32)
        * factor
    )
    value_term = jnp.einsum(
        "hqk,qhd->khd", attn_probs, grad_heads, preferred_element_type=jnp.float32
    )
    key_sum, value_sum = (
        lax.psum_scatter(
            key_term.reshape(-1, feature_width).astype(jnp.bfloat16),
            "col",
            scatter_dimension=0,
            tiled=True,
        ).astype(jnp.float32),
        lax.psum_scatter(
            value_term.reshape(-1, feature_width).astype(jnp.bfloat16),
            "col",
            scatter_dimension=0,
            tiled=True,
        ).astype(jnp.float32),
    )
    out_pair = jnp.concatenate([every_out, swap_dp(every_out)], axis=0)
    grad_pair = lax.all_gather(
        jnp.concatenate([output_grad, grad_other], axis=0), "row", axis=1, tiled=True
    )
    patch_pair = jnp.concatenate([every_patch, patch_other], axis=0)
    out_weight_grad = lax.dot_general(
        out_pair, grad_pair, (((0, 1), (0, 1)), ((), ())), preferred_element_type=jnp.float32
    )
    embed_weight_grad = lax.dot_general(
        patch_pair, grad_pair, (((0, 1), (0, 1)), ((), ())), preferred_element_type=jnp.float32
    )
    return (
        query_grad.reshape(1, local_rows, feature_width),
        key_sum.reshape(1, local_rows, feature_width),
        value_sum.reshape(1, local_rows, feature_width),
        out_weight_grad,
        embed_weight_grad,
    )


def axis_size(axis):
    return lax.psum(1, axis)


def shifted(x, axis, step):
    n = axis_size(axis)
    return lax.ppermute(x, axis, [(j, (j + step) % n) for j in range(n)])


def natural(pieces, axis):
    n = len(pieces)
    order = (lax.axis_index(axis) - jnp.arange(n)) % n
    return jnp.take(jnp.stack(pieces, 0), order, axis=0)


def gather_rows(x, axis):
    n = axis_size(axis)
    pieces = [x] + [shifted(x, axis, s) for s in range(1, n)]
    stacked = natural(pieces, axis)
    return stacked.reshape((n * x.shape[0],) + x.shape[1:])


def group_cols(x, axis, group):
    width = x.shape[1] // axis_size(axis)
    return lax.dynamic_slice_in_dim(x, group * width, width, 1)


def to_heads(x, axis):
    n, me = axis_size(axis), lax.axis_index(axis)
    pieces = [group_cols(x, axis, me)] + [
        shifted(group_cols(x, axis, (me + s) % n), axis, s) for s in range(1, n)
    ]
    stacked = natural(pieces, axis)
    return stacked.reshape((n * x.shape[0],) + stacked.shape[2:])


def from_heads(x, axis):
    n, me = axis_size(axis), lax.axis_index(axis)
    rows = x.shape[0] // n
    block = lambda k: lax.dynamic_slice_in_dim(x, k * rows, rows, 0)
    pieces = [block(me)] + [
        shifted(block((me + s) % n).astype(jnp.bfloat16), axis, s).astype(jnp.float32)
        for s in range(1, n)
    ]
    stacked = natural(pieces, axis)
    return jnp.transpose(stacked, (1, 0, 2)).reshape(rows, n * x.shape[1])


def sum_to_heads(partial, axis):
    n, me = axis_size(axis), lax.axis_index(axis)
    total = group_cols(partial, axis, me)
    for s in range(1, n):
        sent = group_cols(partial, axis, (me - s) % n).astype(jnp.bfloat16)
        total = total + shifted(sent, axis, -s % n).astype(jnp.float32)
    return total


def flat(*arrays):
    return jnp.concatenate([a.reshape(-1) for a in arrays])


def unflat(vector, shapes):
    out, at = [], 0
    for shape in shapes:
        size = int(np.prod(shape))
        out.append(vector[..., at:at + size].reshape(vector.shape[:-1] + shape))
        at += size
    return out


def gather_rows_relayed(x, axis):
    n, me = axis_size(axis), lax.axis_index(axis)
    chips = n // 2
    cross = [x] + [
        lax.ppermute(x, axis, [(j, (j + 2 * s) % n) for j in range(n)]) for s in range(1, chips)
    ]
    partner_own = lax.ppermute(x, axis, [(j, j ^ 1) for j in range(n)])
    if chips > 1:
        relayed = lax.ppermute(jnp.stack(cross[1:], 0), axis, [(j, j ^ 1) for j in range(n)])
        partner = [partner_own] + [relayed[k] for k in range(chips - 1)]
    else:
        partner = [partner_own]
    pieces = jnp.stack(cross + partner, 0)
    j = jnp.arange(n)
    mine = (j % 2) == (me % 2)
    order = jnp.where(mine, ((me - j) % n) // 2, chips + (((me ^ 1) - j) % n) // 2)
    stacked = jnp.take(pieces, order, axis=0)
    return stacked.reshape((n * x.shape[0],) + x.shape[1:])


def roll_blocks(x, shift):
    n = x.shape[0]
    return lax.dynamic_slice_in_dim(jnp.concatenate([x, x], 0), shift % n, n, 0)


def body_heads(patches, queries, attn_keys, attn_values, out_weight, output_grad):
    factor = DH ** (-0.5)
    n, me = axis_size("col"), lax.axis_index("col")
    rank = lax.axis_index("row")
    tokens, width_all = queries.shape[1], queries.shape[2]
    width = width_all // n
    heads = width // DH
    patch_here = patches[0]
    grad_blocks = [output_grad[0]] + [shifted(output_grad[0], "row", s) for s in range(1, n)]
    dense_grad = jnp.concatenate(grad_blocks, 0)
    grad_other = swap_dp(output_grad)
    qkv = jnp.stack([queries[0], attn_keys[0], attn_values[0]], 0)
    part = lambda g: lax.dynamic_slice_in_dim(qkv, g * width, width, 2)
    shapes = [(3, tokens, width), patch_here.shape]
    pieces = [(part(me), patch_here)]
    for s in range(1, n):
        got = shifted(flat(part((me + s) % n), patch_here), "col", s)
        pieces.append(tuple(unflat(got, shapes)))
    grad_partial = lax.dot_general(
        dense_grad, out_weight, (((1,), (1,)), ((), ())), preferred_element_type=jnp.float32
    )
    pieces, grad_partial = lax.optimization_barrier((pieces, grad_partial))
    order = me - rank
    qkv_h = roll_blocks(jnp.stack([p[0] for p in pieces], 0), order)
    every_patch = roll_blocks(jnp.stack([p[1] for p in pieces], 0), order).reshape(n * tokens, -1)
    rows = n * tokens
    qkv_h = jnp.transpose(qkv_h, (1, 0, 2, 3)).reshape(3, rows, heads, DH)
    local_query, all_keys, all_values = qkv_h[0], qkv_h[1], qkv_h[2]
    grad_partial, grad_other = lax.optimization_barrier((grad_partial, grad_other))
    other_blocks = [grad_other[0]] + [shifted(grad_other[0], "row", s) for s in range(1, n)]
    scores = (
        jnp.einsum("qhd,khd->hqk", local_query, all_keys, preferred_element_type=jnp.float32)
        * factor
    )
    row_max = jnp.max(scores, axis=2, keepdims=True)
    log_total = row_max + jnp.log(jnp.sum(jnp.exp(scores - row_max), axis=2, keepdims=True))
    attn_probs = jnp.exp(scores - log_total).astype(jnp.bfloat16)
    attn_out = jnp.einsum(
        "hqk,khd->qhd", attn_probs, all_values, preferred_element_type=jnp.float32
    ).astype(jnp.bfloat16)
    attn_grad = sum_to_heads(grad_partial, "col").astype(jnp.bfloat16)
    grad_heads = attn_grad.reshape(rows, heads, DH)
    prob_grad = jnp.einsum(
        "qhd,khd->hqk", grad_heads, all_values, preferred_element_type=jnp.float32
    )
    row_dot = jnp.transpose(
        jnp.sum(grad_heads.astype(jnp.float32) * attn_out.astype(jnp.float32), axis=2)
    )[:, :, None]
    score_grad = (attn_probs.astype(jnp.float32) * (prob_grad - row_dot)).astype(jnp.bfloat16)
    query_grad = (
        jnp.einsum("hqk,khd->qhd", score_grad, all_keys, preferred_element_type=jnp.float32)
        * factor
    )
    key_grad = (
        jnp.einsum("hqk,qhd->khd", score_grad, local_query, preferred_element_type=jnp.float32)
        * factor
    )
    value_grad = jnp.einsum(
        "hqk,qhd->khd", attn_probs, grad_heads, preferred_element_type=jnp.float32
    )
    other_patch = swap_dp(every_patch)
    out_flat = attn_out.reshape(rows, width)
    own_pair = (out_flat, swap_dp(out_flat))
    attn_grad, sent_out = lax.optimization_barrier((attn_grad, out_flat))
    out_pieces = [own_pair] + [
        (got, swap_dp(got)) for got in (shifted(sent_out, "col", -s % n) for s in range(1, n))
    ]
    out_both = roll_blocks(
        jnp.stack([jnp.concatenate(p, 0) for p in out_pieces], 0), -me
    )
    grad_both = jnp.concatenate([dense_grad] + other_blocks, 0)
    out_weight_grad = lax.dot_general(
        out_both, grad_both, (((1,), (0,)), ((), ())), preferred_element_type=jnp.float32
    ).reshape(width_all, -1)
    embed_weight_grad = contract_rows(jnp.concatenate([every_patch, other_patch], 0), grad_both)
    grad_list = [g.reshape(n, tokens, width) for g in (query_grad, key_grad, value_grad)]
    sendable = roll_blocks(
        jnp.stack([g.astype(jnp.bfloat16) for g in grad_list], 1), rank - me
    )
    sendable, _ = lax.optimization_barrier((sendable, [p[0] for p in out_pieces]))
    mine = jnp.stack(
        [lax.dynamic_index_in_dim(g, (rank - me) % n, 0, keepdims=False) for g in grad_list], 0
    )
    back = jnp.zeros((3, tokens, width_all), jnp.float32)
    back = lax.dynamic_update_slice_in_dim(back, mine, me * width, 2)
    for s in range(1, n):
        got = shifted(sendable[s], "col", -s % n).astype(jnp.float32)
        back = lax.dynamic_update_slice_in_dim(back, got, ((me + s) % n) * width, 2)
    back = back.reshape(3, 1, tokens, width_all)
    return (back[0], back[1], back[2], out_weight_grad, embed_weight_grad)


def body(patches, queries, attn_keys, attn_values, out_weight, output_grad):
    heads_here = queries.shape[2] // DH
    if (
        heads_here % axis_size("col") == 0
        and queries.shape[1] == output_grad.shape[1]
        and axis_size("row") == axis_size("col")
    ):
        return body_heads(patches, queries, attn_keys, attn_values, out_weight, output_grad)
    return body_tokens(patches, queries, attn_keys, attn_values, out_weight, output_grad)


def solution(mesh):
    placed = (
        P("dp", "col", "row"),
        P("dp", "col", "row"),
        P("dp", "col", "row"),
        P("dp", "col", "row"),
        P("row", "col"),
        P("dp", "row", "col"),
    )
    return jax.shard_map(
        body,
        mesh=mesh,
        in_specs=placed,
        out_specs=(
            P("dp", "col", "row"),
            P("dp", "col", "row"),
            P("dp", "col", "row"),
            P("row", "col"),
            P("row", "col"),
        ),
        check_vma=False,
    )
```

```python
import jax
import numpy as np
import jax.numpy as jnp
from jax import lax
from jax.sharding import PartitionSpec as P

DH = 128


def contract_rows(left, right):
    return lax.dot_general(
        left, right, (((0,), (0,)), ((), ())), preferred_element_type=jnp.float32
    )


def swap_dp(x):
    return lax.ppermute(x, "dp", [(0, 1), (1, 0)])


def body_tokens(patches, queries, attn_keys, attn_values, out_weight, output_grad):
    factor = DH ** (-0.5)
    local_rows = queries.shape[1]
    feature_width = queries.shape[2]
    head_count = feature_width // DH
    grad_other = swap_dp(output_grad)
    patch_other = swap_dp(lax.all_gather(patches, "col", axis=1, tiled=True))
    every_key, every_value, every_patch = (
        lax.all_gather(attn_keys, "col", axis=1, tiled=True),
        lax.all_gather(attn_values, "col", axis=1, tiled=True),
        lax.all_gather(patches, "col", axis=1, tiled=True),
    )
    local_query = queries[0].reshape(local_rows, head_count, DH)
    all_keys = every_key[0].reshape(-1, head_count, DH)
    all_values = every_value[0].reshape(-1, head_count, DH)
    scores = (
        jnp.einsum("qhd,khd->hqk", local_query, all_keys, preferred_element_type=jnp.float32)
        * factor
    )
    row_max = jnp.max(scores, axis=2, keepdims=True)
    log_total = row_max + jnp.log(jnp.sum(jnp.exp(scores - row_max), axis=2, keepdims=True))
    attn_probs = jnp.exp(scores - log_total).astype(jnp.bfloat16)
    attn_out = jnp.einsum(
        "hqk,khd->qhd", attn_probs, all_values, preferred_element_type=jnp.float32
    ).astype(jnp.bfloat16)
    out_local = attn_out.reshape(1, local_rows, feature_width)
    dense_grad = lax.all_gather(output_grad, "row", axis=1, tiled=True)[0]
    attn_grad = lax.psum_scatter(
        lax.dot_general(
            dense_grad, out_weight, (((1,), (1,)), ((), ())), preferred_element_type=jnp.float32
        ),
        "col",
        scatter_dimension=0,
        tiled=True,
    ).astype(jnp.bfloat16)
    grad_heads = attn_grad.reshape(local_rows, head_count, DH)
    prob_grad = jnp.einsum(
        "qhd,khd->hqk", grad_heads, all_values, preferred_element_type=jnp.float32
    )
    row_dot = jnp.transpose(
        jnp.sum(grad_heads.astype(jnp.float32) * attn_out.astype(jnp.float32), axis=2)
    )[:, :, None]
    score_grad = (attn_probs.astype(jnp.float32) * (prob_grad - row_dot)).astype(jnp.bfloat16)
    query_grad = (
        jnp.einsum("hqk,khd->qhd", score_grad, all_keys, preferred_element_type=jnp.float32)
        * factor
    )
    every_out = lax.all_gather(out_local, "col", axis=1, tiled=True)
    key_term = (
        jnp.einsum("hqk,qhd->khd", score_grad, local_query, preferred_element_type=jnp.float32)
        * factor
    )
    value_term = jnp.einsum(
        "hqk,qhd->khd", attn_probs, grad_heads, preferred_element_type=jnp.float32
    )
    key_sum, value_sum = (
        lax.psum_scatter(
            key_term.reshape(-1, feature_width).astype(jnp.bfloat16),
            "col",
            scatter_dimension=0,
            tiled=True,
        ).astype(jnp.float32),
        lax.psum_scatter(
            value_term.reshape(-1, feature_width).astype(jnp.bfloat16),
            "col",
            scatter_dimension=0,
            tiled=True,
        ).astype(jnp.float32),
    )
    out_pair = jnp.concatenate([every_out, swap_dp(every_out)], axis=0)
    grad_pair = lax.all_gather(
        jnp.concatenate([output_grad, grad_other], axis=0), "row", axis=1, tiled=True
    )
    patch_pair = jnp.concatenate([every_patch, patch_other], axis=0)
    out_weight_grad = lax.dot_general(
        out_pair, grad_pair, (((0, 1), (0, 1)), ((), ())), preferred_element_type=jnp.float32
    )
    embed_weight_grad = lax.dot_general(
        patch_pair, grad_pair, (((0, 1), (0, 1)), ((), ())), preferred_element_type=jnp.float32
    )
    return (
        query_grad.reshape(1, local_rows, feature_width),
        key_sum.reshape(1, local_rows, feature_width),
        value_sum.reshape(1, local_rows, feature_width),
        out_weight_grad,
        embed_weight_grad,
    )


def axis_size(axis):
    return lax.psum(1, axis)


def shifted(x, axis, step):
    n = axis_size(axis)
    return lax.ppermute(x, axis, [(j, (j + step) % n) for j in range(n)])


def natural(pieces, axis):
    n = len(pieces)
    order = (lax.axis_index(axis) - jnp.arange(n)) % n
    return jnp.take(jnp.stack(pieces, 0), order, axis=0)


def gather_rows(x, axis):
    n = axis_size(axis)
    pieces = [x] + [shifted(x, axis, s) for s in range(1, n)]
    stacked = natural(pieces, axis)
    return stacked.reshape((n * x.shape[0],) + x.shape[1:])


def group_cols(x, axis, group):
    width = x.shape[1] // axis_size(axis)
    return lax.dynamic_slice_in_dim(x, group * width, width, 1)


def to_heads(x, axis):
    n, me = axis_size(axis), lax.axis_index(axis)
    pieces = [group_cols(x, axis, me)] + [
        shifted(group_cols(x, axis, (me + s) % n), axis, s) for s in range(1, n)
    ]
    stacked = natural(pieces, axis)
    return stacked.reshape((n * x.shape[0],) + stacked.shape[2:])


def from_heads(x, axis):
    n, me = axis_size(axis), lax.axis_index(axis)
    rows = x.shape[0] // n
    block = lambda k: lax.dynamic_slice_in_dim(x, k * rows, rows, 0)
    pieces = [block(me)] + [
        shifted(block((me + s) % n).astype(jnp.bfloat16), axis, s).astype(jnp.float32)
        for s in range(1, n)
    ]
    stacked = natural(pieces, axis)
    return jnp.transpose(stacked, (1, 0, 2)).reshape(rows, n * x.shape[1])


def sum_to_heads(partial, axis):
    n, me = axis_size(axis), lax.axis_index(axis)
    total = group_cols(partial, axis, me)
    for s in range(1, n):
        sent = group_cols(partial, axis, (me - s) % n).astype(jnp.bfloat16)
        total = total + shifted(sent, axis, -s % n).astype(jnp.float32)
    return total


def flat(*arrays):
    return jnp.concatenate([a.reshape(-1) for a in arrays])


def unflat(vector, shapes):
    out, at = [], 0
    for shape in shapes:
        size = int(np.prod(shape))
        out.append(vector[..., at:at + size].reshape(vector.shape[:-1] + shape))
        at += size
    return out


def gather_rows_relayed(x, axis):
    n, me = axis_size(axis), lax.axis_index(axis)
    chips = n // 2
    cross = [x] + [
        lax.ppermute(x, axis, [(j, (j + 2 * s) % n) for j in range(n)]) for s in range(1, chips)
    ]
    partner_own = lax.ppermute(x, axis, [(j, j ^ 1) for j in range(n)])
    if chips > 1:
        relayed = lax.ppermute(jnp.stack(cross[1:], 0), axis, [(j, j ^ 1) for j in range(n)])
        partner = [partner_own] + [relayed[k] for k in range(chips - 1)]
    else:
        partner = [partner_own]
    pieces = jnp.stack(cross + partner, 0)
    j = jnp.arange(n)
    mine = (j % 2) == (me % 2)
    order = jnp.where(mine, ((me - j) % n) // 2, chips + (((me ^ 1) - j) % n) // 2)
    stacked = jnp.take(pieces, order, axis=0)
    return stacked.reshape((n * x.shape[0],) + x.shape[1:])


def roll_blocks(x, shift):
    n = x.shape[0]
    return lax.dynamic_slice_in_dim(jnp.concatenate([x, x], 0), shift % n, n, 0)


def body_heads(patches, queries, attn_keys, attn_values, out_weight, output_grad):
    factor = DH ** (-0.5)
    n, me = axis_size("col"), lax.axis_index("col")
    rank = lax.axis_index("row")
    tokens, width_all = queries.shape[1], queries.shape[2]
    width = width_all // n
    heads = width // DH
    patch_here = patches[0]
    grad_blocks = [output_grad[0]] + [shifted(output_grad[0], "row", s) for s in range(1, n)]
    dense_grad = jnp.concatenate(grad_blocks, 0)
    grad_other = swap_dp(output_grad)
    qkv = jnp.stack([queries[0], attn_keys[0], attn_values[0]], 0)
    part = lambda g: lax.dynamic_slice_in_dim(qkv, g * width, width, 2)
    shapes = [(3, tokens, width), patch_here.shape]
    pieces = [(part(me), patch_here)]
    for s in range(1, n):
        got = shifted(flat(part((me + s) % n), patch_here), "col", s)
        pieces.append(tuple(unflat(got, shapes)))
    grad_partial = lax.dot_general(
        dense_grad, out_weight, (((1,), (1,)), ((), ())), preferred_element_type=jnp.float32
    )
    pieces, grad_partial = lax.optimization_barrier((pieces, grad_partial))
    order = me - rank
    qkv_h = roll_blocks(jnp.stack([p[0] for p in pieces], 0), order)
    every_patch = roll_blocks(jnp.stack([p[1] for p in pieces], 0), order).reshape(n * tokens, -1)
    rows = n * tokens
    qkv_h = jnp.transpose(qkv_h, (1, 0, 2, 3)).reshape(3, rows, heads, DH)
    local_query, all_keys, all_values = qkv_h[0], qkv_h[1], qkv_h[2]
    grad_partial, grad_other = lax.optimization_barrier((grad_partial, grad_other))
    other_blocks = [grad_other[0]] + [shifted(grad_other[0], "row", s) for s in range(1, n)]
    scores = (
        jnp.einsum("qhd,khd->hqk", local_query, all_keys, preferred_element_type=jnp.float32)
        * factor
    )
    row_max = jnp.max(scores, axis=2, keepdims=True)
    log_total = row_max + jnp.log(jnp.sum(jnp.exp(scores - row_max), axis=2, keepdims=True))
    attn_probs = jnp.exp(scores - log_total).astype(jnp.bfloat16)
    attn_out = jnp.einsum(
        "hqk,khd->qhd", attn_probs, all_values, preferred_element_type=jnp.float32
    ).astype(jnp.bfloat16)
    attn_grad = sum_to_heads(grad_partial, "col").astype(jnp.bfloat16)
    grad_heads = attn_grad.reshape(rows, heads, DH)
    prob_grad = jnp.einsum(
        "qhd,khd->hqk", grad_heads, all_values, preferred_element_type=jnp.float32
    )
    row_dot = jnp.transpose(
        jnp.sum(grad_heads.astype(jnp.float32) * attn_out.astype(jnp.float32), axis=2)
    )[:, :, None]
    score_grad = (attn_probs.astype(jnp.float32) * (prob_grad - row_dot)).astype(jnp.bfloat16)
    query_grad = (
        jnp.einsum("hqk,khd->qhd", score_grad, all_keys, preferred_element_type=jnp.float32)
        * factor
    )
    key_grad = (
        jnp.einsum("hqk,qhd->khd", score_grad, local_query, preferred_element_type=jnp.float32)
        * factor
    )
    value_grad = jnp.einsum(
        "hqk,qhd->khd", attn_probs, grad_heads, preferred_element_type=jnp.float32
    )
    other_patch = swap_dp(every_patch)
    out_flat = attn_out.reshape(rows, width)
    own_pair = (out_flat, swap_dp(out_flat))
    attn_grad, sent_out = lax.optimization_barrier((attn_grad, out_flat))
    out_pieces = [own_pair] + [
        (got, swap_dp(got)) for got in (shifted(sent_out, "col", -s % n) for s in range(1, n))
    ]
    out_both = roll_blocks(
        jnp.stack([jnp.concatenate(p, 0) for p in out_pieces], 0), -me
    )
    grad_both = jnp.concatenate([dense_grad] + other_blocks, 0)
    out_weight_grad = lax.dot_general(
        out_both, grad_both, (((1,), (0,)), ((), ())), preferred_element_type=jnp.float32
    ).reshape(width_all, -1)
    embed_weight_grad = contract_rows(jnp.concatenate([every_patch, other_patch], 0), grad_both)
    grad_list = [g.reshape(n, tokens, width) for g in (query_grad, key_grad, value_grad)]
    sendable = roll_blocks(
        jnp.stack([g.astype(jnp.bfloat16) for g in grad_list], 1), rank - me
    )
    sendable, _ = lax.optimization_barrier((sendable, [p[0] for p in out_pieces]))
    mine = jnp.stack(
        [lax.dynamic_index_in_dim(g, (rank - me) % n, 0, keepdims=False) for g in grad_list], 0
    )
    back = jnp.zeros((3, tokens, width_all), jnp.float32)
    back = lax.dynamic_update_slice_in_dim(back, mine, me * width, 2)
    received = [shifted(sendable[s], "col", -s % n) for s in range(1, n)]
    received, out_weight_grad = lax.optimization_barrier((received, out_weight_grad))
    for s in range(1, n):
        got = received[s - 1].astype(jnp.float32)
        back = lax.dynamic_update_slice_in_dim(back, got, ((me + s) % n) * width, 2)
    back = back.reshape(3, 1, tokens, width_all)
    return (back[0], back[1], back[2], out_weight_grad, embed_weight_grad)


def body(patches, queries, attn_keys, attn_values, out_weight, output_grad):
    heads_here = queries.shape[2] // DH
    if (
        heads_here % axis_size("col") == 0
        and queries.shape[1] == output_grad.shape[1]
        and axis_size("row") == axis_size("col")
    ):
        return body_heads(patches, queries, attn_keys, attn_values, out_weight, output_grad)
    return body_tokens(patches, queries, attn_keys, attn_values, out_weight, output_grad)


def solution(mesh):
    placed = (
        P("dp", "col", "row"),
        P("dp", "col", "row"),
        P("dp", "col", "row"),
        P("dp", "col", "row"),
        P("row", "col"),
        P("dp", "row", "col"),
    )
    return jax.shard_map(
        body,
        mesh=mesh,
        in_specs=placed,
        out_specs=(
            P("dp", "col", "row"),
            P("dp", "col", "row"),
            P("dp", "col", "row"),
            P("row", "col"),
            P("row", "col"),
        ),
        check_vma=False,
    )
```

```python
import jax
import numpy as np
import jax.numpy as jnp
from jax import lax
from jax.sharding import PartitionSpec as P

DH = 128


def contract_rows(left, right):
    return lax.dot_general(
        left, right, (((0,), (0,)), ((), ())), preferred_element_type=jnp.float32
    )


def swap_dp(x):
    return lax.ppermute(x, "dp", [(0, 1), (1, 0)])


def body_tokens(patches, queries, attn_keys, attn_values, out_weight, output_grad):
    factor = DH ** (-0.5)
    local_rows = queries.shape[1]
    feature_width = queries.shape[2]
    head_count = feature_width // DH
    grad_other = swap_dp(output_grad)
    patch_other = swap_dp(lax.all_gather(patches, "col", axis=1, tiled=True))
    every_key, every_value, every_patch = (
        lax.all_gather(attn_keys, "col", axis=1, tiled=True),
        lax.all_gather(attn_values, "col", axis=1, tiled=True),
        lax.all_gather(patches, "col", axis=1, tiled=True),
    )
    local_query = queries[0].reshape(local_rows, head_count, DH)
    all_keys = every_key[0].reshape(-1, head_count, DH)
    all_values = every_value[0].reshape(-1, head_count, DH)
    scores = (
        jnp.einsum("qhd,khd->hqk", local_query, all_keys, preferred_element_type=jnp.float32)
        * factor
    )
    row_max = jnp.max(scores, axis=2, keepdims=True)
    log_total = row_max + jnp.log(jnp.sum(jnp.exp(scores - row_max), axis=2, keepdims=True))
    attn_probs = jnp.exp(scores - log_total).astype(jnp.bfloat16)
    attn_out = jnp.einsum(
        "hqk,khd->qhd", attn_probs, all_values, preferred_element_type=jnp.float32
    ).astype(jnp.bfloat16)
    out_local = attn_out.reshape(1, local_rows, feature_width)
    dense_grad = lax.all_gather(output_grad, "row", axis=1, tiled=True)[0]
    attn_grad = lax.psum_scatter(
        lax.dot_general(
            dense_grad, out_weight, (((1,), (1,)), ((), ())), preferred_element_type=jnp.float32
        ),
        "col",
        scatter_dimension=0,
        tiled=True,
    ).astype(jnp.bfloat16)
    grad_heads = attn_grad.reshape(local_rows, head_count, DH)
    prob_grad = jnp.einsum(
        "qhd,khd->hqk", grad_heads, all_values, preferred_element_type=jnp.float32
    )
    row_dot = jnp.transpose(
        jnp.sum(grad_heads.astype(jnp.float32) * attn_out.astype(jnp.float32), axis=2)
    )[:, :, None]
    score_grad = (attn_probs.astype(jnp.float32) * (prob_grad - row_dot)).astype(jnp.bfloat16)
    query_grad = (
        jnp.einsum("hqk,khd->qhd", score_grad, all_keys, preferred_element_type=jnp.float32)
        * factor
    )
    every_out = lax.all_gather(out_local, "col", axis=1, tiled=True)
    key_term = (
        jnp.einsum("hqk,qhd->khd", score_grad, local_query, preferred_element_type=jnp.float32)
        * factor
    )
    value_term = jnp.einsum(
        "hqk,qhd->khd", attn_probs, grad_heads, preferred_element_type=jnp.float32
    )
    key_sum, value_sum = (
        lax.psum_scatter(
            key_term.reshape(-1, feature_width).astype(jnp.bfloat16),
            "col",
            scatter_dimension=0,
            tiled=True,
        ).astype(jnp.float32),
        lax.psum_scatter(
            value_term.reshape(-1, feature_width).astype(jnp.bfloat16),
            "col",
            scatter_dimension=0,
            tiled=True,
        ).astype(jnp.float32),
    )
    out_pair = jnp.concatenate([every_out, swap_dp(every_out)], axis=0)
    grad_pair = lax.all_gather(
        jnp.concatenate([output_grad, grad_other], axis=0), "row", axis=1, tiled=True
    )
    patch_pair = jnp.concatenate([every_patch, patch_other], axis=0)
    out_weight_grad = lax.dot_general(
        out_pair, grad_pair, (((0, 1), (0, 1)), ((), ())), preferred_element_type=jnp.float32
    )
    embed_weight_grad = lax.dot_general(
        patch_pair, grad_pair, (((0, 1), (0, 1)), ((), ())), preferred_element_type=jnp.float32
    )
    return (
        query_grad.reshape(1, local_rows, feature_width),
        key_sum.reshape(1, local_rows, feature_width),
        value_sum.reshape(1, local_rows, feature_width),
        out_weight_grad,
        embed_weight_grad,
    )


def axis_size(axis):
    return lax.psum(1, axis)


def shifted(x, axis, step):
    n = axis_size(axis)
    return lax.ppermute(x, axis, [(j, (j + step) % n) for j in range(n)])


def natural(pieces, axis):
    n = len(pieces)
    order = (lax.axis_index(axis) - jnp.arange(n)) % n
    return jnp.take(jnp.stack(pieces, 0), order, axis=0)


def gather_rows(x, axis):
    n = axis_size(axis)
    pieces = [x] + [shifted(x, axis, s) for s in range(1, n)]
    stacked = natural(pieces, axis)
    return stacked.reshape((n * x.shape[0],) + x.shape[1:])


def group_cols(x, axis, group):
    width = x.shape[1] // axis_size(axis)
    return lax.dynamic_slice_in_dim(x, group * width, width, 1)


def to_heads(x, axis):
    n, me = axis_size(axis), lax.axis_index(axis)
    pieces = [group_cols(x, axis, me)] + [
        shifted(group_cols(x, axis, (me + s) % n), axis, s) for s in range(1, n)
    ]
    stacked = natural(pieces, axis)
    return stacked.reshape((n * x.shape[0],) + stacked.shape[2:])


def from_heads(x, axis):
    n, me = axis_size(axis), lax.axis_index(axis)
    rows = x.shape[0] // n
    block = lambda k: lax.dynamic_slice_in_dim(x, k * rows, rows, 0)
    pieces = [block(me)] + [
        shifted(block((me + s) % n).astype(jnp.bfloat16), axis, s).astype(jnp.float32)
        for s in range(1, n)
    ]
    stacked = natural(pieces, axis)
    return jnp.transpose(stacked, (1, 0, 2)).reshape(rows, n * x.shape[1])


def sum_to_heads(partial, axis):
    n, me = axis_size(axis), lax.axis_index(axis)
    total = group_cols(partial, axis, me)
    for s in range(1, n):
        sent = group_cols(partial, axis, (me - s) % n).astype(jnp.bfloat16)
        total = total + shifted(sent, axis, -s % n).astype(jnp.float32)
    return total


def flat(*arrays):
    return jnp.concatenate([a.reshape(-1) for a in arrays])


def unflat(vector, shapes):
    out, at = [], 0
    for shape in shapes:
        size = int(np.prod(shape))
        out.append(vector[..., at:at + size].reshape(vector.shape[:-1] + shape))
        at += size
    return out


def gather_rows_relayed(x, axis):
    n, me = axis_size(axis), lax.axis_index(axis)
    chips = n // 2
    cross = [x] + [
        lax.ppermute(x, axis, [(j, (j + 2 * s) % n) for j in range(n)]) for s in range(1, chips)
    ]
    partner_own = lax.ppermute(x, axis, [(j, j ^ 1) for j in range(n)])
    if chips > 1:
        relayed = lax.ppermute(jnp.stack(cross[1:], 0), axis, [(j, j ^ 1) for j in range(n)])
        partner = [partner_own] + [relayed[k] for k in range(chips - 1)]
    else:
        partner = [partner_own]
    pieces = jnp.stack(cross + partner, 0)
    j = jnp.arange(n)
    mine = (j % 2) == (me % 2)
    order = jnp.where(mine, ((me - j) % n) // 2, chips + (((me ^ 1) - j) % n) // 2)
    stacked = jnp.take(pieces, order, axis=0)
    return stacked.reshape((n * x.shape[0],) + x.shape[1:])


def roll_blocks(x, shift):
    n = x.shape[0]
    return lax.dynamic_slice_in_dim(jnp.concatenate([x, x], 0), shift % n, n, 0)


def body_heads(patches, queries, attn_keys, attn_values, out_weight, output_grad):
    factor = DH ** (-0.5)
    n, me = axis_size("col"), lax.axis_index("col")
    rank = lax.axis_index("row")
    tokens, width_all = queries.shape[1], queries.shape[2]
    width = width_all // n
    heads = width // DH
    patch_here = patches[0]
    grad_blocks = [output_grad[0]] + [shifted(output_grad[0], "row", s) for s in range(1, n)]
    dense_grad = jnp.concatenate(grad_blocks, 0)
    grad_other = swap_dp(output_grad)
    qkv = jnp.stack([queries[0], attn_keys[0], attn_values[0]], 0)
    part = lambda g: lax.dynamic_slice_in_dim(qkv, g * width, width, 2)
    shapes = [(3, tokens, width), patch_here.shape]
    pieces = [(part(me), patch_here)]
    for s in range(1, n):
        got = shifted(flat(part((me + s) % n), patch_here), "col", s)
        pieces.append(tuple(unflat(got, shapes)))
    grad_partial = lax.dot_general(
        dense_grad, out_weight, (((1,), (1,)), ((), ())), preferred_element_type=jnp.float32
    )
    pieces, grad_partial = lax.optimization_barrier((pieces, grad_partial))
    order = me - rank
    qkv_h = roll_blocks(jnp.stack([p[0] for p in pieces], 0), order)
    every_patch = roll_blocks(jnp.stack([p[1] for p in pieces], 0), order).reshape(n * tokens, -1)
    rows = n * tokens
    qkv_h = jnp.transpose(qkv_h, (1, 0, 2, 3)).reshape(3, rows, heads, DH)
    local_query, all_keys, all_values = qkv_h[0], qkv_h[1], qkv_h[2]
    grad_partial, grad_other = lax.optimization_barrier((grad_partial, grad_other))
    other_blocks = [grad_other[0]] + [shifted(grad_other[0], "row", s) for s in range(1, n)]
    scores = (
        jnp.einsum("qhd,khd->hqk", local_query, all_keys, preferred_element_type=jnp.float32)
        * factor
    )
    row_max = jnp.max(scores, axis=2, keepdims=True)
    log_total = row_max + jnp.log(jnp.sum(jnp.exp(scores - row_max), axis=2, keepdims=True))
    attn_probs = jnp.exp(scores - log_total).astype(jnp.bfloat16)
    attn_out = jnp.einsum(
        "hqk,khd->qhd", attn_probs, all_values, preferred_element_type=jnp.float32
    ).astype(jnp.bfloat16)
    attn_grad = sum_to_heads(grad_partial, "col").astype(jnp.bfloat16)
    grad_heads = attn_grad.reshape(rows, heads, DH)
    prob_grad = jnp.einsum(
        "qhd,khd->hqk", grad_heads, all_values, preferred_element_type=jnp.float32
    )
    row_dot = jnp.transpose(
        jnp.sum(grad_heads.astype(jnp.float32) * attn_out.astype(jnp.float32), axis=2)
    )[:, :, None]
    score_grad = (attn_probs.astype(jnp.float32) * (prob_grad - row_dot)).astype(jnp.bfloat16)
    query_grad = (
        jnp.einsum("hqk,khd->qhd", score_grad, all_keys, preferred_element_type=jnp.float32)
        * factor
    )
    key_grad = (
        jnp.einsum("hqk,qhd->khd", score_grad, local_query, preferred_element_type=jnp.float32)
        * factor
    )
    value_grad = jnp.einsum(
        "hqk,qhd->khd", attn_probs, grad_heads, preferred_element_type=jnp.float32
    )
    other_patch = swap_dp(every_patch)
    out_flat = attn_out.reshape(rows, width)
    own_pair = (out_flat, swap_dp(out_flat))
    attn_grad, sent_out = lax.optimization_barrier((attn_grad, out_flat))
    gathered = [shifted(sent_out, "col", -s % n) for s in range(1, n)]
    swapped = swap_dp(jnp.stack(gathered, 0))
    out_pieces = [own_pair] + [(gathered[s - 1], swapped[s - 1]) for s in range(1, n)]
    out_both = roll_blocks(
        jnp.stack([jnp.concatenate(p, 0) for p in out_pieces], 0), -me
    )
    grad_both = jnp.concatenate([dense_grad] + other_blocks, 0)
    out_weight_grad = lax.dot_general(
        out_both, grad_both, (((1,), (0,)), ((), ())), preferred_element_type=jnp.float32
    ).reshape(width_all, -1)
    embed_weight_grad = contract_rows(jnp.concatenate([every_patch, other_patch], 0), grad_both)
    grad_list = [g.reshape(n, tokens, width) for g in (query_grad, key_grad, value_grad)]
    sendable = roll_blocks(
        jnp.stack([g.astype(jnp.bfloat16) for g in grad_list], 1), rank - me
    )
    sendable, _ = lax.optimization_barrier((sendable, gathered))
    mine = jnp.stack(
        [lax.dynamic_index_in_dim(g, (rank - me) % n, 0, keepdims=False) for g in grad_list], 0
    )
    back = jnp.zeros((3, tokens, width_all), jnp.float32)
    back = lax.dynamic_update_slice_in_dim(back, mine, me * width, 2)
    for s in range(1, n):
        got = shifted(sendable[s], "col", -s % n).astype(jnp.float32)
        back = lax.dynamic_update_slice_in_dim(back, got, ((me + s) % n) * width, 2)
    back = back.reshape(3, 1, tokens, width_all)
    return (back[0], back[1], back[2], out_weight_grad, embed_weight_grad)


def body(patches, queries, attn_keys, attn_values, out_weight, output_grad):
    heads_here = queries.shape[2] // DH
    if (
        heads_here % axis_size("col") == 0
        and queries.shape[1] == output_grad.shape[1]
        and axis_size("row") == axis_size("col")
    ):
        return body_heads(patches, queries, attn_keys, attn_values, out_weight, output_grad)
    return body_tokens(patches, queries, attn_keys, attn_values, out_weight, output_grad)


def solution(mesh):
    placed = (
        P("dp", "col", "row"),
        P("dp", "col", "row"),
        P("dp", "col", "row"),
        P("dp", "col", "row"),
        P("row", "col"),
        P("dp", "row", "col"),
    )
    return jax.shard_map(
        body,
        mesh=mesh,
        in_specs=placed,
        out_specs=(
            P("dp", "col", "row"),
            P("dp", "col", "row"),
            P("dp", "col", "row"),
            P("row", "col"),
            P("row", "col"),
        ),
        check_vma=False,
    )
```

```python
import jax
import numpy as np
import jax.numpy as jnp
from jax import lax
from jax.sharding import PartitionSpec as P

DH = 128


def contract_rows(left, right):
    return lax.dot_general(
        left, right, (((0,), (0,)), ((), ())), preferred_element_type=jnp.float32
    )


def swap_dp(x):
    return lax.ppermute(x, "dp", [(0, 1), (1, 0)])


def body_tokens(patches, queries, attn_keys, attn_values, out_weight, output_grad):
    factor = DH ** (-0.5)
    local_rows = queries.shape[1]
    feature_width = queries.shape[2]
    head_count = feature_width // DH
    grad_other = swap_dp(output_grad)
    patch_other = swap_dp(lax.all_gather(patches, "col", axis=1, tiled=True))
    every_key, every_value, every_patch = (
        lax.all_gather(attn_keys, "col", axis=1, tiled=True),
        lax.all_gather(attn_values, "col", axis=1, tiled=True),
        lax.all_gather(patches, "col", axis=1, tiled=True),
    )
    local_query = queries[0].reshape(local_rows, head_count, DH)
    all_keys = every_key[0].reshape(-1, head_count, DH)
    all_values = every_value[0].reshape(-1, head_count, DH)
    scores = (
        jnp.einsum("qhd,khd->hqk", local_query, all_keys, preferred_element_type=jnp.float32)
        * factor
    )
    row_max = jnp.max(scores, axis=2, keepdims=True)
    log_total = row_max + jnp.log(jnp.sum(jnp.exp(scores - row_max), axis=2, keepdims=True))
    attn_probs = jnp.exp(scores - log_total).astype(jnp.bfloat16)
    attn_out = jnp.einsum(
        "hqk,khd->qhd", attn_probs, all_values, preferred_element_type=jnp.float32
    ).astype(jnp.bfloat16)
    out_local = attn_out.reshape(1, local_rows, feature_width)
    dense_grad = lax.all_gather(output_grad, "row", axis=1, tiled=True)[0]
    attn_grad = lax.psum_scatter(
        lax.dot_general(
            dense_grad, out_weight, (((1,), (1,)), ((), ())), preferred_element_type=jnp.float32
        ),
        "col",
        scatter_dimension=0,
        tiled=True,
    ).astype(jnp.bfloat16)
    grad_heads = attn_grad.reshape(local_rows, head_count, DH)
    prob_grad = jnp.einsum(
        "qhd,khd->hqk", grad_heads, all_values, preferred_element_type=jnp.float32
    )
    row_dot = jnp.transpose(
        jnp.sum(grad_heads.astype(jnp.float32) * attn_out.astype(jnp.float32), axis=2)
    )[:, :, None]
    score_grad = (attn_probs.astype(jnp.float32) * (prob_grad - row_dot)).astype(jnp.bfloat16)
    query_grad = (
        jnp.einsum("hqk,khd->qhd", score_grad, all_keys, preferred_element_type=jnp.float32)
        * factor
    )
    every_out = lax.all_gather(out_local, "col", axis=1, tiled=True)
    key_term = (
        jnp.einsum("hqk,qhd->khd", score_grad, local_query, preferred_element_type=jnp.float32)
        * factor
    )
    value_term = jnp.einsum(
        "hqk,qhd->khd", attn_probs, grad_heads, preferred_element_type=jnp.float32
    )
    key_sum, value_sum = (
        lax.psum_scatter(
            key_term.reshape(-1, feature_width).astype(jnp.bfloat16),
            "col",
            scatter_dimension=0,
            tiled=True,
        ).astype(jnp.float32),
        lax.psum_scatter(
            value_term.reshape(-1, feature_width).astype(jnp.bfloat16),
            "col",
            scatter_dimension=0,
            tiled=True,
        ).astype(jnp.float32),
    )
    out_pair = jnp.concatenate([every_out, swap_dp(every_out)], axis=0)
    grad_pair = lax.all_gather(
        jnp.concatenate([output_grad, grad_other], axis=0), "row", axis=1, tiled=True
    )
    patch_pair = jnp.concatenate([every_patch, patch_other], axis=0)
    out_weight_grad = lax.dot_general(
        out_pair, grad_pair, (((0, 1), (0, 1)), ((), ())), preferred_element_type=jnp.float32
    )
    embed_weight_grad = lax.dot_general(
        patch_pair, grad_pair, (((0, 1), (0, 1)), ((), ())), preferred_element_type=jnp.float32
    )
    return (
        query_grad.reshape(1, local_rows, feature_width),
        key_sum.reshape(1, local_rows, feature_width),
        value_sum.reshape(1, local_rows, feature_width),
        out_weight_grad,
        embed_weight_grad,
    )


def axis_size(axis):
    return lax.psum(1, axis)


def shifted(x, axis, step):
    n = axis_size(axis)
    return lax.ppermute(x, axis, [(j, (j + step) % n) for j in range(n)])


def natural(pieces, axis):
    n = len(pieces)
    order = (lax.axis_index(axis) - jnp.arange(n)) % n
    return jnp.take(jnp.stack(pieces, 0), order, axis=0)


def gather_rows(x, axis):
    n = axis_size(axis)
    pieces = [x] + [shifted(x, axis, s) for s in range(1, n)]
    stacked = natural(pieces, axis)
    return stacked.reshape((n * x.shape[0],) + x.shape[1:])


def group_cols(x, axis, group):
    width = x.shape[1] // axis_size(axis)
    return lax.dynamic_slice_in_dim(x, group * width, width, 1)


def to_heads(x, axis):
    n, me = axis_size(axis), lax.axis_index(axis)
    pieces = [group_cols(x, axis, me)] + [
        shifted(group_cols(x, axis, (me + s) % n), axis, s) for s in range(1, n)
    ]
    stacked = natural(pieces, axis)
    return stacked.reshape((n * x.shape[0],) + stacked.shape[2:])


def from_heads(x, axis):
    n, me = axis_size(axis), lax.axis_index(axis)
    rows = x.shape[0] // n
    block = lambda k: lax.dynamic_slice_in_dim(x, k * rows, rows, 0)
    pieces = [block(me)] + [
        shifted(block((me + s) % n).astype(jnp.bfloat16), axis, s).astype(jnp.float32)
        for s in range(1, n)
    ]
    stacked = natural(pieces, axis)
    return jnp.transpose(stacked, (1, 0, 2)).reshape(rows, n * x.shape[1])


def sum_to_heads(partial, axis):
    n, me = axis_size(axis), lax.axis_index(axis)
    total = group_cols(partial, axis, me)
    for s in range(1, n):
        sent = group_cols(partial, axis, (me - s) % n).astype(jnp.bfloat16)
        total = total + shifted(sent, axis, -s % n).astype(jnp.float32)
    return total


def flat(*arrays):
    return jnp.concatenate([a.reshape(-1) for a in arrays])


def unflat(vector, shapes):
    out, at = [], 0
    for shape in shapes:
        size = int(np.prod(shape))
        out.append(vector[..., at:at + size].reshape(vector.shape[:-1] + shape))
        at += size
    return out


def gather_rows_relayed(x, axis):
    n, me = axis_size(axis), lax.axis_index(axis)
    chips = n // 2
    cross = [x] + [
        lax.ppermute(x, axis, [(j, (j + 2 * s) % n) for j in range(n)]) for s in range(1, chips)
    ]
    partner_own = lax.ppermute(x, axis, [(j, j ^ 1) for j in range(n)])
    if chips > 1:
        relayed = lax.ppermute(jnp.stack(cross[1:], 0), axis, [(j, j ^ 1) for j in range(n)])
        partner = [partner_own] + [relayed[k] for k in range(chips - 1)]
    else:
        partner = [partner_own]
    pieces = jnp.stack(cross + partner, 0)
    j = jnp.arange(n)
    mine = (j % 2) == (me % 2)
    order = jnp.where(mine, ((me - j) % n) // 2, chips + (((me ^ 1) - j) % n) // 2)
    stacked = jnp.take(pieces, order, axis=0)
    return stacked.reshape((n * x.shape[0],) + x.shape[1:])


def roll_blocks(x, shift):
    n = x.shape[0]
    return lax.dynamic_slice_in_dim(jnp.concatenate([x, x], 0), shift % n, n, 0)


def relayed_blocks(x, axis):
    n, me = axis_size(axis), lax.axis_index(axis)
    if n != 4:
        return [x] + [shifted(x, axis, s) for s in range(1, n)]
    across = lax.ppermute(x, axis, [(j, (j + 2) % n) for j in range(n)])
    partner = lax.ppermute(x, axis, [(j, j ^ 1) for j in range(n)])
    forwarded = lax.ppermute(across, axis, [(j, j ^ 1) for j in range(n)])
    even = (me % 2) == 0
    return [
        x,
        jnp.where(even, forwarded, partner),
        across,
        jnp.where(even, partner, forwarded),
    ]


def body_heads(patches, queries, attn_keys, attn_values, out_weight, output_grad):
    factor = DH ** (-0.5)
    n, me = axis_size("col"), lax.axis_index("col")
    rank = lax.axis_index("row")
    tokens, width_all = queries.shape[1], queries.shape[2]
    width = width_all // n
    heads = width // DH
    patch_here = patches[0]
    grad_blocks = relayed_blocks(output_grad[0], "row")
    dense_grad = jnp.concatenate(grad_blocks, 0)
    grad_other = swap_dp(output_grad)
    qkv = jnp.stack([queries[0], attn_keys[0], attn_values[0]], 0)
    part = lambda g: lax.dynamic_slice_in_dim(qkv, g * width, width, 2)
    shapes = [(3, tokens, width), patch_here.shape]
    pieces = [(part(me), patch_here)]
    for s in range(1, n):
        got = shifted(flat(part((me + s) % n), patch_here), "col", s)
        pieces.append(tuple(unflat(got, shapes)))
    grad_partial = lax.dot_general(
        dense_grad, out_weight, (((1,), (1,)), ((), ())), preferred_element_type=jnp.float32
    )
    pieces, grad_partial = lax.optimization_barrier((pieces, grad_partial))
    order = me - rank
    qkv_h = roll_blocks(jnp.stack([p[0] for p in pieces], 0), order)
    every_patch = roll_blocks(jnp.stack([p[1] for p in pieces], 0), order).reshape(n * tokens, -1)
    rows = n * tokens
    qkv_h = jnp.transpose(qkv_h, (1, 0, 2, 3)).reshape(3, rows, heads, DH)
    local_query, all_keys, all_values = qkv_h[0], qkv_h[1], qkv_h[2]
    grad_partial, grad_other = lax.optimization_barrier((grad_partial, grad_other))
    other_blocks = [grad_other[0]] + [shifted(grad_other[0], "row", s) for s in range(1, n)]
    scores = (
        jnp.einsum("qhd,khd->hqk", local_query, all_keys, preferred_element_type=jnp.float32)
        * factor
    )
    row_max = jnp.max(scores, axis=2, keepdims=True)
    log_total = row_max + jnp.log(jnp.sum(jnp.exp(scores - row_max), axis=2, keepdims=True))
    attn_probs = jnp.exp(scores - log_total).astype(jnp.bfloat16)
    attn_out = jnp.einsum(
        "hqk,khd->qhd", attn_probs, all_values, preferred_element_type=jnp.float32
    ).astype(jnp.bfloat16)
    attn_grad = sum_to_heads(grad_partial, "col").astype(jnp.bfloat16)
    grad_heads = attn_grad.reshape(rows, heads, DH)
    prob_grad = jnp.einsum(
        "qhd,khd->hqk", grad_heads, all_values, preferred_element_type=jnp.float32
    )
    row_dot = jnp.transpose(
        jnp.sum(grad_heads.astype(jnp.float32) * attn_out.astype(jnp.float32), axis=2)
    )[:, :, None]
    score_grad = (attn_probs.astype(jnp.float32) * (prob_grad - row_dot)).astype(jnp.bfloat16)
    query_grad = (
        jnp.einsum("hqk,khd->qhd", score_grad, all_keys, preferred_element_type=jnp.float32)
        * factor
    )
    key_grad = (
        jnp.einsum("hqk,qhd->khd", score_grad, local_query, preferred_element_type=jnp.float32)
        * factor
    )
    value_grad = jnp.einsum(
        "hqk,qhd->khd", attn_probs, grad_heads, preferred_element_type=jnp.float32
    )
    other_patch = swap_dp(every_patch)
    out_flat = attn_out.reshape(rows, width)
    own_pair = (out_flat, swap_dp(out_flat))
    attn_grad, sent_out = lax.optimization_barrier((attn_grad, out_flat))
    out_pieces = [own_pair] + [
        (got, swap_dp(got)) for got in (shifted(sent_out, "col", -s % n) for s in range(1, n))
    ]
    out_both = roll_blocks(
        jnp.stack([jnp.concatenate(p, 0) for p in out_pieces], 0), -me
    )
    grad_both = jnp.concatenate([dense_grad] + other_blocks, 0)
    out_weight_grad = lax.dot_general(
        out_both, grad_both, (((1,), (0,)), ((), ())), preferred_element_type=jnp.float32
    ).reshape(width_all, -1)
    embed_weight_grad = contract_rows(jnp.concatenate([every_patch, other_patch], 0), grad_both)
    grad_list = [g.reshape(n, tokens, width) for g in (query_grad, key_grad, value_grad)]
    sendable = roll_blocks(
        jnp.stack([g.astype(jnp.bfloat16) for g in grad_list], 1), rank - me
    )
    sendable, out_both = lax.optimization_barrier((sendable, out_both))
    mine = jnp.stack(
        [lax.dynamic_index_in_dim(g, (rank - me) % n, 0, keepdims=False) for g in grad_list], 0
    )
    back = jnp.zeros((3, tokens, width_all), jnp.float32)
    back = lax.dynamic_update_slice_in_dim(back, mine, me * width, 2)
    for s in range(1, n):
        got = shifted(sendable[s], "col", -s % n).astype(jnp.float32)
        back = lax.dynamic_update_slice_in_dim(back, got, ((me + s) % n) * width, 2)
    back = back.reshape(3, 1, tokens, width_all)
    return (back[0], back[1], back[2], out_weight_grad, embed_weight_grad)


def body(patches, queries, attn_keys, attn_values, out_weight, output_grad):
    heads_here = queries.shape[2] // DH
    if (
        heads_here % axis_size("col") == 0
        and queries.shape[1] == output_grad.shape[1]
        and axis_size("row") == axis_size("col")
    ):
        return body_heads(patches, queries, attn_keys, attn_values, out_weight, output_grad)
    return body_tokens(patches, queries, attn_keys, attn_values, out_weight, output_grad)


def solution(mesh):
    placed = (
        P("dp", "col", "row"),
        P("dp", "col", "row"),
        P("dp", "col", "row"),
        P("dp", "col", "row"),
        P("row", "col"),
        P("dp", "row", "col"),
    )
    return jax.shard_map(
        body,
        mesh=mesh,
        in_specs=placed,
        out_specs=(
            P("dp", "col", "row"),
            P("dp", "col", "row"),
            P("dp", "col", "row"),
            P("row", "col"),
            P("row", "col"),
        ),
        check_vma=False,
    )
```

```python
import jax
import numpy as np
import jax.numpy as jnp
from jax import lax
from jax.sharding import PartitionSpec as P

DH = 128


def contract_rows(left, right):
    return lax.dot_general(
        left, right, (((0,), (0,)), ((), ())), preferred_element_type=jnp.float32
    )


def swap_dp(x):
    return lax.ppermute(x, "dp", [(0, 1), (1, 0)])


def body_tokens(patches, queries, attn_keys, attn_values, out_weight, output_grad):
    factor = DH ** (-0.5)
    local_rows = queries.shape[1]
    feature_width = queries.shape[2]
    head_count = feature_width // DH
    grad_other = swap_dp(output_grad)
    patch_other = swap_dp(lax.all_gather(patches, "col", axis=1, tiled=True))
    every_key, every_value, every_patch = (
        lax.all_gather(attn_keys, "col", axis=1, tiled=True),
        lax.all_gather(attn_values, "col", axis=1, tiled=True),
        lax.all_gather(patches, "col", axis=1, tiled=True),
    )
    local_query = queries[0].reshape(local_rows, head_count, DH)
    all_keys = every_key[0].reshape(-1, head_count, DH)
    all_values = every_value[0].reshape(-1, head_count, DH)
    scores = (
        jnp.einsum("qhd,khd->hqk", local_query, all_keys, preferred_element_type=jnp.float32)
        * factor
    )
    row_max = jnp.max(scores, axis=2, keepdims=True)
    log_total = row_max + jnp.log(jnp.sum(jnp.exp(scores - row_max), axis=2, keepdims=True))
    attn_probs = jnp.exp(scores - log_total).astype(jnp.bfloat16)
    attn_out = jnp.einsum(
        "hqk,khd->qhd", attn_probs, all_values, preferred_element_type=jnp.float32
    ).astype(jnp.bfloat16)
    out_local = attn_out.reshape(1, local_rows, feature_width)
    dense_grad = lax.all_gather(output_grad, "row", axis=1, tiled=True)[0]
    attn_grad = lax.psum_scatter(
        lax.dot_general(
            dense_grad, out_weight, (((1,), (1,)), ((), ())), preferred_element_type=jnp.float32
        ),
        "col",
        scatter_dimension=0,
        tiled=True,
    ).astype(jnp.bfloat16)
    grad_heads = attn_grad.reshape(local_rows, head_count, DH)
    prob_grad = jnp.einsum(
        "qhd,khd->hqk", grad_heads, all_values, preferred_element_type=jnp.float32
    )
    row_dot = jnp.transpose(
        jnp.sum(grad_heads.astype(jnp.float32) * attn_out.astype(jnp.float32), axis=2)
    )[:, :, None]
    score_grad = (attn_probs.astype(jnp.float32) * (prob_grad - row_dot)).astype(jnp.bfloat16)
    query_grad = (
        jnp.einsum("hqk,khd->qhd", score_grad, all_keys, preferred_element_type=jnp.float32)
        * factor
    )
    every_out = lax.all_gather(out_local, "col", axis=1, tiled=True)
    key_term = (
        jnp.einsum("hqk,qhd->khd", score_grad, local_query, preferred_element_type=jnp.float32)
        * factor
    )
    value_term = jnp.einsum(
        "hqk,qhd->khd", attn_probs, grad_heads, preferred_element_type=jnp.float32
    )
    key_sum, value_sum = (
        lax.psum_scatter(
            key_term.reshape(-1, feature_width).astype(jnp.bfloat16),
            "col",
            scatter_dimension=0,
            tiled=True,
        ).astype(jnp.float32),
        lax.psum_scatter(
            value_term.reshape(-1, feature_width).astype(jnp.bfloat16),
            "col",
            scatter_dimension=0,
            tiled=True,
        ).astype(jnp.float32),
    )
    out_pair = jnp.concatenate([every_out, swap_dp(every_out)], axis=0)
    grad_pair = lax.all_gather(
        jnp.concatenate([output_grad, grad_other], axis=0), "row", axis=1, tiled=True
    )
    patch_pair = jnp.concatenate([every_patch, patch_other], axis=0)
    out_weight_grad = lax.dot_general(
        out_pair, grad_pair, (((0, 1), (0, 1)), ((), ())), preferred_element_type=jnp.float32
    )
    embed_weight_grad = lax.dot_general(
        patch_pair, grad_pair, (((0, 1), (0, 1)), ((), ())), preferred_element_type=jnp.float32
    )
    return (
        query_grad.reshape(1, local_rows, feature_width),
        key_sum.reshape(1, local_rows, feature_width),
        value_sum.reshape(1, local_rows, feature_width),
        out_weight_grad,
        embed_weight_grad,
    )


def axis_size(axis):
    return lax.psum(1, axis)


def shifted(x, axis, step):
    n = axis_size(axis)
    return lax.ppermute(x, axis, [(j, (j + step) % n) for j in range(n)])


def natural(pieces, axis):
    n = len(pieces)
    order = (lax.axis_index(axis) - jnp.arange(n)) % n
    return jnp.take(jnp.stack(pieces, 0), order, axis=0)


def gather_rows(x, axis):
    n = axis_size(axis)
    pieces = [x] + [shifted(x, axis, s) for s in range(1, n)]
    stacked = natural(pieces, axis)
    return stacked.reshape((n * x.shape[0],) + x.shape[1:])


def group_cols(x, axis, group):
    width = x.shape[1] // axis_size(axis)
    return lax.dynamic_slice_in_dim(x, group * width, width, 1)


def to_heads(x, axis):
    n, me = axis_size(axis), lax.axis_index(axis)
    pieces = [group_cols(x, axis, me)] + [
        shifted(group_cols(x, axis, (me + s) % n), axis, s) for s in range(1, n)
    ]
    stacked = natural(pieces, axis)
    return stacked.reshape((n * x.shape[0],) + stacked.shape[2:])


def from_heads(x, axis):
    n, me = axis_size(axis), lax.axis_index(axis)
    rows = x.shape[0] // n
    block = lambda k: lax.dynamic_slice_in_dim(x, k * rows, rows, 0)
    pieces = [block(me)] + [
        shifted(block((me + s) % n).astype(jnp.bfloat16), axis, s).astype(jnp.float32)
        for s in range(1, n)
    ]
    stacked = natural(pieces, axis)
    return jnp.transpose(stacked, (1, 0, 2)).reshape(rows, n * x.shape[1])


def sum_to_heads(partial, axis):
    n, me = axis_size(axis), lax.axis_index(axis)
    total = group_cols(partial, axis, me)
    for s in range(1, n):
        sent = group_cols(partial, axis, (me - s) % n).astype(jnp.bfloat16)
        total = total + shifted(sent, axis, -s % n).astype(jnp.float32)
    return total


def flat(*arrays):
    return jnp.concatenate([a.reshape(-1) for a in arrays])


def unflat(vector, shapes):
    out, at = [], 0
    for shape in shapes:
        size = int(np.prod(shape))
        out.append(vector[..., at:at + size].reshape(vector.shape[:-1] + shape))
        at += size
    return out


def gather_rows_relayed(x, axis):
    n, me = axis_size(axis), lax.axis_index(axis)
    chips = n // 2
    cross = [x] + [
        lax.ppermute(x, axis, [(j, (j + 2 * s) % n) for j in range(n)]) for s in range(1, chips)
    ]
    partner_own = lax.ppermute(x, axis, [(j, j ^ 1) for j in range(n)])
    if chips > 1:
        relayed = lax.ppermute(jnp.stack(cross[1:], 0), axis, [(j, j ^ 1) for j in range(n)])
        partner = [partner_own] + [relayed[k] for k in range(chips - 1)]
    else:
        partner = [partner_own]
    pieces = jnp.stack(cross + partner, 0)
    j = jnp.arange(n)
    mine = (j % 2) == (me % 2)
    order = jnp.where(mine, ((me - j) % n) // 2, chips + (((me ^ 1) - j) % n) // 2)
    stacked = jnp.take(pieces, order, axis=0)
    return stacked.reshape((n * x.shape[0],) + x.shape[1:])


def roll_blocks(x, shift):
    n = x.shape[0]
    return lax.dynamic_slice_in_dim(jnp.concatenate([x, x], 0), shift % n, n, 0)


def body_heads(patches, queries, attn_keys, attn_values, out_weight, output_grad):
    factor = DH ** (-0.5)
    n, me = axis_size("col"), lax.axis_index("col")
    rank = lax.axis_index("row")
    tokens, width_all = queries.shape[1], queries.shape[2]
    width = width_all // n
    heads = width // DH
    patch_here = patches[0]
    grad_blocks = [output_grad[0]] + [shifted(output_grad[0], "row", s) for s in range(1, n)]
    dense_grad = jnp.concatenate(grad_blocks, 0)
    grad_other = swap_dp(output_grad)
    qkv = jnp.stack([queries[0], attn_keys[0], attn_values[0]], 0)
    part = lambda g: lax.dynamic_slice_in_dim(qkv, g * width, width, 2)
    shapes = [(3, tokens, width), patch_here.shape]
    pieces = [(part(me), patch_here)]
    for s in range(1, n):
        got = shifted(flat(part((me + s) % n), patch_here), "col", s)
        pieces.append(tuple(unflat(got, shapes)))
    grad_partial = lax.dot_general(
        dense_grad, out_weight, (((1,), (1,)), ((), ())), preferred_element_type=jnp.float32
    )
    pieces, grad_partial = lax.optimization_barrier((pieces, grad_partial))
    order = me - rank
    qkv_h = roll_blocks(jnp.stack([p[0] for p in pieces], 0), order)
    every_patch = roll_blocks(jnp.stack([p[1] for p in pieces], 0), order).reshape(n * tokens, -1)
    rows = n * tokens
    qkv_h = jnp.transpose(qkv_h, (1, 0, 2, 3)).reshape(3, rows, heads, DH)
    local_query, all_keys, all_values = qkv_h[0], qkv_h[1], qkv_h[2]
    grad_partial, grad_other = lax.optimization_barrier((grad_partial, grad_other))
    other_blocks = [grad_other[0]] + [shifted(grad_other[0], "row", s) for s in range(1, n)]
    scores = (
        jnp.einsum("qhd,khd->hqk", local_query, all_keys, preferred_element_type=jnp.float32)
        * factor
    )
    row_max = jnp.max(scores, axis=2, keepdims=True)
    log_total = row_max + jnp.log(jnp.sum(jnp.exp(scores - row_max), axis=2, keepdims=True))
    attn_probs = jnp.exp(scores - log_total).astype(jnp.bfloat16)
    attn_out = jnp.einsum(
        "hqk,khd->qhd", attn_probs, all_values, preferred_element_type=jnp.float32
    ).astype(jnp.bfloat16)
    attn_grad = sum_to_heads(grad_partial, "col").astype(jnp.bfloat16)
    grad_heads = attn_grad.reshape(rows, heads, DH)
    prob_grad = jnp.einsum(
        "qhd,khd->hqk", grad_heads, all_values, preferred_element_type=jnp.float32
    )
    row_dot = jnp.transpose(
        jnp.sum(grad_heads.astype(jnp.float32) * attn_out.astype(jnp.float32), axis=2)
    )[:, :, None]
    score_grad = (attn_probs.astype(jnp.float32) * (prob_grad - row_dot)).astype(jnp.bfloat16)
    query_grad = (
        jnp.einsum("hqk,khd->qhd", score_grad, all_keys, preferred_element_type=jnp.float32)
        * factor
    )
    key_grad = (
        jnp.einsum("hqk,qhd->khd", score_grad, local_query, preferred_element_type=jnp.float32)
        * factor
    )
    value_grad = jnp.einsum(
        "hqk,qhd->khd", attn_probs, grad_heads, preferred_element_type=jnp.float32
    )
    other_patch = swap_dp(every_patch)
    out_flat = attn_out.reshape(rows, width)
    own_pair = (out_flat, swap_dp(out_flat))
    attn_grad, sent_out = lax.optimization_barrier((attn_grad, out_flat))
    out_pieces = [own_pair] + [
        (got, swap_dp(got)) for got in (shifted(sent_out, "col", -s % n) for s in range(1, n))
    ]
    out_both = roll_blocks(
        jnp.stack([jnp.concatenate(p, 0) for p in out_pieces], 0), -me
    )
    grad_both = jnp.concatenate([dense_grad] + other_blocks, 0)
    out_weight_grad = lax.dot_general(
        out_both, grad_both, (((1,), (0,)), ((), ())), preferred_element_type=jnp.float32
    ).reshape(width_all, -1)
    embed_weight_grad = contract_rows(jnp.concatenate([every_patch, other_patch], 0), grad_both)
    grad_list = [g.reshape(n, tokens, width) for g in (query_grad, key_grad, value_grad)]
    sendable = roll_blocks(
        jnp.stack([g.astype(jnp.bfloat16) for g in grad_list], 1), rank - me
    )
    mine = jnp.stack(
        [lax.dynamic_index_in_dim(g, (rank - me) % n, 0, keepdims=False) for g in grad_list], 0
    )
    back = jnp.zeros((3, tokens, width_all), jnp.float32)
    back = lax.dynamic_update_slice_in_dim(back, mine, me * width, 2)
    for s in range(1, n):
        got = shifted(sendable[s], "col", -s % n).astype(jnp.float32)
        back = lax.dynamic_update_slice_in_dim(back, got, ((me + s) % n) * width, 2)
    back = back.reshape(3, 1, tokens, width_all)
    return (back[0], back[1], back[2], out_weight_grad, embed_weight_grad)


def body(patches, queries, attn_keys, attn_values, out_weight, output_grad):
    heads_here = queries.shape[2] // DH
    if (
        heads_here % axis_size("col") == 0
        and queries.shape[1] == output_grad.shape[1]
        and axis_size("row") == axis_size("col")
    ):
        return body_heads(patches, queries, attn_keys, attn_values, out_weight, output_grad)
    return body_tokens(patches, queries, attn_keys, attn_values, out_weight, output_grad)


def solution(mesh):
    placed = (
        P("dp", "col", "row"),
        P("dp", "col", "row"),
        P("dp", "col", "row"),
        P("dp", "col", "row"),
        P("row", "col"),
        P("dp", "row", "col"),
    )
    return jax.shard_map(
        body,
        mesh=mesh,
        in_specs=placed,
        out_specs=(
            P("dp", "col", "row"),
            P("dp", "col", "row"),
            P("dp", "col", "row"),
            P("row", "col"),
            P("row", "col"),
        ),
        check_vma=False,
    )
```

```python
import jax
import numpy as np
import jax.numpy as jnp
from jax import lax
from jax.sharding import PartitionSpec as P

DH = 128


def contract_rows(left, right):
    return lax.dot_general(
        left, right, (((0,), (0,)), ((), ())), preferred_element_type=jnp.float32
    )


def swap_dp(x):
    return lax.ppermute(x, "dp", [(0, 1), (1, 0)])


def body_tokens(patches, queries, attn_keys, attn_values, out_weight, output_grad):
    factor = DH ** (-0.5)
    local_rows = queries.shape[1]
    feature_width = queries.shape[2]
    head_count = feature_width // DH
    grad_other = swap_dp(output_grad)
    patch_other = swap_dp(lax.all_gather(patches, "col", axis=1, tiled=True))
    every_key, every_value, every_patch = (
        lax.all_gather(attn_keys, "col", axis=1, tiled=True),
        lax.all_gather(attn_values, "col", axis=1, tiled=True),
        lax.all_gather(patches, "col", axis=1, tiled=True),
    )
    local_query = queries[0].reshape(local_rows, head_count, DH)
    all_keys = every_key[0].reshape(-1, head_count, DH)
    all_values = every_value[0].reshape(-1, head_count, DH)
    scores = (
        jnp.einsum("qhd,khd->hqk", local_query, all_keys, preferred_element_type=jnp.float32)
        * factor
    )
    row_max = jnp.max(scores, axis=2, keepdims=True)
    log_total = row_max + jnp.log(jnp.sum(jnp.exp(scores - row_max), axis=2, keepdims=True))
    attn_probs = jnp.exp(scores - log_total).astype(jnp.bfloat16)
    attn_out = jnp.einsum(
        "hqk,khd->qhd", attn_probs, all_values, preferred_element_type=jnp.float32
    ).astype(jnp.bfloat16)
    out_local = attn_out.reshape(1, local_rows, feature_width)
    dense_grad = lax.all_gather(output_grad, "row", axis=1, tiled=True)[0]
    attn_grad = lax.psum_scatter(
        lax.dot_general(
            dense_grad, out_weight, (((1,), (1,)), ((), ())), preferred_element_type=jnp.float32
        ),
        "col",
        scatter_dimension=0,
        tiled=True,
    ).astype(jnp.bfloat16)
    grad_heads = attn_grad.reshape(local_rows, head_count, DH)
    prob_grad = jnp.einsum(
        "qhd,khd->hqk", grad_heads, all_values, preferred_element_type=jnp.float32
    )
    row_dot = jnp.transpose(
        jnp.sum(grad_heads.astype(jnp.float32) * attn_out.astype(jnp.float32), axis=2)
    )[:, :, None]
    score_grad = (attn_probs.astype(jnp.float32) * (prob_grad - row_dot)).astype(jnp.bfloat16)
    query_grad = (
        jnp.einsum("hqk,khd->qhd", score_grad, all_keys, preferred_element_type=jnp.float32)
        * factor
    )
    every_out = lax.all_gather(out_local, "col", axis=1, tiled=True)
    key_term = (
        jnp.einsum("hqk,qhd->khd", score_grad, local_query, preferred_element_type=jnp.float32)
        * factor
    )
    value_term = jnp.einsum(
        "hqk,qhd->khd", attn_probs, grad_heads, preferred_element_type=jnp.float32
    )
    key_sum, value_sum = (
        lax.psum_scatter(
            key_term.reshape(-1, feature_width).astype(jnp.bfloat16),
            "col",
            scatter_dimension=0,
            tiled=True,
        ).astype(jnp.float32),
        lax.psum_scatter(
            value_term.reshape(-1, feature_width).astype(jnp.bfloat16),
            "col",
            scatter_dimension=0,
            tiled=True,
        ).astype(jnp.float32),
    )
    out_pair = jnp.concatenate([every_out, swap_dp(every_out)], axis=0)
    grad_pair = lax.all_gather(
        jnp.concatenate([output_grad, grad_other], axis=0), "row", axis=1, tiled=True
    )
    patch_pair = jnp.concatenate([every_patch, patch_other], axis=0)
    out_weight_grad = lax.dot_general(
        out_pair, grad_pair, (((0, 1), (0, 1)), ((), ())), preferred_element_type=jnp.float32
    )
    embed_weight_grad = lax.dot_general(
        patch_pair, grad_pair, (((0, 1), (0, 1)), ((), ())), preferred_element_type=jnp.float32
    )
    return (
        query_grad.reshape(1, local_rows, feature_width),
        key_sum.reshape(1, local_rows, feature_width),
        value_sum.reshape(1, local_rows, feature_width),
        out_weight_grad,
        embed_weight_grad,
    )


def axis_size(axis):
    return lax.psum(1, axis)


def shifted(x, axis, step):
    n = axis_size(axis)
    return lax.ppermute(x, axis, [(j, (j + step) % n) for j in range(n)])


def natural(pieces, axis):
    n = len(pieces)
    order = (lax.axis_index(axis) - jnp.arange(n)) % n
    return jnp.take(jnp.stack(pieces, 0), order, axis=0)


def gather_rows(x, axis):
    n = axis_size(axis)
    pieces = [x] + [shifted(x, axis, s) for s in range(1, n)]
    stacked = natural(pieces, axis)
    return stacked.reshape((n * x.shape[0],) + x.shape[1:])


def group_cols(x, axis, group):
    width = x.shape[1] // axis_size(axis)
    return lax.dynamic_slice_in_dim(x, group * width, width, 1)


def to_heads(x, axis):
    n, me = axis_size(axis), lax.axis_index(axis)
    pieces = [group_cols(x, axis, me)] + [
        shifted(group_cols(x, axis, (me + s) % n), axis, s) for s in range(1, n)
    ]
    stacked = natural(pieces, axis)
    return stacked.reshape((n * x.shape[0],) + stacked.shape[2:])


def from_heads(x, axis):
    n, me = axis_size(axis), lax.axis_index(axis)
    rows = x.shape[0] // n
    block = lambda k: lax.dynamic_slice_in_dim(x, k * rows, rows, 0)
    pieces = [block(me)] + [
        shifted(block((me + s) % n).astype(jnp.bfloat16), axis, s).astype(jnp.float32)
        for s in range(1, n)
    ]
    stacked = natural(pieces, axis)
    return jnp.transpose(stacked, (1, 0, 2)).reshape(rows, n * x.shape[1])


def sum_to_heads(partial, axis):
    n, me = axis_size(axis), lax.axis_index(axis)
    total = group_cols(partial, axis, me)
    for s in range(1, n):
        sent = group_cols(partial, axis, (me - s) % n).astype(jnp.bfloat16)
        total = total + shifted(sent, axis, -s % n).astype(jnp.float32)
    return total


def flat(*arrays):
    return jnp.concatenate([a.reshape(-1) for a in arrays])


def unflat(vector, shapes):
    out, at = [], 0
    for shape in shapes:
        size = int(np.prod(shape))
        out.append(vector[..., at:at + size].reshape(vector.shape[:-1] + shape))
        at += size
    return out


def gather_rows_relayed(x, axis):
    n, me = axis_size(axis), lax.axis_index(axis)
    chips = n // 2
    cross = [x] + [
        lax.ppermute(x, axis, [(j, (j + 2 * s) % n) for j in range(n)]) for s in range(1, chips)
    ]
    partner_own = lax.ppermute(x, axis, [(j, j ^ 1) for j in range(n)])
    if chips > 1:
        relayed = lax.ppermute(jnp.stack(cross[1:], 0), axis, [(j, j ^ 1) for j in range(n)])
        partner = [partner_own] + [relayed[k] for k in range(chips - 1)]
    else:
        partner = [partner_own]
    pieces = jnp.stack(cross + partner, 0)
    j = jnp.arange(n)
    mine = (j % 2) == (me % 2)
    order = jnp.where(mine, ((me - j) % n) // 2, chips + (((me ^ 1) - j) % n) // 2)
    stacked = jnp.take(pieces, order, axis=0)
    return stacked.reshape((n * x.shape[0],) + x.shape[1:])


def roll_blocks(x, shift):
    n = x.shape[0]
    return lax.dynamic_slice_in_dim(jnp.concatenate([x, x], 0), shift % n, n, 0)


def body_heads(patches, queries, attn_keys, attn_values, out_weight, output_grad):
    factor = DH ** (-0.5)
    n, me = axis_size("col"), lax.axis_index("col")
    rank = lax.axis_index("row")
    tokens, width_all = queries.shape[1], queries.shape[2]
    width = width_all // n
    heads = width // DH
    patch_here = patches[0]
    grad_blocks = [output_grad[0]] + [shifted(output_grad[0], "row", s) for s in range(1, n)]
    dense_grad = jnp.concatenate(grad_blocks, 0)
    grad_other = swap_dp(output_grad)
    sources = (queries[0], attn_keys[0], attn_values[0])
    part = lambda g: [lax.dynamic_slice_in_dim(a, g * width, width, 1) for a in sources]
    shapes = [(3, tokens, width), patch_here.shape]
    pieces = [(jnp.stack(part(me), 0), patch_here)]
    for s in range(1, n):
        got = shifted(flat(*part((me + s) % n), patch_here), "col", s)
        pieces.append(tuple(unflat(got, shapes)))
    grad_partial = lax.dot_general(
        dense_grad, out_weight, (((1,), (1,)), ((), ())), preferred_element_type=jnp.float32
    )
    pieces, grad_partial = lax.optimization_barrier((pieces, grad_partial))
    order = me - rank
    qkv_h = roll_blocks(jnp.stack([p[0] for p in pieces], 0), order)
    every_patch = roll_blocks(jnp.stack([p[1] for p in pieces], 0), order).reshape(n * tokens, -1)
    rows = n * tokens
    qkv_h = jnp.transpose(qkv_h, (1, 0, 2, 3)).reshape(3, rows, heads, DH)
    local_query, all_keys, all_values = qkv_h[0], qkv_h[1], qkv_h[2]
    grad_partial, grad_other = lax.optimization_barrier((grad_partial, grad_other))
    other_blocks = [grad_other[0]] + [shifted(grad_other[0], "row", s) for s in range(1, n)]
    scores = (
        jnp.einsum("qhd,khd->hqk", local_query, all_keys, preferred_element_type=jnp.float32)
        * factor
    )
    row_max = jnp.max(scores, axis=2, keepdims=True)
    log_total = row_max + jnp.log(jnp.sum(jnp.exp(scores - row_max), axis=2, keepdims=True))
    attn_probs = jnp.exp(scores - log_total).astype(jnp.bfloat16)
    attn_out = jnp.einsum(
        "hqk,khd->qhd", attn_probs, all_values, preferred_element_type=jnp.float32
    ).astype(jnp.bfloat16)
    attn_grad = sum_to_heads(grad_partial, "col").astype(jnp.bfloat16)
    grad_heads = attn_grad.reshape(rows, heads, DH)
    prob_grad = jnp.einsum(
        "qhd,khd->hqk", grad_heads, all_values, preferred_element_type=jnp.float32
    )
    row_dot = jnp.transpose(
        jnp.sum(grad_heads.astype(jnp.float32) * attn_out.astype(jnp.float32), axis=2)
    )[:, :, None]
    score_grad = (attn_probs.astype(jnp.float32) * (prob_grad - row_dot)).astype(jnp.bfloat16)
    query_grad = (
        jnp.einsum("hqk,khd->qhd", score_grad, all_keys, preferred_element_type=jnp.float32)
        * factor
    )
    key_grad = (
        jnp.einsum("hqk,qhd->khd", score_grad, local_query, preferred_element_type=jnp.float32)
        * factor
    )
    value_grad = jnp.einsum(
        "hqk,qhd->khd", attn_probs, grad_heads, preferred_element_type=jnp.float32
    )
    other_patch = swap_dp(every_patch)
    out_flat = attn_out.reshape(rows, width)
    own_pair = (out_flat, swap_dp(out_flat))
    attn_grad, sent_out = lax.optimization_barrier((attn_grad, out_flat))
    out_pieces = [own_pair] + [
        (got, swap_dp(got)) for got in (shifted(sent_out, "col", -s % n) for s in range(1, n))
    ]
    out_both = roll_blocks(
        jnp.stack([jnp.concatenate(p, 0) for p in out_pieces], 0), -me
    )
    grad_both = jnp.concatenate([dense_grad] + other_blocks, 0)
    out_weight_grad = lax.dot_general(
        out_both, grad_both, (((1,), (0,)), ((), ())), preferred_element_type=jnp.float32
    ).reshape(width_all, -1)
    embed_weight_grad = contract_rows(jnp.concatenate([every_patch, other_patch], 0), grad_both)
    grad_list = [g.reshape(n, tokens, width) for g in (query_grad, key_grad, value_grad)]
    sendable = roll_blocks(
        jnp.stack([g.astype(jnp.bfloat16) for g in grad_list], 1), rank - me
    )
    sendable, out_both = lax.optimization_barrier((sendable, out_both))
    mine = jnp.stack(
        [lax.dynamic_index_in_dim(g, (rank - me) % n, 0, keepdims=False) for g in grad_list], 0
    )
    back = jnp.zeros((3, tokens, width_all), jnp.float32)
    back = lax.dynamic_update_slice_in_dim(back, mine, me * width, 2)
    for s in range(1, n):
        got = shifted(sendable[s], "col", -s % n).astype(jnp.float32)
        back = lax.dynamic_update_slice_in_dim(back, got, ((me + s) % n) * width, 2)
    back = back.reshape(3, 1, tokens, width_all)
    return (back[0], back[1], back[2], out_weight_grad, embed_weight_grad)


def body(patches, queries, attn_keys, attn_values, out_weight, output_grad):
    heads_here = queries.shape[2] // DH
    if (
        heads_here % axis_size("col") == 0
        and queries.shape[1] == output_grad.shape[1]
        and axis_size("row") == axis_size("col")
    ):
        return body_heads(patches, queries, attn_keys, attn_values, out_weight, output_grad)
    return body_tokens(patches, queries, attn_keys, attn_values, out_weight, output_grad)


def solution(mesh):
    placed = (
        P("dp", "col", "row"),
        P("dp", "col", "row"),
        P("dp", "col", "row"),
        P("dp", "col", "row"),
        P("row", "col"),
        P("dp", "row", "col"),
    )
    return jax.shard_map(
        body,
        mesh=mesh,
        in_specs=placed,
        out_specs=(
            P("dp", "col", "row"),
            P("dp", "col", "row"),
            P("dp", "col", "row"),
            P("row", "col"),
            P("row", "col"),
        ),
        check_vma=False,
    )
```

```python
import jax
import numpy as np
import jax.numpy as jnp
from jax import lax
from jax.sharding import PartitionSpec as P

DH = 128


def contract_rows(left, right):
    return lax.dot_general(
        left, right, (((0,), (0,)), ((), ())), preferred_element_type=jnp.float32
    )


def swap_dp(x):
    return lax.ppermute(x, "dp", [(0, 1), (1, 0)])


def body_tokens(patches, queries, attn_keys, attn_values, out_weight, output_grad):
    factor = DH ** (-0.5)
    local_rows = queries.shape[1]
    feature_width = queries.shape[2]
    head_count = feature_width // DH
    grad_other = swap_dp(output_grad)
    patch_other = swap_dp(lax.all_gather(patches, "col", axis=1, tiled=True))
    every_key, every_value, every_patch = (
        lax.all_gather(attn_keys, "col", axis=1, tiled=True),
        lax.all_gather(attn_values, "col", axis=1, tiled=True),
        lax.all_gather(patches, "col", axis=1, tiled=True),
    )
    local_query = queries[0].reshape(local_rows, head_count, DH)
    all_keys = every_key[0].reshape(-1, head_count, DH)
    all_values = every_value[0].reshape(-1, head_count, DH)
    scores = (
        jnp.einsum("qhd,khd->hqk", local_query, all_keys, preferred_element_type=jnp.float32)
        * factor
    )
    row_max = jnp.max(scores, axis=2, keepdims=True)
    log_total = row_max + jnp.log(jnp.sum(jnp.exp(scores - row_max), axis=2, keepdims=True))
    attn_probs = jnp.exp(scores - log_total).astype(jnp.bfloat16)
    attn_out = jnp.einsum(
        "hqk,khd->qhd", attn_probs, all_values, preferred_element_type=jnp.float32
    ).astype(jnp.bfloat16)
    out_local = attn_out.reshape(1, local_rows, feature_width)
    dense_grad = lax.all_gather(output_grad, "row", axis=1, tiled=True)[0]
    attn_grad = lax.psum_scatter(
        lax.dot_general(
            dense_grad, out_weight, (((1,), (1,)), ((), ())), preferred_element_type=jnp.float32
        ),
        "col",
        scatter_dimension=0,
        tiled=True,
    ).astype(jnp.bfloat16)
    grad_heads = attn_grad.reshape(local_rows, head_count, DH)
    prob_grad = jnp.einsum(
        "qhd,khd->hqk", grad_heads, all_values, preferred_element_type=jnp.float32
    )
    row_dot = jnp.transpose(
        jnp.sum(grad_heads.astype(jnp.float32) * attn_out.astype(jnp.float32), axis=2)
    )[:, :, None]
    score_grad = (attn_probs.astype(jnp.float32) * (prob_grad - row_dot)).astype(jnp.bfloat16)
    query_grad = (
        jnp.einsum("hqk,khd->qhd", score_grad, all_keys, preferred_element_type=jnp.float32)
        * factor
    )
    every_out = lax.all_gather(out_local, "col", axis=1, tiled=True)
    key_term = (
        jnp.einsum("hqk,qhd->khd", score_grad, local_query, preferred_element_type=jnp.float32)
        * factor
    )
    value_term = jnp.einsum(
        "hqk,qhd->khd", attn_probs, grad_heads, preferred_element_type=jnp.float32
    )
    key_sum, value_sum = (
        lax.psum_scatter(
            key_term.reshape(-1, feature_width).astype(jnp.bfloat16),
            "col",
            scatter_dimension=0,
            tiled=True,
        ).astype(jnp.float32),
        lax.psum_scatter(
            value_term.reshape(-1, feature_width).astype(jnp.bfloat16),
            "col",
            scatter_dimension=0,
            tiled=True,
        ).astype(jnp.float32),
    )
    out_pair = jnp.concatenate([every_out, swap_dp(every_out)], axis=0)
    grad_pair = lax.all_gather(
        jnp.concatenate([output_grad, grad_other], axis=0), "row", axis=1, tiled=True
    )
    patch_pair = jnp.concatenate([every_patch, patch_other], axis=0)
    out_weight_grad = lax.dot_general(
        out_pair, grad_pair, (((0, 1), (0, 1)), ((), ())), preferred_element_type=jnp.float32
    )
    embed_weight_grad = lax.dot_general(
        patch_pair, grad_pair, (((0, 1), (0, 1)), ((), ())), preferred_element_type=jnp.float32
    )
    return (
        query_grad.reshape(1, local_rows, feature_width),
        key_sum.reshape(1, local_rows, feature_width),
        value_sum.reshape(1, local_rows, feature_width),
        out_weight_grad,
        embed_weight_grad,
    )


def axis_size(axis):
    return lax.psum(1, axis)


def shifted(x, axis, step):
    n = axis_size(axis)
    return lax.ppermute(x, axis, [(j, (j + step) % n) for j in range(n)])


def natural(pieces, axis):
    n = len(pieces)
    order = (lax.axis_index(axis) - jnp.arange(n)) % n
    return jnp.take(jnp.stack(pieces, 0), order, axis=0)


def gather_rows(x, axis):
    n = axis_size(axis)
    pieces = [x] + [shifted(x, axis, s) for s in range(1, n)]
    stacked = natural(pieces, axis)
    return stacked.reshape((n * x.shape[0],) + x.shape[1:])


def group_cols(x, axis, group):
    width = x.shape[1] // axis_size(axis)
    return lax.dynamic_slice_in_dim(x, group * width, width, 1)


def to_heads(x, axis):
    n, me = axis_size(axis), lax.axis_index(axis)
    pieces = [group_cols(x, axis, me)] + [
        shifted(group_cols(x, axis, (me + s) % n), axis, s) for s in range(1, n)
    ]
    stacked = natural(pieces, axis)
    return stacked.reshape((n * x.shape[0],) + stacked.shape[2:])


def from_heads(x, axis):
    n, me = axis_size(axis), lax.axis_index(axis)
    rows = x.shape[0] // n
    block = lambda k: lax.dynamic_slice_in_dim(x, k * rows, rows, 0)
    pieces = [block(me)] + [
        shifted(block((me + s) % n).astype(jnp.bfloat16), axis, s).astype(jnp.float32)
        for s in range(1, n)
    ]
    stacked = natural(pieces, axis)
    return jnp.transpose(stacked, (1, 0, 2)).reshape(rows, n * x.shape[1])


def sum_to_heads(partial, axis):
    n, me = axis_size(axis), lax.axis_index(axis)
    total = group_cols(partial, axis, me)
    for s in range(1, n):
        sent = group_cols(partial, axis, (me - s) % n).astype(jnp.bfloat16)
        total = total + shifted(sent, axis, -s % n).astype(jnp.float32)
    return total


def flat(*arrays):
    return jnp.concatenate([a.reshape(-1) for a in arrays])


def unflat(vector, shapes):
    out, at = [], 0
    for shape in shapes:
        size = int(np.prod(shape))
        out.append(vector[..., at:at + size].reshape(vector.shape[:-1] + shape))
        at += size
    return out


def gather_rows_relayed(x, axis):
    n, me = axis_size(axis), lax.axis_index(axis)
    chips = n // 2
    cross = [x] + [
        lax.ppermute(x, axis, [(j, (j + 2 * s) % n) for j in range(n)]) for s in range(1, chips)
    ]
    partner_own = lax.ppermute(x, axis, [(j, j ^ 1) for j in range(n)])
    if chips > 1:
        relayed = lax.ppermute(jnp.stack(cross[1:], 0), axis, [(j, j ^ 1) for j in range(n)])
        partner = [partner_own] + [relayed[k] for k in range(chips - 1)]
    else:
        partner = [partner_own]
    pieces = jnp.stack(cross + partner, 0)
    j = jnp.arange(n)
    mine = (j % 2) == (me % 2)
    order = jnp.where(mine, ((me - j) % n) // 2, chips + (((me ^ 1) - j) % n) // 2)
    stacked = jnp.take(pieces, order, axis=0)
    return stacked.reshape((n * x.shape[0],) + x.shape[1:])


def roll_blocks(x, shift):
    n = x.shape[0]
    return lax.dynamic_slice_in_dim(jnp.concatenate([x, x], 0), shift % n, n, 0)


def body_heads(patches, queries, attn_keys, attn_values, out_weight, output_grad):
    factor = DH ** (-0.5)
    n, me = axis_size("col"), lax.axis_index("col")
    rank = lax.axis_index("row")
    tokens, width_all = queries.shape[1], queries.shape[2]
    width = width_all // n
    heads = width // DH
    patch_here = patches[0]
    grad_blocks = [output_grad[0]] + [shifted(output_grad[0], "row", s) for s in range(1, n)]
    dense_grad = jnp.concatenate(grad_blocks, 0)
    grad_other = swap_dp(output_grad)
    sources = (queries[0], attn_keys[0], attn_values[0])
    part = lambda g: [lax.dynamic_slice_in_dim(a, g * width, width, 1) for a in sources]
    shapes = [(3, tokens, width), patch_here.shape]
    packets = [shifted(flat(*part((me + s) % n), patch_here), "col", s) for s in range(1, n)]
    grad_partial = lax.dot_general(
        dense_grad, out_weight, (((1,), (1,)), ((), ())), preferred_element_type=jnp.float32
    )
    packets, grad_partial = lax.optimization_barrier((packets, grad_partial))
    pieces = [(jnp.stack(part(me), 0), patch_here)] + [tuple(unflat(p, shapes)) for p in packets]
    order = me - rank
    qkv_h = roll_blocks(jnp.stack([p[0] for p in pieces], 0), order)
    every_patch = roll_blocks(jnp.stack([p[1] for p in pieces], 0), order).reshape(n * tokens, -1)
    rows = n * tokens
    qkv_h = jnp.transpose(qkv_h, (1, 0, 2, 3)).reshape(3, rows, heads, DH)
    local_query, all_keys, all_values = qkv_h[0], qkv_h[1], qkv_h[2]
    grad_partial, grad_other = lax.optimization_barrier((grad_partial, grad_other))
    other_blocks = [grad_other[0]] + [shifted(grad_other[0], "row", s) for s in range(1, n)]
    scores = (
        jnp.einsum("qhd,khd->hqk", local_query, all_keys, preferred_element_type=jnp.float32)
        * factor
    )
    row_max = jnp.max(scores, axis=2, keepdims=True)
    log_total = row_max + jnp.log(jnp.sum(jnp.exp(scores - row_max), axis=2, keepdims=True))
    attn_probs = jnp.exp(scores - log_total).astype(jnp.bfloat16)
    attn_out = jnp.einsum(
        "hqk,khd->qhd", attn_probs, all_values, preferred_element_type=jnp.float32
    ).astype(jnp.bfloat16)
    attn_grad = sum_to_heads(grad_partial, "col").astype(jnp.bfloat16)
    grad_heads = attn_grad.reshape(rows, heads, DH)
    prob_grad = jnp.einsum(
        "qhd,khd->hqk", grad_heads, all_values, preferred_element_type=jnp.float32
    )
    row_dot = jnp.transpose(
        jnp.sum(grad_heads.astype(jnp.float32) * attn_out.astype(jnp.float32), axis=2)
    )[:, :, None]
    score_grad = (attn_probs.astype(jnp.float32) * (prob_grad - row_dot)).astype(jnp.bfloat16)
    query_grad = (
        jnp.einsum("hqk,khd->qhd", score_grad, all_keys, preferred_element_type=jnp.float32)
        * factor
    )
    key_grad = (
        jnp.einsum("hqk,qhd->khd", score_grad, local_query, preferred_element_type=jnp.float32)
        * factor
    )
    value_grad = jnp.einsum(
        "hqk,qhd->khd", attn_probs, grad_heads, preferred_element_type=jnp.float32
    )
    other_patch = swap_dp(every_patch)
    out_flat = attn_out.reshape(rows, width)
    own_pair = (out_flat, swap_dp(out_flat))
    attn_grad, sent_out = lax.optimization_barrier((attn_grad, out_flat))
    out_pieces = [own_pair] + [
        (got, swap_dp(got)) for got in (shifted(sent_out, "col", -s % n) for s in range(1, n))
    ]
    out_both = roll_blocks(
        jnp.stack([jnp.concatenate(p, 0) for p in out_pieces], 0), -me
    )
    grad_both = jnp.concatenate([dense_grad] + other_blocks, 0)
    out_weight_grad = lax.dot_general(
        out_both, grad_both, (((1,), (0,)), ((), ())), preferred_element_type=jnp.float32
    ).reshape(width_all, -1)
    embed_weight_grad = contract_rows(jnp.concatenate([every_patch, other_patch], 0), grad_both)
    grad_list = [g.reshape(n, tokens, width) for g in (query_grad, key_grad, value_grad)]
    sendable = roll_blocks(
        jnp.stack([g.astype(jnp.bfloat16) for g in grad_list], 1), rank - me
    )
    sendable, out_both = lax.optimization_barrier((sendable, out_both))
    mine = jnp.stack(
        [lax.dynamic_index_in_dim(g, (rank - me) % n, 0, keepdims=False) for g in grad_list], 0
    )
    back = jnp.zeros((3, tokens, width_all), jnp.float32)
    back = lax.dynamic_update_slice_in_dim(back, mine, me * width, 2)
    for s in range(1, n):
        got = shifted(sendable[s], "col", -s % n).astype(jnp.float32)
        back = lax.dynamic_update_slice_in_dim(back, got, ((me + s) % n) * width, 2)
    back = back.reshape(3, 1, tokens, width_all)
    return (back[0], back[1], back[2], out_weight_grad, embed_weight_grad)


def body(patches, queries, attn_keys, attn_values, out_weight, output_grad):
    heads_here = queries.shape[2] // DH
    if (
        heads_here % axis_size("col") == 0
        and queries.shape[1] == output_grad.shape[1]
        and axis_size("row") == axis_size("col")
    ):
        return body_heads(patches, queries, attn_keys, attn_values, out_weight, output_grad)
    return body_tokens(patches, queries, attn_keys, attn_values, out_weight, output_grad)


def solution(mesh):
    placed = (
        P("dp", "col", "row"),
        P("dp", "col", "row"),
        P("dp", "col", "row"),
        P("dp", "col", "row"),
        P("row", "col"),
        P("dp", "row", "col"),
    )
    return jax.shard_map(
        body,
        mesh=mesh,
        in_specs=placed,
        out_specs=(
            P("dp", "col", "row"),
            P("dp", "col", "row"),
            P("dp", "col", "row"),
            P("row", "col"),
            P("row", "col"),
        ),
        check_vma=False,
    )
```

```python
import jax
import numpy as np
import jax.numpy as jnp
from jax import lax
from jax.sharding import PartitionSpec as P

DH = 128


def contract_rows(left, right):
    return lax.dot_general(
        left, right, (((0,), (0,)), ((), ())), preferred_element_type=jnp.float32
    )


def swap_dp(x):
    return lax.ppermute(x, "dp", [(0, 1), (1, 0)])


def body_tokens(patches, queries, attn_keys, attn_values, out_weight, output_grad):
    factor = DH ** (-0.5)
    local_rows = queries.shape[1]
    feature_width = queries.shape[2]
    head_count = feature_width // DH
    grad_other = swap_dp(output_grad)
    patch_other = swap_dp(lax.all_gather(patches, "col", axis=1, tiled=True))
    every_key, every_value, every_patch = (
        lax.all_gather(attn_keys, "col", axis=1, tiled=True),
        lax.all_gather(attn_values, "col", axis=1, tiled=True),
        lax.all_gather(patches, "col", axis=1, tiled=True),
    )
    local_query = queries[0].reshape(local_rows, head_count, DH)
    all_keys = every_key[0].reshape(-1, head_count, DH)
    all_values = every_value[0].reshape(-1, head_count, DH)
    scores = (
        jnp.einsum("qhd,khd->hqk", local_query, all_keys, preferred_element_type=jnp.float32)
        * factor
    )
    row_max = jnp.max(scores, axis=2, keepdims=True)
    log_total = row_max + jnp.log(jnp.sum(jnp.exp(scores - row_max), axis=2, keepdims=True))
    attn_probs = jnp.exp(scores - log_total).astype(jnp.bfloat16)
    attn_out = jnp.einsum(
        "hqk,khd->qhd", attn_probs, all_values, preferred_element_type=jnp.float32
    ).astype(jnp.bfloat16)
    out_local = attn_out.reshape(1, local_rows, feature_width)
    dense_grad = lax.all_gather(output_grad, "row", axis=1, tiled=True)[0]
    attn_grad = lax.psum_scatter(
        lax.dot_general(
            dense_grad, out_weight, (((1,), (1,)), ((), ())), preferred_element_type=jnp.float32
        ),
        "col",
        scatter_dimension=0,
        tiled=True,
    ).astype(jnp.bfloat16)
    grad_heads = attn_grad.reshape(local_rows, head_count, DH)
    prob_grad = jnp.einsum(
        "qhd,khd->hqk", grad_heads, all_values, preferred_element_type=jnp.float32
    )
    row_dot = jnp.transpose(
        jnp.sum(grad_heads.astype(jnp.float32) * attn_out.astype(jnp.float32), axis=2)
    )[:, :, None]
    score_grad = (attn_probs.astype(jnp.float32) * (prob_grad - row_dot)).astype(jnp.bfloat16)
    query_grad = (
        jnp.einsum("hqk,khd->qhd", score_grad, all_keys, preferred_element_type=jnp.float32)
        * factor
    )
    every_out = lax.all_gather(out_local, "col", axis=1, tiled=True)
    key_term = (
        jnp.einsum("hqk,qhd->khd", score_grad, local_query, preferred_element_type=jnp.float32)
        * factor
    )
    value_term = jnp.einsum(
        "hqk,qhd->khd", attn_probs, grad_heads, preferred_element_type=jnp.float32
    )
    key_sum, value_sum = (
        lax.psum_scatter(
            key_term.reshape(-1, feature_width).astype(jnp.bfloat16),
            "col",
            scatter_dimension=0,
            tiled=True,
        ).astype(jnp.float32),
        lax.psum_scatter(
            value_term.reshape(-1, feature_width).astype(jnp.bfloat16),
            "col",
            scatter_dimension=0,
            tiled=True,
        ).astype(jnp.float32),
    )
    out_pair = jnp.concatenate([every_out, swap_dp(every_out)], axis=0)
    grad_pair = lax.all_gather(
        jnp.concatenate([output_grad, grad_other], axis=0), "row", axis=1, tiled=True
    )
    patch_pair = jnp.concatenate([every_patch, patch_other], axis=0)
    out_weight_grad = lax.dot_general(
        out_pair, grad_pair, (((0, 1), (0, 1)), ((), ())), preferred_element_type=jnp.float32
    )
    embed_weight_grad = lax.dot_general(
        patch_pair, grad_pair, (((0, 1), (0, 1)), ((), ())), preferred_element_type=jnp.float32
    )
    return (
        query_grad.reshape(1, local_rows, feature_width),
        key_sum.reshape(1, local_rows, feature_width),
        value_sum.reshape(1, local_rows, feature_width),
        out_weight_grad,
        embed_weight_grad,
    )


def axis_size(axis):
    return lax.psum(1, axis)


def shifted(x, axis, step):
    n = axis_size(axis)
    return lax.ppermute(x, axis, [(j, (j + step) % n) for j in range(n)])


def natural(pieces, axis):
    n = len(pieces)
    order = (lax.axis_index(axis) - jnp.arange(n)) % n
    return jnp.take(jnp.stack(pieces, 0), order, axis=0)


def gather_rows(x, axis):
    n = axis_size(axis)
    pieces = [x] + [shifted(x, axis, s) for s in range(1, n)]
    stacked = natural(pieces, axis)
    return stacked.reshape((n * x.shape[0],) + x.shape[1:])


def group_cols(x, axis, group):
    width = x.shape[1] // axis_size(axis)
    return lax.dynamic_slice_in_dim(x, group * width, width, 1)


def to_heads(x, axis):
    n, me = axis_size(axis), lax.axis_index(axis)
    pieces = [group_cols(x, axis, me)] + [
        shifted(group_cols(x, axis, (me + s) % n), axis, s) for s in range(1, n)
    ]
    stacked = natural(pieces, axis)
    return stacked.reshape((n * x.shape[0],) + stacked.shape[2:])


def from_heads(x, axis):
    n, me = axis_size(axis), lax.axis_index(axis)
    rows = x.shape[0] // n
    block = lambda k: lax.dynamic_slice_in_dim(x, k * rows, rows, 0)
    pieces = [block(me)] + [
        shifted(block((me + s) % n).astype(jnp.bfloat16), axis, s).astype(jnp.float32)
        for s in range(1, n)
    ]
    stacked = natural(pieces, axis)
    return jnp.transpose(stacked, (1, 0, 2)).reshape(rows, n * x.shape[1])


def sum_to_heads(partial, axis):
    n, me = axis_size(axis), lax.axis_index(axis)
    total = group_cols(partial, axis, me)
    for s in range(1, n):
        sent = group_cols(partial, axis, (me - s) % n).astype(jnp.bfloat16)
        total = total + shifted(sent, axis, -s % n).astype(jnp.float32)
    return total


def flat(*arrays):
    return jnp.concatenate([a.reshape(-1) for a in arrays])


def unflat(vector, shapes):
    out, at = [], 0
    for shape in shapes:
        size = int(np.prod(shape))
        out.append(vector[..., at:at + size].reshape(vector.shape[:-1] + shape))
        at += size
    return out


def gather_rows_relayed(x, axis):
    n, me = axis_size(axis), lax.axis_index(axis)
    chips = n // 2
    cross = [x] + [
        lax.ppermute(x, axis, [(j, (j + 2 * s) % n) for j in range(n)]) for s in range(1, chips)
    ]
    partner_own = lax.ppermute(x, axis, [(j, j ^ 1) for j in range(n)])
    if chips > 1:
        relayed = lax.ppermute(jnp.stack(cross[1:], 0), axis, [(j, j ^ 1) for j in range(n)])
        partner = [partner_own] + [relayed[k] for k in range(chips - 1)]
    else:
        partner = [partner_own]
    pieces = jnp.stack(cross + partner, 0)
    j = jnp.arange(n)
    mine = (j % 2) == (me % 2)
    order = jnp.where(mine, ((me - j) % n) // 2, chips + (((me ^ 1) - j) % n) // 2)
    stacked = jnp.take(pieces, order, axis=0)
    return stacked.reshape((n * x.shape[0],) + x.shape[1:])


def roll_blocks(x, shift):
    n = x.shape[0]
    return lax.dynamic_slice_in_dim(jnp.concatenate([x, x], 0), shift % n, n, 0)


def body_heads(patches, queries, attn_keys, attn_values, out_weight, output_grad):
    factor = DH ** (-0.5)
    n, me = axis_size("col"), lax.axis_index("col")
    rank = lax.axis_index("row")
    tokens, width_all = queries.shape[1], queries.shape[2]
    width = width_all // n
    heads = width // DH
    patch_here = patches[0]
    grad_blocks = [output_grad[0]] + [shifted(output_grad[0], "row", s) for s in range(1, n)]
    dense_grad = jnp.concatenate(grad_blocks, 0)
    grad_other = swap_dp(output_grad)
    sources = (queries[0], attn_keys[0], attn_values[0])
    part = lambda g: [lax.dynamic_slice_in_dim(a, g * width, width, 1) for a in sources]
    shapes = [(3, tokens, width), patch_here.shape]
    pieces = [(jnp.stack(part(me), 0), patch_here)]
    for s in range(1, n):
        got = shifted(flat(*part((me + s) % n), patch_here), "col", s)
        pieces.append(tuple(unflat(got, shapes)))
    grad_partial = lax.dot_general(
        dense_grad, out_weight, (((1,), (1,)), ((), ())), preferred_element_type=jnp.float32
    )
    pieces, grad_partial = lax.optimization_barrier((pieces, grad_partial))
    order = me - rank
    qkv_h = roll_blocks(jnp.stack([p[0] for p in pieces], 0), order)
    every_patch = roll_blocks(jnp.stack([p[1] for p in pieces], 0), order).reshape(n * tokens, -1)
    rows = n * tokens
    qkv_h = jnp.transpose(qkv_h, (1, 0, 2, 3)).reshape(3, rows, heads, DH)
    local_query, all_keys, all_values = qkv_h[0], qkv_h[1], qkv_h[2]
    grad_partial, grad_other = lax.optimization_barrier((grad_partial, grad_other))
    other_blocks = [grad_other[0]] + [shifted(grad_other[0], "row", s) for s in range(1, n)]
    scores = (
        jnp.einsum("qhd,khd->hqk", local_query, all_keys, preferred_element_type=jnp.float32)
        * factor
    )
    row_max = jnp.max(scores, axis=2, keepdims=True)
    log_total = row_max + jnp.log(jnp.sum(jnp.exp(scores - row_max), axis=2, keepdims=True))
    attn_probs = jnp.exp(scores - log_total).astype(jnp.bfloat16)
    attn_out = jnp.einsum(
        "hqk,khd->qhd", attn_probs, all_values, preferred_element_type=jnp.float32
    ).astype(jnp.bfloat16)
    attn_grad = sum_to_heads(grad_partial, "col").astype(jnp.bfloat16)
    grad_heads = attn_grad.reshape(rows, heads, DH)
    prob_grad = jnp.einsum(
        "qhd,khd->hqk", grad_heads, all_values, preferred_element_type=jnp.float32
    )
    row_dot = jnp.transpose(
        jnp.sum(grad_heads.astype(jnp.float32) * attn_out.astype(jnp.float32), axis=2)
    )[:, :, None]
    score_grad = (attn_probs.astype(jnp.float32) * (prob_grad - row_dot)).astype(jnp.bfloat16)
    query_grad = (
        jnp.einsum("hqk,khd->qhd", score_grad, all_keys, preferred_element_type=jnp.float32)
        * factor
    )
    key_grad = (
        jnp.einsum("hqk,qhd->khd", score_grad, local_query, preferred_element_type=jnp.float32)
        * factor
    )
    value_grad = jnp.einsum(
        "hqk,qhd->khd", attn_probs, grad_heads, preferred_element_type=jnp.float32
    )
    other_patch = swap_dp(every_patch)
    out_flat = attn_out.reshape(rows, width)
    own_pair = (out_flat, swap_dp(out_flat))
    attn_grad, sent_out = lax.optimization_barrier((attn_grad, out_flat))
    out_pieces = [own_pair] + [
        (got, swap_dp(got)) for got in (shifted(sent_out, "col", -s % n) for s in range(1, n))
    ]
    out_both = roll_blocks(
        jnp.stack([jnp.concatenate(p, 0) for p in out_pieces], 0), -me
    )
    grad_both = jnp.concatenate([dense_grad] + other_blocks, 0)
    embed_weight_grad = contract_rows(jnp.concatenate([every_patch, other_patch], 0), grad_both)
    grad_list = [g.reshape(n, tokens, width) for g in (query_grad, key_grad, value_grad)]
    sendable = roll_blocks(
        jnp.stack([g.astype(jnp.bfloat16) for g in grad_list], 1), rank - me
    )
    sendable, out_both = lax.optimization_barrier((sendable, out_both))
    out_weight_grad = lax.dot_general(
        out_both, grad_both, (((1,), (0,)), ((), ())), preferred_element_type=jnp.float32
    ).reshape(width_all, -1)
    mine = jnp.stack(
        [lax.dynamic_index_in_dim(g, (rank - me) % n, 0, keepdims=False) for g in grad_list], 0
    )
    back = jnp.zeros((3, tokens, width_all), jnp.float32)
    back = lax.dynamic_update_slice_in_dim(back, mine, me * width, 2)
    for s in range(1, n):
        got = shifted(sendable[s], "col", -s % n).astype(jnp.float32)
        back = lax.dynamic_update_slice_in_dim(back, got, ((me + s) % n) * width, 2)
    back = back.reshape(3, 1, tokens, width_all)
    return (back[0], back[1], back[2], out_weight_grad, embed_weight_grad)


def body(patches, queries, attn_keys, attn_values, out_weight, output_grad):
    heads_here = queries.shape[2] // DH
    if (
        heads_here % axis_size("col") == 0
        and queries.shape[1] == output_grad.shape[1]
        and axis_size("row") == axis_size("col")
    ):
        return body_heads(patches, queries, attn_keys, attn_values, out_weight, output_grad)
    return body_tokens(patches, queries, attn_keys, attn_values, out_weight, output_grad)


def solution(mesh):
    placed = (
        P("dp", "col", "row"),
        P("dp", "col", "row"),
        P("dp", "col", "row"),
        P("dp", "col", "row"),
        P("row", "col"),
        P("dp", "row", "col"),
    )
    return jax.shard_map(
        body,
        mesh=mesh,
        in_specs=placed,
        out_specs=(
            P("dp", "col", "row"),
            P("dp", "col", "row"),
            P("dp", "col", "row"),
            P("row", "col"),
            P("row", "col"),
        ),
        check_vma=False,
    )
```

```python
import jax
import numpy as np
import jax.numpy as jnp
from jax import lax
from jax.sharding import PartitionSpec as P

DH = 128


def contract_rows(left, right):
    return lax.dot_general(
        left, right, (((0,), (0,)), ((), ())), preferred_element_type=jnp.float32
    )


def swap_dp(x):
    return lax.ppermute(x, "dp", [(0, 1), (1, 0)])


def body_tokens(patches, queries, attn_keys, attn_values, out_weight, output_grad):
    factor = DH ** (-0.5)
    local_rows = queries.shape[1]
    feature_width = queries.shape[2]
    head_count = feature_width // DH
    grad_other = swap_dp(output_grad)
    patch_other = swap_dp(lax.all_gather(patches, "col", axis=1, tiled=True))
    every_key, every_value, every_patch = (
        lax.all_gather(attn_keys, "col", axis=1, tiled=True),
        lax.all_gather(attn_values, "col", axis=1, tiled=True),
        lax.all_gather(patches, "col", axis=1, tiled=True),
    )
    local_query = queries[0].reshape(local_rows, head_count, DH)
    all_keys = every_key[0].reshape(-1, head_count, DH)
    all_values = every_value[0].reshape(-1, head_count, DH)
    scores = (
        jnp.einsum("qhd,khd->hqk", local_query, all_keys, preferred_element_type=jnp.float32)
        * factor
    )
    row_max = jnp.max(scores, axis=2, keepdims=True)
    log_total = row_max + jnp.log(jnp.sum(jnp.exp(scores - row_max), axis=2, keepdims=True))
    attn_probs = jnp.exp(scores - log_total).astype(jnp.bfloat16)
    attn_out = jnp.einsum(
        "hqk,khd->qhd", attn_probs, all_values, preferred_element_type=jnp.float32
    ).astype(jnp.bfloat16)
    out_local = attn_out.reshape(1, local_rows, feature_width)
    dense_grad = lax.all_gather(output_grad, "row", axis=1, tiled=True)[0]
    attn_grad = lax.psum_scatter(
        lax.dot_general(
            dense_grad, out_weight, (((1,), (1,)), ((), ())), preferred_element_type=jnp.float32
        ),
        "col",
        scatter_dimension=0,
        tiled=True,
    ).astype(jnp.bfloat16)
    grad_heads = attn_grad.reshape(local_rows, head_count, DH)
    prob_grad = jnp.einsum(
        "qhd,khd->hqk", grad_heads, all_values, preferred_element_type=jnp.float32
    )
    row_dot = jnp.transpose(
        jnp.sum(grad_heads.astype(jnp.float32) * attn_out.astype(jnp.float32), axis=2)
    )[:, :, None]
    score_grad = (attn_probs.astype(jnp.float32) * (prob_grad - row_dot)).astype(jnp.bfloat16)
    query_grad = (
        jnp.einsum("hqk,khd->qhd", score_grad, all_keys, preferred_element_type=jnp.float32)
        * factor
    )
    every_out = lax.all_gather(out_local, "col", axis=1, tiled=True)
    key_term = (
        jnp.einsum("hqk,qhd->khd", score_grad, local_query, preferred_element_type=jnp.float32)
        * factor
    )
    value_term = jnp.einsum(
        "hqk,qhd->khd", attn_probs, grad_heads, preferred_element_type=jnp.float32
    )
    key_sum, value_sum = (
        lax.psum_scatter(
            key_term.reshape(-1, feature_width).astype(jnp.bfloat16),
            "col",
            scatter_dimension=0,
            tiled=True,
        ).astype(jnp.float32),
        lax.psum_scatter(
            value_term.reshape(-1, feature_width).astype(jnp.bfloat16),
            "col",
            scatter_dimension=0,
            tiled=True,
        ).astype(jnp.float32),
    )
    out_pair = jnp.concatenate([every_out, swap_dp(every_out)], axis=0)
    grad_pair = lax.all_gather(
        jnp.concatenate([output_grad, grad_other], axis=0), "row", axis=1, tiled=True
    )
    patch_pair = jnp.concatenate([every_patch, patch_other], axis=0)
    out_weight_grad = lax.dot_general(
        out_pair, grad_pair, (((0, 1), (0, 1)), ((), ())), preferred_element_type=jnp.float32
    )
    embed_weight_grad = lax.dot_general(
        patch_pair, grad_pair, (((0, 1), (0, 1)), ((), ())), preferred_element_type=jnp.float32
    )
    return (
        query_grad.reshape(1, local_rows, feature_width),
        key_sum.reshape(1, local_rows, feature_width),
        value_sum.reshape(1, local_rows, feature_width),
        out_weight_grad,
        embed_weight_grad,
    )


def axis_size(axis):
    return lax.psum(1, axis)


def shifted(x, axis, step):
    n = axis_size(axis)
    return lax.ppermute(x, axis, [(j, (j + step) % n) for j in range(n)])


def natural(pieces, axis):
    n = len(pieces)
    order = (lax.axis_index(axis) - jnp.arange(n)) % n
    return jnp.take(jnp.stack(pieces, 0), order, axis=0)


def gather_rows(x, axis):
    n = axis_size(axis)
    pieces = [x] + [shifted(x, axis, s) for s in range(1, n)]
    stacked = natural(pieces, axis)
    return stacked.reshape((n * x.shape[0],) + x.shape[1:])


def group_cols(x, axis, group):
    width = x.shape[1] // axis_size(axis)
    return lax.dynamic_slice_in_dim(x, group * width, width, 1)


def to_heads(x, axis):
    n, me = axis_size(axis), lax.axis_index(axis)
    pieces = [group_cols(x, axis, me)] + [
        shifted(group_cols(x, axis, (me + s) % n), axis, s) for s in range(1, n)
    ]
    stacked = natural(pieces, axis)
    return stacked.reshape((n * x.shape[0],) + stacked.shape[2:])


def from_heads(x, axis):
    n, me = axis_size(axis), lax.axis_index(axis)
    rows = x.shape[0] // n
    block = lambda k: lax.dynamic_slice_in_dim(x, k * rows, rows, 0)
    pieces = [block(me)] + [
        shifted(block((me + s) % n).astype(jnp.bfloat16), axis, s).astype(jnp.float32)
        for s in range(1, n)
    ]
    stacked = natural(pieces, axis)
    return jnp.transpose(stacked, (1, 0, 2)).reshape(rows, n * x.shape[1])


def sum_to_heads(partial, axis):
    n, me = axis_size(axis), lax.axis_index(axis)
    total = group_cols(partial, axis, me)
    for s in range(1, n):
        sent = group_cols(partial, axis, (me - s) % n).astype(jnp.bfloat16)
        total = total + shifted(sent, axis, -s % n).astype(jnp.float32)
    return total


def flat(*arrays):
    return jnp.concatenate([a.reshape(-1) for a in arrays])


def unflat(vector, shapes):
    out, at = [], 0
    for shape in shapes:
        size = int(np.prod(shape))
        out.append(vector[..., at:at + size].reshape(vector.shape[:-1] + shape))
        at += size
    return out


def gather_rows_relayed(x, axis):
    n, me = axis_size(axis), lax.axis_index(axis)
    chips = n // 2
    cross = [x] + [
        lax.ppermute(x, axis, [(j, (j + 2 * s) % n) for j in range(n)]) for s in range(1, chips)
    ]
    partner_own = lax.ppermute(x, axis, [(j, j ^ 1) for j in range(n)])
    if chips > 1:
        relayed = lax.ppermute(jnp.stack(cross[1:], 0), axis, [(j, j ^ 1) for j in range(n)])
        partner = [partner_own] + [relayed[k] for k in range(chips - 1)]
    else:
        partner = [partner_own]
    pieces = jnp.stack(cross + partner, 0)
    j = jnp.arange(n)
    mine = (j % 2) == (me % 2)
    order = jnp.where(mine, ((me - j) % n) // 2, chips + (((me ^ 1) - j) % n) // 2)
    stacked = jnp.take(pieces, order, axis=0)
    return stacked.reshape((n * x.shape[0],) + x.shape[1:])


def roll_blocks(x, shift):
    n = x.shape[0]
    return lax.dynamic_slice_in_dim(jnp.concatenate([x, x], 0), shift % n, n, 0)


def body_heads(patches, queries, attn_keys, attn_values, out_weight, output_grad):
    factor = DH ** (-0.5)
    n, me = axis_size("col"), lax.axis_index("col")
    rank = lax.axis_index("row")
    tokens, width_all = queries.shape[1], queries.shape[2]
    width = width_all // n
    heads = width // DH
    patch_here = patches[0]
    grad_blocks = [output_grad[0]] + [shifted(output_grad[0], "row", s) for s in range(1, n)]
    dense_grad = jnp.concatenate(grad_blocks, 0)
    grad_other = swap_dp(output_grad)
    sources = (queries[0], attn_keys[0], attn_values[0])
    part = lambda g: [lax.dynamic_slice_in_dim(a, g * width, width, 1) for a in sources]
    shapes = [(3, tokens, width), patch_here.shape]
    pieces = [(jnp.stack(part(me), 0), patch_here)]
    for s in range(1, n):
        got = shifted(flat(*part((me + s) % n), patch_here), "col", s)
        pieces.append(tuple(unflat(got, shapes)))
    grad_partial = lax.dot_general(
        dense_grad, out_weight, (((1,), (1,)), ((), ())), preferred_element_type=jnp.float32
    )
    pieces, grad_partial = lax.optimization_barrier((pieces, grad_partial))
    order = me - rank
    qkv_h = roll_blocks(jnp.stack([p[0] for p in pieces], 0), order)
    every_patch = roll_blocks(jnp.stack([p[1] for p in pieces], 0), order).reshape(n * tokens, -1)
    rows = n * tokens
    qkv_h = jnp.transpose(qkv_h, (1, 0, 2, 3)).reshape(3, rows, heads, DH)
    local_query, all_keys, all_values = qkv_h[0], qkv_h[1], qkv_h[2]
    grad_partial, grad_other = lax.optimization_barrier((grad_partial, grad_other))
    other_blocks = [grad_other[0]] + [shifted(grad_other[0], "row", s) for s in range(1, n)]
    scores = (
        jnp.einsum("qhd,khd->hqk", local_query, all_keys, preferred_element_type=jnp.float32)
        * factor
    )
    row_max = jnp.max(scores, axis=2, keepdims=True)
    log_total = row_max + jnp.log(jnp.sum(jnp.exp(scores - row_max), axis=2, keepdims=True))
    attn_probs = jnp.exp(scores - log_total).astype(jnp.bfloat16)
    attn_out = jnp.einsum(
        "hqk,khd->qhd", attn_probs, all_values, preferred_element_type=jnp.float32
    ).astype(jnp.bfloat16)
    attn_grad = sum_to_heads(grad_partial, "col").astype(jnp.bfloat16)
    grad_heads = attn_grad.reshape(rows, heads, DH)
    prob_grad = jnp.einsum(
        "qhd,khd->hqk", grad_heads, all_values, preferred_element_type=jnp.float32
    )
    row_dot = jnp.transpose(
        jnp.sum(grad_heads.astype(jnp.float32) * attn_out.astype(jnp.float32), axis=2)
    )[:, :, None]
    score_grad = (attn_probs.astype(jnp.float32) * (prob_grad - row_dot)).astype(jnp.bfloat16)
    query_grad = (
        jnp.einsum("hqk,khd->qhd", score_grad, all_keys, preferred_element_type=jnp.float32)
        * factor
    )
    key_grad = (
        jnp.einsum("hqk,qhd->khd", score_grad, local_query, preferred_element_type=jnp.float32)
        * factor
    )
    value_grad = jnp.einsum(
        "hqk,qhd->khd", attn_probs, grad_heads, preferred_element_type=jnp.float32
    )
    other_patch = swap_dp(every_patch)
    out_flat = attn_out.reshape(rows, width)
    own_pair = (out_flat, swap_dp(out_flat))
    attn_grad, sent_out = lax.optimization_barrier((attn_grad, out_flat))
    out_pieces = [own_pair] + [
        (got, swap_dp(got)) for got in (shifted(sent_out, "col", -s % n) for s in range(1, n))
    ]
    out_both = roll_blocks(
        jnp.stack([jnp.concatenate(p, 0) for p in out_pieces], 0), -me
    )
    grad_both = jnp.concatenate([dense_grad] + other_blocks, 0)
    embed_weight_grad = contract_rows(jnp.concatenate([every_patch, other_patch], 0), grad_both)
    grad_list = [g.reshape(n, tokens, width) for g in (query_grad, key_grad, value_grad)]
    sendable = roll_blocks(
        jnp.stack([g.astype(jnp.bfloat16) for g in grad_list], 1), rank - me
    )
    sendable, _ = lax.optimization_barrier((sendable, [p[0] for p in out_pieces]))
    out_both, sendable = lax.optimization_barrier((out_both, sendable))
    out_weight_grad = lax.dot_general(
        out_both, grad_both, (((1,), (0,)), ((), ())), preferred_element_type=jnp.float32
    ).reshape(width_all, -1)
    mine = jnp.stack(
        [lax.dynamic_index_in_dim(g, (rank - me) % n, 0, keepdims=False) for g in grad_list], 0
    )
    back = jnp.zeros((3, tokens, width_all), jnp.float32)
    back = lax.dynamic_update_slice_in_dim(back, mine, me * width, 2)
    for s in range(1, n):
        got = shifted(sendable[s], "col", -s % n).astype(jnp.float32)
        back = lax.dynamic_update_slice_in_dim(back, got, ((me + s) % n) * width, 2)
    back = back.reshape(3, 1, tokens, width_all)
    return (back[0], back[1], back[2], out_weight_grad, embed_weight_grad)


def body(patches, queries, attn_keys, attn_values, out_weight, output_grad):
    heads_here = queries.shape[2] // DH
    if (
        heads_here % axis_size("col") == 0
        and queries.shape[1] == output_grad.shape[1]
        and axis_size("row") == axis_size("col")
    ):
        return body_heads(patches, queries, attn_keys, attn_values, out_weight, output_grad)
    return body_tokens(patches, queries, attn_keys, attn_values, out_weight, output_grad)


def solution(mesh):
    placed = (
        P("dp", "col", "row"),
        P("dp", "col", "row"),
        P("dp", "col", "row"),
        P("dp", "col", "row"),
        P("row", "col"),
        P("dp", "row", "col"),
    )
    return jax.shard_map(
        body,
        mesh=mesh,
        in_specs=placed,
        out_specs=(
            P("dp", "col", "row"),
            P("dp", "col", "row"),
            P("dp", "col", "row"),
            P("row", "col"),
            P("row", "col"),
        ),
        check_vma=False,
    )
```

```python
import jax
import numpy as np
import jax.numpy as jnp
from jax import lax
from jax.sharding import PartitionSpec as P

DH = 128


def contract_rows(left, right):
    return lax.dot_general(
        left, right, (((0,), (0,)), ((), ())), preferred_element_type=jnp.float32
    )


def swap_dp(x):
    return lax.ppermute(x, "dp", [(0, 1), (1, 0)])


def body_tokens(patches, queries, attn_keys, attn_values, out_weight, output_grad):
    factor = DH ** (-0.5)
    local_rows = queries.shape[1]
    feature_width = queries.shape[2]
    head_count = feature_width // DH
    grad_other = swap_dp(output_grad)
    patch_other = swap_dp(lax.all_gather(patches, "col", axis=1, tiled=True))
    every_key, every_value, every_patch = (
        lax.all_gather(attn_keys, "col", axis=1, tiled=True),
        lax.all_gather(attn_values, "col", axis=1, tiled=True),
        lax.all_gather(patches, "col", axis=1, tiled=True),
    )
    local_query = queries[0].reshape(local_rows, head_count, DH)
    all_keys = every_key[0].reshape(-1, head_count, DH)
    all_values = every_value[0].reshape(-1, head_count, DH)
    scores = (
        jnp.einsum("qhd,khd->hqk", local_query, all_keys, preferred_element_type=jnp.float32)
        * factor
    )
    row_max = jnp.max(scores, axis=2, keepdims=True)
    log_total = row_max + jnp.log(jnp.sum(jnp.exp(scores - row_max), axis=2, keepdims=True))
    attn_probs = jnp.exp(scores - log_total).astype(jnp.bfloat16)
    attn_out = jnp.einsum(
        "hqk,khd->qhd", attn_probs, all_values, preferred_element_type=jnp.float32
    ).astype(jnp.bfloat16)
    out_local = attn_out.reshape(1, local_rows, feature_width)
    dense_grad = lax.all_gather(output_grad, "row", axis=1, tiled=True)[0]
    attn_grad = lax.psum_scatter(
        lax.dot_general(
            dense_grad, out_weight, (((1,), (1,)), ((), ())), preferred_element_type=jnp.float32
        ),
        "col",
        scatter_dimension=0,
        tiled=True,
    ).astype(jnp.bfloat16)
    grad_heads = attn_grad.reshape(local_rows, head_count, DH)
    prob_grad = jnp.einsum(
        "qhd,khd->hqk", grad_heads, all_values, preferred_element_type=jnp.float32
    )
    row_dot = jnp.transpose(
        jnp.sum(grad_heads.astype(jnp.float32) * attn_out.astype(jnp.float32), axis=2)
    )[:, :, None]
    score_grad = (attn_probs.astype(jnp.float32) * (prob_grad - row_dot)).astype(jnp.bfloat16)
    query_grad = (
        jnp.einsum("hqk,khd->qhd", score_grad, all_keys, preferred_element_type=jnp.float32)
        * factor
    )
    every_out = lax.all_gather(out_local, "col", axis=1, tiled=True)
    key_term = (
        jnp.einsum("hqk,qhd->khd", score_grad, local_query, preferred_element_type=jnp.float32)
        * factor
    )
    value_term = jnp.einsum(
        "hqk,qhd->khd", attn_probs, grad_heads, preferred_element_type=jnp.float32
    )
    key_sum, value_sum = (
        lax.psum_scatter(
            key_term.reshape(-1, feature_width).astype(jnp.bfloat16),
            "col",
            scatter_dimension=0,
            tiled=True,
        ).astype(jnp.float32),
        lax.psum_scatter(
            value_term.reshape(-1, feature_width).astype(jnp.bfloat16),
            "col",
            scatter_dimension=0,
            tiled=True,
        ).astype(jnp.float32),
    )
    out_pair = jnp.concatenate([every_out, swap_dp(every_out)], axis=0)
    grad_pair = lax.all_gather(
        jnp.concatenate([output_grad, grad_other], axis=0), "row", axis=1, tiled=True
    )
    patch_pair = jnp.concatenate([every_patch, patch_other], axis=0)
    out_weight_grad = lax.dot_general(
        out_pair, grad_pair, (((0, 1), (0, 1)), ((), ())), preferred_element_type=jnp.float32
    )
    embed_weight_grad = lax.dot_general(
        patch_pair, grad_pair, (((0, 1), (0, 1)), ((), ())), preferred_element_type=jnp.float32
    )
    return (
        query_grad.reshape(1, local_rows, feature_width),
        key_sum.reshape(1, local_rows, feature_width),
        value_sum.reshape(1, local_rows, feature_width),
        out_weight_grad,
        embed_weight_grad,
    )


def axis_size(axis):
    return lax.psum(1, axis)


def shifted(x, axis, step):
    n = axis_size(axis)
    return lax.ppermute(x, axis, [(j, (j + step) % n) for j in range(n)])


def natural(pieces, axis):
    n = len(pieces)
    order = (lax.axis_index(axis) - jnp.arange(n)) % n
    return jnp.take(jnp.stack(pieces, 0), order, axis=0)


def gather_rows(x, axis):
    n = axis_size(axis)
    pieces = [x] + [shifted(x, axis, s) for s in range(1, n)]
    stacked = natural(pieces, axis)
    return stacked.reshape((n * x.shape[0],) + x.shape[1:])


def group_cols(x, axis, group):
    width = x.shape[1] // axis_size(axis)
    return lax.dynamic_slice_in_dim(x, group * width, width, 1)


def to_heads(x, axis):
    n, me = axis_size(axis), lax.axis_index(axis)
    pieces = [group_cols(x, axis, me)] + [
        shifted(group_cols(x, axis, (me + s) % n), axis, s) for s in range(1, n)
    ]
    stacked = natural(pieces, axis)
    return stacked.reshape((n * x.shape[0],) + stacked.shape[2:])


def from_heads(x, axis):
    n, me = axis_size(axis), lax.axis_index(axis)
    rows = x.shape[0] // n
    block = lambda k: lax.dynamic_slice_in_dim(x, k * rows, rows, 0)
    pieces = [block(me)] + [
        shifted(block((me + s) % n).astype(jnp.bfloat16), axis, s).astype(jnp.float32)
        for s in range(1, n)
    ]
    stacked = natural(pieces, axis)
    return jnp.transpose(stacked, (1, 0, 2)).reshape(rows, n * x.shape[1])


def sum_to_heads(partial, axis):
    n, me = axis_size(axis), lax.axis_index(axis)
    total = group_cols(partial, axis, me)
    for s in range(1, n):
        sent = group_cols(partial, axis, (me - s) % n).astype(jnp.bfloat16)
        total = total + shifted(sent, axis, -s % n).astype(jnp.float32)
    return total


def flat(*arrays):
    return jnp.concatenate([a.reshape(-1) for a in arrays])


def unflat(vector, shapes):
    out, at = [], 0
    for shape in shapes:
        size = int(np.prod(shape))
        out.append(vector[..., at:at + size].reshape(vector.shape[:-1] + shape))
        at += size
    return out


def gather_rows_relayed(x, axis):
    n, me = axis_size(axis), lax.axis_index(axis)
    chips = n // 2
    cross = [x] + [
        lax.ppermute(x, axis, [(j, (j + 2 * s) % n) for j in range(n)]) for s in range(1, chips)
    ]
    partner_own = lax.ppermute(x, axis, [(j, j ^ 1) for j in range(n)])
    if chips > 1:
        relayed = lax.ppermute(jnp.stack(cross[1:], 0), axis, [(j, j ^ 1) for j in range(n)])
        partner = [partner_own] + [relayed[k] for k in range(chips - 1)]
    else:
        partner = [partner_own]
    pieces = jnp.stack(cross + partner, 0)
    j = jnp.arange(n)
    mine = (j % 2) == (me % 2)
    order = jnp.where(mine, ((me - j) % n) // 2, chips + (((me ^ 1) - j) % n) // 2)
    stacked = jnp.take(pieces, order, axis=0)
    return stacked.reshape((n * x.shape[0],) + x.shape[1:])


def roll_blocks(x, shift):
    n = x.shape[0]
    return lax.dynamic_slice_in_dim(jnp.concatenate([x, x], 0), shift % n, n, 0)


def body_heads(patches, queries, attn_keys, attn_values, out_weight, output_grad):
    factor = DH ** (-0.5)
    n, me = axis_size("col"), lax.axis_index("col")
    rank = lax.axis_index("row")
    tokens, width_all = queries.shape[1], queries.shape[2]
    width = width_all // n
    heads = width // DH
    patch_here = patches[0]
    grad_blocks = [output_grad[0]] + [shifted(output_grad[0], "row", s) for s in range(1, n)]
    dense_grad = jnp.concatenate(grad_blocks, 0)
    grad_other = swap_dp(output_grad)
    sources = (queries[0], attn_keys[0], attn_values[0])
    part = lambda g: [lax.dynamic_slice_in_dim(a, g * width, width, 1) for a in sources]
    shapes = [(3, tokens, width), patch_here.shape]
    pieces = [(jnp.stack(part(me), 0), patch_here)]
    for s in range(1, n):
        got = shifted(flat(*part((me + s) % n), patch_here), "col", s)
        pieces.append(tuple(unflat(got, shapes)))
    grad_partial = lax.dot_general(
        dense_grad, out_weight, (((1,), (1,)), ((), ())), preferred_element_type=jnp.float32
    )
    pieces, grad_partial = lax.optimization_barrier((pieces, grad_partial))
    order = me - rank
    qkv_h = roll_blocks(jnp.stack([p[0] for p in pieces], 0), order)
    every_patch = roll_blocks(jnp.stack([p[1] for p in pieces], 0), order).reshape(n * tokens, -1)
    rows = n * tokens
    qkv_h = jnp.transpose(qkv_h, (1, 0, 2, 3)).reshape(3, rows, heads, DH)
    local_query, all_keys, all_values = qkv_h[0], qkv_h[1], qkv_h[2]
    grad_partial, grad_other = lax.optimization_barrier((grad_partial, grad_other))
    other_blocks = [grad_other[0]] + [shifted(grad_other[0], "row", s) for s in range(1, n)]
    scores = (
        jnp.einsum("qhd,khd->hqk", local_query, all_keys, preferred_element_type=jnp.float32)
        * factor
    )
    row_max = jnp.max(scores, axis=2, keepdims=True)
    log_total = row_max + jnp.log(jnp.sum(jnp.exp(scores - row_max), axis=2, keepdims=True))
    attn_probs = jnp.exp(scores - log_total).astype(jnp.bfloat16)
    attn_out = jnp.einsum(
        "hqk,khd->qhd", attn_probs, all_values, preferred_element_type=jnp.float32
    ).astype(jnp.bfloat16)
    attn_grad = sum_to_heads(grad_partial, "col").astype(jnp.bfloat16)
    grad_heads = attn_grad.reshape(rows, heads, DH)
    prob_grad = jnp.einsum(
        "qhd,khd->hqk", grad_heads, all_values, preferred_element_type=jnp.float32
    )
    row_dot = jnp.transpose(
        jnp.sum(grad_heads.astype(jnp.float32) * attn_out.astype(jnp.float32), axis=2)
    )[:, :, None]
    score_grad = (attn_probs.astype(jnp.float32) * (prob_grad - row_dot)).astype(jnp.bfloat16)
    query_grad = (
        jnp.einsum("hqk,khd->qhd", score_grad, all_keys, preferred_element_type=jnp.float32)
        * factor
    )
    key_grad = (
        jnp.einsum("hqk,qhd->khd", score_grad, local_query, preferred_element_type=jnp.float32)
        * factor
    )
    value_grad = jnp.einsum(
        "hqk,qhd->khd", attn_probs, grad_heads, preferred_element_type=jnp.float32
    )
    other_patch = swap_dp(every_patch)
    out_flat = attn_out.reshape(rows, width)
    own_pair = (out_flat, swap_dp(out_flat))
    attn_grad, sent_out = lax.optimization_barrier((attn_grad, out_flat))
    out_pieces = [own_pair] + [
        (got, swap_dp(got)) for got in (shifted(sent_out, "col", -s % n) for s in range(1, n))
    ]
    out_both = roll_blocks(
        jnp.stack([jnp.concatenate(p, 0) for p in out_pieces], 0), -me
    )
    grad_both = jnp.concatenate([dense_grad] + other_blocks, 0)
    embed_weight_grad = contract_rows(jnp.concatenate([every_patch, other_patch], 0), grad_both)
    grad_list = [g.reshape(n, tokens, width) for g in (query_grad, key_grad, value_grad)]
    sendable = roll_blocks(
        jnp.stack([g.astype(jnp.bfloat16) for g in grad_list], 1), rank - me
    )
    early = [p[0] for p in out_pieces] + [out_pieces[k][1] for k in range(n) if k != n // 2]
    sendable, _ = lax.optimization_barrier((sendable, early))
    out_both, sendable = lax.optimization_barrier((out_both, sendable))
    out_weight_grad = lax.dot_general(
        out_both, grad_both, (((1,), (0,)), ((), ())), preferred_element_type=jnp.float32
    ).reshape(width_all, -1)
    mine = jnp.stack(
        [lax.dynamic_index_in_dim(g, (rank - me) % n, 0, keepdims=False) for g in grad_list], 0
    )
    back = jnp.zeros((3, tokens, width_all), jnp.float32)
    back = lax.dynamic_update_slice_in_dim(back, mine, me * width, 2)
    for s in range(1, n):
        got = shifted(sendable[s], "col", -s % n).astype(jnp.float32)
        back = lax.dynamic_update_slice_in_dim(back, got, ((me + s) % n) * width, 2)
    back = back.reshape(3, 1, tokens, width_all)
    return (back[0], back[1], back[2], out_weight_grad, embed_weight_grad)


def body(patches, queries, attn_keys, attn_values, out_weight, output_grad):
    heads_here = queries.shape[2] // DH
    if (
        heads_here % axis_size("col") == 0
        and queries.shape[1] == output_grad.shape[1]
        and axis_size("row") == axis_size("col")
    ):
        return body_heads(patches, queries, attn_keys, attn_values, out_weight, output_grad)
    return body_tokens(patches, queries, attn_keys, attn_values, out_weight, output_grad)


def solution(mesh):
    placed = (
        P("dp", "col", "row"),
        P("dp", "col", "row"),
        P("dp", "col", "row"),
        P("dp", "col", "row"),
        P("row", "col"),
        P("dp", "row", "col"),
    )
    return jax.shard_map(
        body,
        mesh=mesh,
        in_specs=placed,
        out_specs=(
            P("dp", "col", "row"),
            P("dp", "col", "row"),
            P("dp", "col", "row"),
            P("row", "col"),
            P("row", "col"),
        ),
        check_vma=False,
    )
```
